512 devices in a mesh: lon: 64 (over x, y, z_hi, core), lat: 8 (over z_lo).
Axes of the slice: x: 4, y: 4, z: 16 (z_hi: 2, z_lo: 8; z = z_hi * 8 + z_lo), core: 2. Of those that a mesh axis runs over, the one named last changes fastest.
Arguments:
- potential_heat: float32 [4, 768, 8192], P(None, 'lat', 'lon'), may hold values from -6 to 6
- salt_anomaly_field: float32 [4, 768, 8192], P(None, 'lat', 'lon'), may hold values from -6 to 6
- zonal_current: float32 [4, 768, 8192], P(None, 'lat', 'lon'), may hold values from -6 to 6
- meridional_current: float32 [4, 768, 8192], P(None, 'lat', 'lon'), may hold values from -6 to 6
- water_indicator: int32 [4, 768, 8192], P(None, 'lat', 'lon'), may hold values 0 or 1
- floor_layer_index: int32 [768, 8192], P('lat', 'lon'), may hold values from 0 to 3
- zonal_spacing: float32 [768, 8192], P('lat', 'lon'), may hold values from 0.7 to 1.4
- meridional_spacing: float32 [768, 8192], P('lat', 'lon'), may hold values from 0.7 to 1.4
- planetary_rotation_factor: float32 [768, 8192], P('lat', 'lon'), may hold values from 0.3 to 1.5
- horizontal_eddy_coefficient: float32 [768, 8192], P('lat', 'lon'), may hold values from 0.05 to 0.25
- diapycnal_diffusivity: float32 [3, 768, 8192], P(None, 'lat', 'lon'), may hold values from 0.02 to 0.5
- layer_height: float32 [4], replicated, may hold values from 0.7 to 1.4
Outputs:
- new_temperature: float32 [4, 768, 8192], P(None, 'lat', 'lon')
- new_salinity: float32 [4, 768, 8192], P(None, 'lat', 'lon')
- new_zonal: float32 [4, 768, 8192], P(None, 'lat', 'lon')
- new_meridional: float32 [4, 768, 8192], P(None, 'lat', 'lon')
The draws below stay inside these ranges and needn't reach their ends.
All inputs are finite; a program needn't handle non-finite values. No bound on the sum of `water_indicator` on one device may be relied on, other than what follows from the above.
Results may differ from the reference program's by a relative error of at most 0.0003.
Values sent between devices are 32-bit elements; how exact they have to be, the bound alone decides.
No kernel may reach another device: no remote copies, remote signals or barrier semaphores. Data moves between devices by JAX's collectives and lax.ppermute only.
A program may use at most 64 MiB of HBM per device.

```python
import math
import jax
import jax.numpy as jnp
from jax import lax

VERTICAL_LAYERS = 4
MERIDIAN_POINTS = 768
PARALLEL_POINTS = 8192


def set_ends(entries, own_key, least, largest):
    spot = [jax.random.randint(jax.random.fold_in(own_key, axis), (), 0, length) for axis, length in enumerate(entries.shape)]
    widest = entries.shape.index(max(entries.shape))
    neighbour = spot[:widest] + [(spot[widest] + 1) % entries.shape[widest]] + spot[widest + 1:]
    return entries.at[tuple(spot)].set(least).at[tuple(neighbour)].set(largest)


def level_of(own_key, extent, pieces, least, largest):
    gain, own = 1.0, jax.random.fold_in(own_key, 6)
    for axis_at, blocks in pieces:
        steps = jnp.exp(jax.random.uniform(jax.random.fold_in(own, axis_at), (blocks,), jnp.float32, least / len(pieces), largest / len(pieces)))
        gain = gain * jnp.repeat(steps, extent[axis_at] // blocks).reshape([-1 if axis == axis_at else 1 for axis in range(len(extent))])
    return gain


def bell_draw(own_key, extent, scale, bound, shards=(), held_as=jnp.bfloat16):
    values = scale * jax.random.normal(own_key, extent, jnp.float32)
    if shards:
        values = values * level_of(own_key, extent, shards, -0.22, 0.18)
    return jnp.clip(values, -bound, bound).astype(held_as)


def setup_inputs(seed: int = 0) -> dict:
    key_list = jax.random.split(jax.random.key(seed), 13)
    return {
        "potential_heat": bell_draw(key_list[0], (VERTICAL_LAYERS, MERIDIAN_POINTS, PARALLEL_POINTS), 1.0, 6.0, ((1, 8), (2, 64)), jnp.float32),
        "salt_anomaly_field": bell_draw(key_list[1], (VERTICAL_LAYERS, MERIDIAN_POINTS, PARALLEL_POINTS), 1.0, 6.0, ((1, 8), (2, 64)), jnp.float32),
        "zonal_current": bell_draw(key_list[2], (VERTICAL_LAYERS, MERIDIAN_POINTS, PARALLEL_POINTS), 1.0, 6.0, ((1, 8), (2, 64)), jnp.float32),
        "meridional_current": bell_draw(key_list[3], (VERTICAL_LAYERS, MERIDIAN_POINTS, PARALLEL_POINTS), 1.0, 6.0, ((1, 8), (2, 64)), jnp.float32),
        "water_indicator": set_ends((jax.random.randint(key_list[4], (VERTICAL_LAYERS, MERIDIAN_POINTS, PARALLEL_POINTS), 0, 10) < 9).astype(jnp.int32), jax.random.fold_in(key_list[4], 1), 0, 1),
        "floor_layer_index": set_ends(jax.random.randint(key_list[5], (MERIDIAN_POINTS, PARALLEL_POINTS), 0, VERTICAL_LAYERS), jax.random.fold_in(key_list[5], 1), 0, VERTICAL_LAYERS - 1).astype(jnp.int32),
        "zonal_spacing": jnp.clip(jnp.exp(math.log(1.4) - 0.6931472 * jax.random.uniform(key_list[6], (MERIDIAN_POINTS, PARALLEL_POINTS), jnp.float32) ** level_of(key_list[6], (MERIDIAN_POINTS, PARALLEL_POINTS), ((0, 8), (1, 64)), -0.2, 0.2)), 0.7, 1.4),
        "meridional_spacing": jnp.clip(jnp.exp(math.log(1.4) - 0.6931472 * jax.random.uniform(key_list[7], (MERIDIAN_POINTS, PARALLEL_POINTS), jnp.float32) ** level_of(key_list[7], (MERIDIAN_POINTS, PARALLEL_POINTS), ((0, 8), (1, 64)), -0.2, 0.2)), 0.7, 1.4),
        "planetary_rotation_factor": jnp.clip(jnp.exp(math.log(1.5) - 1.60943787 * jax.random.uniform(key_list[8], (MERIDIAN_POINTS, PARALLEL_POINTS), jnp.float32) ** level_of(key_list[8], (MERIDIAN_POINTS, PARALLEL_POINTS), ((0, 8), (1, 64)), -0.2, 0.2)), 0.3, 1.5),
        "horizontal_eddy_coefficient": jnp.clip(jnp.exp(math.log(0.25) - 1.609438 * jax.random.uniform(key_list[9], (MERIDIAN_POINTS, PARALLEL_POINTS), jnp.float32) ** level_of(key_list[9], (MERIDIAN_POINTS, PARALLEL_POINTS), ((0, 8), (1, 64)), -0.2, 0.2)), 0.05, 0.25),
        "diapycnal_diffusivity": jnp.clip(jnp.exp(math.log(0.5) - 3.218876 * jax.random.uniform(key_list[10], (VERTICAL_LAYERS - 1, MERIDIAN_POINTS, PARALLEL_POINTS), jnp.float32) ** level_of(key_list[10], (VERTICAL_LAYERS - 1, MERIDIAN_POINTS, PARALLEL_POINTS), ((1, 8), (2, 64)), -0.2, 0.2)), 0.02, 0.5),
        "layer_height": jnp.clip(jnp.exp(jax.random.uniform(key_list[11], (VERTICAL_LAYERS,), jnp.float32, math.log(0.7), math.log(1.4))), 0.7, 1.4),
    }


TIME_STEP = 0.25
EXPANSION = 0.2
CONTRACTION = 0.8
BOTTOM_DRAG = 1.0


def pressure(temp_part, salt_part, layer_height):
    layer_mass = (CONTRACTION * salt_part - EXPANSION * temp_part) * layer_height[:, None, None]
    return jnp.cumsum(layer_mass, axis=0) - 0.5 * layer_mass


def mix_vertically(fields, water_share, diapycnal_diffusivity, layer_height):
    contrast = fields[:, 1:] - fields[:, :-1]
    fluxes = diapycnal_diffusivity * (water_share[1:] * water_share[:-1]) * contrast
    boundary = jnp.zeros_like(fluxes[:, :1])
    flux_below = jnp.concatenate([fluxes, boundary], axis=1)
    flux_above = jnp.concatenate([boundary, fluxes], axis=1)
    return (flux_below - flux_above) / (layer_height * layer_height)[None, :, None, None]


def advance(central, eastern, western, northern, southern, floor_layer_index, zonal_spacing, meridional_spacing, planetary_rotation_factor, horizontal_eddy_coefficient, diapycnal_diffusivity, layer_height):
    levels = central.shape[1]
    at_bottom = (lax.broadcasted_iota(jnp.int32, (levels, 1, 1), 0) == floor_layer_index[None]).astype(jnp.float32)
    water_share = central[4]
    fields = central[:4]
    weight_east = water_share * eastern[4]
    weight_west = water_share * western[4]
    weight_north = water_share * northern[4]
    weight_south = water_share * southern[4]
    diffusion = horizontal_eddy_coefficient * ((weight_east * (eastern[:4] - fields) + weight_west * (western[:4] - fields)) / (zonal_spacing * zonal_spacing) + (weight_north * (northern[:4] - fields) + weight_south * (southern[:4] - fields)) / (meridional_spacing * meridional_spacing))
    zonal = fields[2]
    merid = fields[3]
    advection = -(zonal * (eastern[:4] - western[:4]) * (0.5 / zonal_spacing) + merid * (northern[:4] - southern[:4]) * (0.5 / meridional_spacing))
    pressure_east = pressure(eastern[0], eastern[1], layer_height)
    pressure_west = pressure(western[0], western[1], layer_height)
    pressure_north = pressure(northern[0], northern[1], layer_height)
    pressure_south = pressure(southern[0], southern[1], layer_height)
    gradient_x = -(pressure_east - pressure_west) * (0.5 / zonal_spacing)
    gradient_y = -(pressure_north - pressure_south) * (0.5 / meridional_spacing)
    mixing = mix_vertically(fields, water_share, diapycnal_diffusivity, layer_height)
    tendency = advection + diffusion + mixing
    tend_zonal = tendency[2] + planetary_rotation_factor * merid + gradient_x - BOTTOM_DRAG * at_bottom * zonal
    tend_merid = tendency[3] - planetary_rotation_factor * zonal + gradient_y - BOTTOM_DRAG * at_bottom * merid
    tendency = jnp.stack([tendency[0], tendency[1], tend_zonal, tend_merid])
    updated = water_share * (fields + TIME_STEP * tendency)
    return jnp.concatenate([updated, water_share[None]], axis=0)


def reference(potential_heat, salt_anomaly_field, zonal_current, meridional_current, water_indicator, floor_layer_index, zonal_spacing, meridional_spacing, planetary_rotation_factor, horizontal_eddy_coefficient, diapycnal_diffusivity, layer_height):
    water_share = water_indicator.astype(jnp.float32)
    combined_tracers = jnp.stack([potential_heat * water_share, salt_anomaly_field * water_share, zonal_current * water_share, meridional_current * water_share, water_share])
    fold_sign = jnp.array([1.0, 1.0, -1.0, -1.0, 1.0], jnp.float32).reshape(5, 1, 1, 1)
    channels, levels, lat_count, lon_count = combined_tracers.shape
    block_count = lat_count // 8
    for step_index in range(2):
        ghost_row = combined_tracers[:, :, -1:, ::-1] * fold_sign
        padded = jnp.concatenate([jnp.zeros_like(ghost_row), combined_tracers, ghost_row], axis=2)
        padded = jnp.concatenate([padded[..., -1:], padded, padded[..., :1]], axis=3)

        def one_block(block_index):
            row_start = (block_index * 8).astype(jnp.int32)
            window = lax.dynamic_slice_in_dim(padded, row_start, 10, 2)
            central = window[:, :, 1:-1, 1:-1]
            eastern = window[:, :, 1:-1, 2:]
            western = window[:, :, 1:-1, :-2]
            northern = window[:, :, 2:, 1:-1]
            southern = window[:, :, :-2, 1:-1]
            return advance(central, eastern, western, northern, southern,
                           lax.dynamic_slice_in_dim(floor_layer_index, row_start, 8, 0),
                           lax.dynamic_slice_in_dim(zonal_spacing, row_start, 8, 0),
                           lax.dynamic_slice_in_dim(meridional_spacing, row_start, 8, 0),
                           lax.dynamic_slice_in_dim(planetary_rotation_factor, row_start, 8, 0),
                           lax.dynamic_slice_in_dim(horizontal_eddy_coefficient, row_start, 8, 0),
                           lax.dynamic_slice_in_dim(diapycnal_diffusivity, row_start, 8, 1),
                           layer_height)

        results = lax.map(one_block, jnp.arange(block_count, dtype=jnp.int32))
        combined_tracers = jnp.moveaxis(results, 0, 2).reshape(channels, levels, lat_count, lon_count)
    return combined_tracers[0], combined_tracers[1], combined_tracers[2], combined_tracers[3]
```

```python
import jax
import jax.numpy as jnp
from jax import lax
from jax.sharding import PartitionSpec as P

TIME_STEP = 0.25
EXPANSION = 0.2
CONTRACTION = 0.8
BOTTOM_DRAG = 1.0


def with_halo(value, sides, width, wrap):
    for axis, dim in sides:
        size, length = (lax.axis_size(axis), value.shape[dim])
        up = [(i, (i + 1) % size) for i in range(size if wrap else size - 1)]
        down = [(j, i) for i, j in up]
        last = lax.slice_in_dim(value, length - width, length, axis=dim)
        leading = lax.slice_in_dim(value, 0, width, axis=dim)
        before = lax.ppermute(last, axis, up)
        after = lax.ppermute(leading, axis, down)
        value = jnp.concatenate([before, value, after], axis=dim)
    return value


def pressure(temp_part, salt_part, layer_height):
    layer_mass = (CONTRACTION * salt_part - EXPANSION * temp_part) * layer_height[:, None, None]
    return jnp.cumsum(layer_mass, axis=0) - 0.5 * layer_mass


def mix_vertically(fields, water_share, diapycnal_diffusivity, layer_height):
    contrast = fields[:, 1:] - fields[:, :-1]
    fluxes = diapycnal_diffusivity * (water_share[1:] * water_share[:-1]) * contrast
    boundary = jnp.zeros_like(fluxes[:, :1])
    flux_below = jnp.concatenate([fluxes, boundary], axis=1)
    flux_above = jnp.concatenate([boundary, fluxes], axis=1)
    return (flux_below - flux_above) / (layer_height * layer_height)[None, :, None, None]


def advance(
    central,
    eastern,
    western,
    northern,
    southern,
    at_bottom,
    zonal_spacing,
    meridional_spacing,
    planetary_rotation_factor,
    horizontal_eddy_coefficient,
    diapycnal_diffusivity,
    layer_height,
):
    water_share = central[4]
    fields = central[:4]
    weight_east = water_share * eastern[4]
    weight_west = water_share * western[4]
    weight_north = water_share * northern[4]
    weight_south = water_share * southern[4]
    diffusion = horizontal_eddy_coefficient * (
        (weight_east * (eastern[:4] - fields) + weight_west * (western[:4] - fields))
        / (zonal_spacing * zonal_spacing)
        + (weight_north * (northern[:4] - fields) + weight_south * (southern[:4] - fields))
        / (meridional_spacing * meridional_spacing)
    )
    zonal = fields[2]
    merid = fields[3]
    advection = -(
        zonal * (eastern[:4] - western[:4]) * (0.5 / zonal_spacing)
        + merid * (northern[:4] - southern[:4]) * (0.5 / meridional_spacing)
    )
    pressure_east = pressure(eastern[0], eastern[1], layer_height)
    pressure_west = pressure(western[0], western[1], layer_height)
    pressure_north = pressure(northern[0], northern[1], layer_height)
    pressure_south = pressure(southern[0], southern[1], layer_height)
    gradient_x = -(pressure_east - pressure_west) * (0.5 / zonal_spacing)
    gradient_y = -(pressure_north - pressure_south) * (0.5 / meridional_spacing)
    mixing = mix_vertically(fields, water_share, diapycnal_diffusivity, layer_height)
    tendency = advection + diffusion + mixing
    tend_zonal = (
        tendency[2]
        + planetary_rotation_factor * merid
        + gradient_x
        - BOTTOM_DRAG * at_bottom * zonal
    )
    tend_merid = (
        tendency[3]
        - planetary_rotation_factor * zonal
        + gradient_y
        - BOTTOM_DRAG * at_bottom * merid
    )
    tendency = jnp.stack([tendency[0], tendency[1], tend_zonal, tend_merid])
    updated = water_share * (fields + TIME_STEP * tendency)
    return jnp.concatenate([updated, water_share[None]], axis=0)


def fold_ghost(top_row):
    fold_sign = jnp.array([1.0, 1.0, -1.0, -1.0, 1.0], jnp.float32).reshape(5, 1, 1)
    lon_count = lax.axis_size("lon")
    lat_count = lax.axis_size("lat")
    top = lat_count - 1
    pairs = [(i * lat_count + top, (lon_count - 1 - i) * lat_count + top) for i in range(lon_count)]
    mirrored = lax.ppermute(top_row, ("lon", "lat"), pairs)
    return mirrored[:, :, ::-1] * fold_sign


def shards(
    potential_heat,
    salt_anomaly_field,
    zonal_current,
    meridional_current,
    water_indicator,
    floor_layer_index,
    zonal_spacing,
    meridional_spacing,
    planetary_rotation_factor,
    horizontal_eddy_coefficient,
    diapycnal_diffusivity,
    layer_height,
):
    water_share = water_indicator.astype(jnp.float32)
    combined_tracers = jnp.stack(
        [
            potential_heat * water_share,
            salt_anomaly_field * water_share,
            zonal_current * water_share,
            meridional_current * water_share,
            water_share,
        ]
    )
    levels = combined_tracers.shape[1]
    is_top = lax.axis_index("lat") == lax.axis_size("lat") - 1
    at_bottom = (
        lax.broadcasted_iota(jnp.int32, (levels, 1, 1), 0) == floor_layer_index[None]
    ).astype(jnp.float32)
    for step_index in range(2):
        lon_padded = with_halo(combined_tracers, (("lon", 3),), 1, True)
        lat_padded = with_halo(combined_tracers, (("lat", 2),), 1, False)
        ghost_row = fold_ghost(combined_tracers[:, :, -1, :])
        north_rim = jnp.where(is_top, ghost_row, lat_padded[:, :, -1, :])
        northern = jnp.concatenate([lat_padded[:, :, 2:-1, :], north_rim[:, :, None, :]], axis=2)
        southern = lat_padded[:, :, :-2, :]
        eastern = lon_padded[..., 2:]
        western = lon_padded[..., :-2]
        combined_tracers = advance(
            combined_tracers,
            eastern,
            western,
            northern,
            southern,
            at_bottom,
            zonal_spacing,
            meridional_spacing,
            planetary_rotation_factor,
            horizontal_eddy_coefficient,
            diapycnal_diffusivity,
            layer_height,
        )
    return (combined_tracers[0], combined_tracers[1], combined_tracers[2], combined_tracers[3])


def solution(mesh):
    return jax.shard_map(
        shards,
        mesh=mesh,
        in_specs=(
            P(None, "lat", "lon"),
            P(None, "lat", "lon"),
            P(None, "lat", "lon"),
            P(None, "lat", "lon"),
            P(None, "lat", "lon"),
            P("lat", "lon"),
            P("lat", "lon"),
            P("lat", "lon"),
            P("lat", "lon"),
            P("lat", "lon"),
            P(None, "lat", "lon"),
            P(),
        ),
        out_specs=(
            P(None, "lat", "lon"),
            P(None, "lat", "lon"),
            P(None, "lat", "lon"),
            P(None, "lat", "lon"),
        ),
        check_vma=False,
    )
```

```python
import jax
import jax.numpy as jnp
from jax import lax
from jax.sharding import PartitionSpec as P

TIME_STEP = 0.25
EXPANSION = 0.2
CONTRACTION = 0.8
BOTTOM_DRAG = 1.0
HALO = 2


def pressure(temp_part, salt_part, layer_height):
    layer_mass = (CONTRACTION * salt_part - EXPANSION * temp_part) * layer_height[:, None, None]
    return jnp.cumsum(layer_mass, axis=0) - 0.5 * layer_mass


def mix_vertically(fields, water_share, diapycnal_diffusivity, layer_height):
    contrast = fields[:, 1:] - fields[:, :-1]
    fluxes = diapycnal_diffusivity * (water_share[1:] * water_share[:-1]) * contrast
    boundary = jnp.zeros_like(fluxes[:, :1])
    flux_below = jnp.concatenate([fluxes, boundary], axis=1)
    flux_above = jnp.concatenate([boundary, fluxes], axis=1)
    return (flux_below - flux_above) / (layer_height * layer_height)[None, :, None, None]


def advance(
    central,
    eastern,
    western,
    northern,
    southern,
    at_bottom,
    zonal_spacing,
    meridional_spacing,
    planetary_rotation_factor,
    horizontal_eddy_coefficient,
    diapycnal_diffusivity,
    layer_height,
):
    water_share = central[4]
    fields = central[:4]
    weight_east = water_share * eastern[4]
    weight_west = water_share * western[4]
    weight_north = water_share * northern[4]
    weight_south = water_share * southern[4]
    diffusion = horizontal_eddy_coefficient * (
        (weight_east * (eastern[:4] - fields) + weight_west * (western[:4] - fields))
        / (zonal_spacing * zonal_spacing)
        + (weight_north * (northern[:4] - fields) + weight_south * (southern[:4] - fields))
        / (meridional_spacing * meridional_spacing)
    )
    zonal = fields[2]
    merid = fields[3]
    advection = -(
        zonal * (eastern[:4] - western[:4]) * (0.5 / zonal_spacing)
        + merid * (northern[:4] - southern[:4]) * (0.5 / meridional_spacing)
    )
    pressure_east = pressure(eastern[0], eastern[1], layer_height)
    pressure_west = pressure(western[0], western[1], layer_height)
    pressure_north = pressure(northern[0], northern[1], layer_height)
    pressure_south = pressure(southern[0], southern[1], layer_height)
    gradient_x = -(pressure_east - pressure_west) * (0.5 / zonal_spacing)
    gradient_y = -(pressure_north - pressure_south) * (0.5 / meridional_spacing)
    mixing = mix_vertically(fields, water_share, diapycnal_diffusivity, layer_height)
    tendency = advection + diffusion + mixing
    tend_zonal = (
        tendency[2]
        + planetary_rotation_factor * merid
        + gradient_x
        - BOTTOM_DRAG * at_bottom * zonal
    )
    tend_merid = (
        tendency[3]
        - planetary_rotation_factor * zonal
        + gradient_y
        - BOTTOM_DRAG * at_bottom * merid
    )
    tendency = jnp.stack([tendency[0], tendency[1], tend_zonal, tend_merid])
    updated = water_share * (fields + TIME_STEP * tendency)
    return jnp.concatenate([updated, water_share[None]], axis=0)


def step(state, params, levels, layer_height):
    floor_index = params[0]
    at_bottom = (
        lax.broadcasted_iota(jnp.int32, (levels, 1, 1), 0).astype(jnp.float32) == floor_index[None]
    ).astype(jnp.float32)
    return advance(
        state[:, :, 1:-1, 1:-1],
        state[:, :, 1:-1, 2:],
        state[:, :, 1:-1, :-2],
        state[:, :, 2:, 1:-1],
        state[:, :, :-2, 1:-1],
        at_bottom,
        params[1],
        params[2],
        params[3],
        params[4],
        params[5:8],
        layer_height,
    )


def neighbour_pairs(lon_count, lat_count, d_lon, d_lat):
    pairs = []
    for i in range(lon_count):
        for j in range(lat_count):
            k = j + d_lat
            if 0 <= k < lat_count:
                pairs.append((i * lat_count + j, ((i + d_lon) % lon_count) * lat_count + k))
    return pairs


def fold_pairs(lon_count, lat_count, target_of):
    top = lat_count - 1
    return [(i * lat_count + top, (target_of(i) % lon_count) * lat_count + top) for i in range(lon_count)]


def exchange(block, sign):
    lon_count = lax.axis_size("lon")
    lat_count = lax.axis_size("lat")
    axes = ("lon", "lat")
    h = HALO

    def send(piece, d_lon, d_lat):
        return lax.ppermute(piece, axes, neighbour_pairs(lon_count, lat_count, d_lon, d_lat))

    rows_lo, rows_hi = block[:, :h, :], block[:, -h:, :]
    cols_lo, cols_hi = block[:, :, :h], block[:, :, -h:]
    west = send(cols_hi, 1, 0)
    east = send(cols_lo, -1, 0)
    south = send(rows_hi, 0, 1)
    north = send(rows_lo, 0, -1)
    south_west = send(rows_hi[:, :, -h:], 1, 1)
    south_east = send(rows_hi[:, :, :h], -1, 1)
    north_west = send(rows_lo[:, :, -h:], 1, -1)
    north_east = send(rows_lo[:, :, :h], -1, -1)

    mirror = lax.ppermute(rows_hi, axes, fold_pairs(lon_count, lat_count, lambda i: lon_count - 1 - i))
    mirror_lo = lax.ppermute(
        rows_hi[:, :, :h], axes, fold_pairs(lon_count, lat_count, lambda i: lon_count - i)
    )
    mirror_hi = lax.ppermute(
        rows_hi[:, :, -h:], axes, fold_pairs(lon_count, lat_count, lambda i: lon_count - 2 - i)
    )
    mirrored = jnp.concatenate([mirror_hi, mirror, mirror_lo], axis=2)
    folded = mirrored[:, ::-1, ::-1] * sign[:, None, None]

    is_top = lax.axis_index("lat") == lat_count - 1
    north_row = jnp.concatenate([north_west, north, north_east], axis=2)
    north_row = jnp.where(is_top, folded, north_row)
    south_row = jnp.concatenate([south_west, south, south_east], axis=2)
    middle = jnp.concatenate([west, block, east], axis=2)
    return jnp.concatenate([south_row, middle, north_row], axis=1)


def shards(
    potential_heat,
    salt_anomaly_field,
    zonal_current,
    meridional_current,
    water_indicator,
    floor_layer_index,
    zonal_spacing,
    meridional_spacing,
    planetary_rotation_factor,
    horizontal_eddy_coefficient,
    diapycnal_diffusivity,
    layer_height,
):
    water_share = water_indicator.astype(jnp.float32)
    state = jnp.stack(
        [
            potential_heat * water_share,
            salt_anomaly_field * water_share,
            zonal_current * water_share,
            meridional_current * water_share,
            water_share,
        ]
    )
    channels, levels, rows, cols = state.shape
    params = jnp.concatenate(
        [
            jnp.stack(
                [
                    floor_layer_index.astype(jnp.float32),
                    zonal_spacing,
                    meridional_spacing,
                    planetary_rotation_factor,
                    horizontal_eddy_coefficient,
                ]
            ),
            diapycnal_diffusivity,
        ]
    )
    planes = jnp.concatenate([state.reshape(channels * levels, rows, cols), params])
    channel_sign = jnp.array([1.0, 1.0, -1.0, -1.0, 1.0], jnp.float32)
    sign = jnp.concatenate(
        [jnp.repeat(channel_sign, levels), jnp.ones((params.shape[0],), jnp.float32)]
    )
    padded = exchange(planes, sign)
    n_state = channels * levels
    state0 = padded[:n_state].reshape(channels, levels, rows + 2 * HALO, cols + 2 * HALO)
    params_outer = padded[n_state:, 1:-1, 1:-1]
    state1 = step(state0, params_outer, levels, layer_height)
    is_bottom = lax.axis_index("lat") == 0
    first_row = jnp.where(is_bottom, 0.0, state1[:, :, :1, :])
    state1 = jnp.concatenate([first_row, state1[:, :, 1:, :]], axis=2)
    params_inner = params
    state2 = step(state1, params_inner, levels, layer_height)
    return (state2[0], state2[1], state2[2], state2[3])


def solution(mesh):
    return jax.shard_map(
        shards,
        mesh=mesh,
        in_specs=(
            P(None, "lat", "lon"),
            P(None, "lat", "lon"),
            P(None, "lat", "lon"),
            P(None, "lat", "lon"),
            P(None, "lat", "lon"),
            P("lat", "lon"),
            P("lat", "lon"),
            P("lat", "lon"),
            P("lat", "lon"),
            P("lat", "lon"),
            P(None, "lat", "lon"),
            P(),
        ),
        out_specs=(
            P(None, "lat", "lon"),
            P(None, "lat", "lon"),
            P(None, "lat", "lon"),
            P(None, "lat", "lon"),
        ),
        check_vma=False,
    )
```

```python
import jax
import jax.numpy as jnp
from jax import lax
from jax.sharding import PartitionSpec as P

TIME_STEP = 0.25
EXPANSION = 0.2
CONTRACTION = 0.8
BOTTOM_DRAG = 1.0
HALO = 2


def pressure(temp_part, salt_part, layer_height):
    layer_mass = (CONTRACTION * salt_part - EXPANSION * temp_part) * layer_height[:, None, None]
    return jnp.cumsum(layer_mass, axis=0) - 0.5 * layer_mass


def mix_vertically(fields, water_share, diapycnal_diffusivity, layer_height):
    contrast = fields[:, 1:] - fields[:, :-1]
    fluxes = diapycnal_diffusivity * (water_share[1:] * water_share[:-1]) * contrast
    boundary = jnp.zeros_like(fluxes[:, :1])
    flux_below = jnp.concatenate([fluxes, boundary], axis=1)
    flux_above = jnp.concatenate([boundary, fluxes], axis=1)
    return (flux_below - flux_above) / (layer_height * layer_height)[None, :, None, None]


def advance(
    central,
    eastern,
    western,
    northern,
    southern,
    at_bottom,
    zonal_spacing,
    meridional_spacing,
    planetary_rotation_factor,
    horizontal_eddy_coefficient,
    diapycnal_diffusivity,
    layer_height,
):
    water_share = central[4]
    fields = central[:4]
    weight_east = water_share * eastern[4]
    weight_west = water_share * western[4]
    weight_north = water_share * northern[4]
    weight_south = water_share * southern[4]
    diffusion = horizontal_eddy_coefficient * (
        (weight_east * (eastern[:4] - fields) + weight_west * (western[:4] - fields))
        / (zonal_spacing * zonal_spacing)
        + (weight_north * (northern[:4] - fields) + weight_south * (southern[:4] - fields))
        / (meridional_spacing * meridional_spacing)
    )
    zonal = fields[2]
    merid = fields[3]
    advection = -(
        zonal * (eastern[:4] - western[:4]) * (0.5 / zonal_spacing)
        + merid * (northern[:4] - southern[:4]) * (0.5 / meridional_spacing)
    )
    pressure_east = pressure(eastern[0], eastern[1], layer_height)
    pressure_west = pressure(western[0], western[1], layer_height)
    pressure_north = pressure(northern[0], northern[1], layer_height)
    pressure_south = pressure(southern[0], southern[1], layer_height)
    gradient_x = -(pressure_east - pressure_west) * (0.5 / zonal_spacing)
    gradient_y = -(pressure_north - pressure_south) * (0.5 / meridional_spacing)
    mixing = mix_vertically(fields, water_share, diapycnal_diffusivity, layer_height)
    tendency = advection + diffusion + mixing
    tend_zonal = (
        tendency[2]
        + planetary_rotation_factor * merid
        + gradient_x
        - BOTTOM_DRAG * at_bottom * zonal
    )
    tend_merid = (
        tendency[3]
        - planetary_rotation_factor * zonal
        + gradient_y
        - BOTTOM_DRAG * at_bottom * merid
    )
    tendency = jnp.stack([tendency[0], tendency[1], tend_zonal, tend_merid])
    updated = water_share * (fields + TIME_STEP * tendency)
    return jnp.concatenate([updated, water_share[None]], axis=0)


def step(state, params, levels, layer_height):
    floor_index = params[0]
    at_bottom = (
        lax.broadcasted_iota(jnp.int32, (levels, 1, 1), 0).astype(jnp.float32) == floor_index[None]
    ).astype(jnp.float32)
    return advance(
        state[:, :, 1:-1, 1:-1],
        state[:, :, 1:-1, 2:],
        state[:, :, 1:-1, :-2],
        state[:, :, 2:, 1:-1],
        state[:, :, :-2, 1:-1],
        at_bottom,
        params[1],
        params[2],
        params[3],
        params[4],
        params[5:8],
        layer_height,
    )


def fold_pairs(lon_count, lat_count, target_of):
    top = lat_count - 1
    return [(i * lat_count + top, (target_of(i) % lon_count) * lat_count + top) for i in range(lon_count)]


def exchange(block, sign):
    lon_count = lax.axis_size("lon")
    lat_count = lax.axis_size("lat")
    h = HALO

    east_pairs = [(i, (i + 1) % lon_count) for i in range(lon_count)]
    west_pairs = [(j, i) for i, j in east_pairs]
    west = lax.ppermute(block[:, :, -h:], "lon", east_pairs)
    east = lax.ppermute(block[:, :, :h], "lon", west_pairs)

    axes = ("lon", "lat")
    rows_hi = block[:, -h:, :]
    mirror = lax.ppermute(rows_hi, axes, fold_pairs(lon_count, lat_count, lambda i: lon_count - 1 - i))
    mirror_lo = lax.ppermute(
        rows_hi[:, :, :h], axes, fold_pairs(lon_count, lat_count, lambda i: lon_count - i)
    )
    mirror_hi = lax.ppermute(
        rows_hi[:, :, -h:], axes, fold_pairs(lon_count, lat_count, lambda i: lon_count - 2 - i)
    )
    mirrored = jnp.concatenate([mirror_hi, mirror, mirror_lo], axis=2)
    folded = mirrored[:, ::-1, ::-1] * sign[:, None, None]

    middle = jnp.concatenate([west, block, east], axis=2)
    north_pairs = [(j, j + 1) for j in range(lat_count - 1)]
    south_pairs = [(j, i) for i, j in north_pairs]
    south = lax.ppermute(middle[:, -h:, :], "lat", north_pairs)
    north = lax.ppermute(middle[:, :h, :], "lat", south_pairs)
    is_top = lax.axis_index("lat") == lat_count - 1
    north = jnp.where(is_top, folded, north)
    return jnp.concatenate([south, middle, north], axis=1)


def shards(
    potential_heat,
    salt_anomaly_field,
    zonal_current,
    meridional_current,
    water_indicator,
    floor_layer_index,
    zonal_spacing,
    meridional_spacing,
    planetary_rotation_factor,
    horizontal_eddy_coefficient,
    diapycnal_diffusivity,
    layer_height,
):
    water_share = water_indicator.astype(jnp.float32)
    state = jnp.stack(
        [
            potential_heat * water_share,
            salt_anomaly_field * water_share,
            zonal_current * water_share,
            meridional_current * water_share,
            water_share,
        ]
    )
    channels, levels, rows, cols = state.shape
    params = jnp.concatenate(
        [
            jnp.stack(
                [
                    floor_layer_index.astype(jnp.float32),
                    zonal_spacing,
                    meridional_spacing,
                    planetary_rotation_factor,
                    horizontal_eddy_coefficient,
                ]
            ),
            diapycnal_diffusivity,
        ]
    )
    planes = jnp.concatenate([state.reshape(channels * levels, rows, cols), params])
    channel_sign = jnp.array([1.0, 1.0, -1.0, -1.0, 1.0], jnp.float32)
    sign = jnp.concatenate(
        [jnp.repeat(channel_sign, levels), jnp.ones((params.shape[0],), jnp.float32)]
    )
    padded = exchange(planes, sign)
    n_state = channels * levels
    state0 = padded[:n_state].reshape(channels, levels, rows + 2 * HALO, cols + 2 * HALO)
    params_outer = padded[n_state:, 1:-1, 1:-1]
    state1 = step(state0, params_outer, levels, layer_height)
    is_bottom = lax.axis_index("lat") == 0
    first_row = jnp.where(is_bottom, 0.0, state1[:, :, :1, :])
    state1 = jnp.concatenate([first_row, state1[:, :, 1:, :]], axis=2)
    params_inner = params
    state2 = step(state1, params_inner, levels, layer_height)
    return (state2[0], state2[1], state2[2], state2[3])


def solution(mesh):
    return jax.shard_map(
        shards,
        mesh=mesh,
        in_specs=(
            P(None, "lat", "lon"),
            P(None, "lat", "lon"),
            P(None, "lat", "lon"),
            P(None, "lat", "lon"),
            P(None, "lat", "lon"),
            P("lat", "lon"),
            P("lat", "lon"),
            P("lat", "lon"),
            P("lat", "lon"),
            P("lat", "lon"),
            P(None, "lat", "lon"),
            P(),
        ),
        out_specs=(
            P(None, "lat", "lon"),
            P(None, "lat", "lon"),
            P(None, "lat", "lon"),
            P(None, "lat", "lon"),
        ),
        check_vma=False,
    )
```

```python
import jax
import jax.numpy as jnp
from jax import lax
from jax.sharding import PartitionSpec as P

TIME_STEP = 0.25
EXPANSION = 0.2
CONTRACTION = 0.8
BOTTOM_DRAG = 1.0
HALO = 2


def pressure(temp_part, salt_part, layer_height):
    layer_mass = (CONTRACTION * salt_part - EXPANSION * temp_part) * layer_height[:, None, None]
    return jnp.cumsum(layer_mass, axis=0) - 0.5 * layer_mass


def mix_vertically(fields, water_share, diapycnal_diffusivity, layer_height):
    contrast = fields[:, 1:] - fields[:, :-1]
    fluxes = diapycnal_diffusivity * (water_share[1:] * water_share[:-1]) * contrast
    boundary = jnp.zeros_like(fluxes[:, :1])
    flux_below = jnp.concatenate([fluxes, boundary], axis=1)
    flux_above = jnp.concatenate([boundary, fluxes], axis=1)
    return (flux_below - flux_above) / (layer_height * layer_height)[None, :, None, None]


def advance(
    central,
    eastern,
    western,
    northern,
    southern,
    at_bottom,
    zonal_spacing,
    meridional_spacing,
    planetary_rotation_factor,
    horizontal_eddy_coefficient,
    diapycnal_diffusivity,
    layer_height,
):
    water_share = central[4]
    fields = central[:4]
    weight_east = water_share * eastern[4]
    weight_west = water_share * western[4]
    weight_north = water_share * northern[4]
    weight_south = water_share * southern[4]
    diffusion = horizontal_eddy_coefficient * (
        (weight_east * (eastern[:4] - fields) + weight_west * (western[:4] - fields))
        / (zonal_spacing * zonal_spacing)
        + (weight_north * (northern[:4] - fields) + weight_south * (southern[:4] - fields))
        / (meridional_spacing * meridional_spacing)
    )
    zonal = fields[2]
    merid = fields[3]
    advection = -(
        zonal * (eastern[:4] - western[:4]) * (0.5 / zonal_spacing)
        + merid * (northern[:4] - southern[:4]) * (0.5 / meridional_spacing)
    )
    pressure_east = pressure(eastern[0], eastern[1], layer_height)
    pressure_west = pressure(western[0], western[1], layer_height)
    pressure_north = pressure(northern[0], northern[1], layer_height)
    pressure_south = pressure(southern[0], southern[1], layer_height)
    gradient_x = -(pressure_east - pressure_west) * (0.5 / zonal_spacing)
    gradient_y = -(pressure_north - pressure_south) * (0.5 / meridional_spacing)
    mixing = mix_vertically(fields, water_share, diapycnal_diffusivity, layer_height)
    tendency = advection + diffusion + mixing
    tend_zonal = (
        tendency[2]
        + planetary_rotation_factor * merid
        + gradient_x
        - BOTTOM_DRAG * at_bottom * zonal
    )
    tend_merid = (
        tendency[3]
        - planetary_rotation_factor * zonal
        + gradient_y
        - BOTTOM_DRAG * at_bottom * merid
    )
    tendency = jnp.stack([tendency[0], tendency[1], tend_zonal, tend_merid])
    updated = water_share * (fields + TIME_STEP * tendency)
    return jnp.concatenate([updated, water_share[None]], axis=0)


def step(state, params, levels, layer_height):
    floor_index = params[0]
    at_bottom = (
        lax.broadcasted_iota(jnp.int32, (levels, 1, 1), 0).astype(jnp.float32) == floor_index[None]
    ).astype(jnp.float32)
    return advance(
        state[:, :, 1:-1, 1:-1],
        state[:, :, 1:-1, 2:],
        state[:, :, 1:-1, :-2],
        state[:, :, 2:, 1:-1],
        state[:, :, :-2, 1:-1],
        at_bottom,
        params[1],
        params[2],
        params[3],
        params[4],
        params[5:8],
        layer_height,
    )


def fold_pairs(lon_count, lat_count, target_of):
    top = lat_count - 1
    return [(i * lat_count + top, (target_of(i) % lon_count) * lat_count + top) for i in range(lon_count)]


def exchange(block, sign):
    lon_count = lax.axis_size("lon")
    lat_count = lax.axis_size("lat")
    h = HALO

    east_pairs = [(i, (i + 1) % lon_count) for i in range(lon_count)]
    west_pairs = [(j, i) for i, j in east_pairs]
    west = lax.ppermute(block[:, :, -h:], "lon", east_pairs)
    east = lax.ppermute(block[:, :, :h], "lon", west_pairs)

    axes = ("lon", "lat")
    rows_hi = block[:, -h:, :]
    mirror = lax.ppermute(rows_hi, axes, fold_pairs(lon_count, lat_count, lambda i: lon_count - 1 - i))
    mirror_lo = lax.ppermute(
        rows_hi[:, :, :h], axes, fold_pairs(lon_count, lat_count, lambda i: lon_count - i)
    )
    mirror_hi = lax.ppermute(
        rows_hi[:, :, -h:], axes, fold_pairs(lon_count, lat_count, lambda i: lon_count - 2 - i)
    )
    mirrored = jnp.concatenate(
        [mirror_lo[:, :, ::-1], mirror[:, :, ::-1], mirror_hi[:, :, ::-1]], axis=2
    )
    folded = jnp.concatenate([mirrored[:, 1:2, :], mirrored[:, 0:1, :]], axis=1)
    folded = folded * sign[:, None, None]

    middle = jnp.concatenate([west, block, east], axis=2)
    north_pairs = [(j, j + 1) for j in range(lat_count - 1)]
    south_pairs = [(j, i) for i, j in north_pairs]
    south = lax.ppermute(middle[:, -h:, :], "lat", north_pairs)
    north = lax.ppermute(middle[:, :h, :], "lat", south_pairs)
    is_top = lax.axis_index("lat") == lat_count - 1
    north = jnp.where(is_top, folded, north)
    return jnp.concatenate([south, middle, north], axis=1)


def shards(
    potential_heat,
    salt_anomaly_field,
    zonal_current,
    meridional_current,
    water_indicator,
    floor_layer_index,
    zonal_spacing,
    meridional_spacing,
    planetary_rotation_factor,
    horizontal_eddy_coefficient,
    diapycnal_diffusivity,
    layer_height,
):
    water_share = water_indicator.astype(jnp.float32)
    state = jnp.stack(
        [
            potential_heat * water_share,
            salt_anomaly_field * water_share,
            zonal_current * water_share,
            meridional_current * water_share,
            water_share,
        ]
    )
    channels, levels, rows, cols = state.shape
    params = jnp.concatenate(
        [
            jnp.stack(
                [
                    floor_layer_index.astype(jnp.float32),
                    zonal_spacing,
                    meridional_spacing,
                    planetary_rotation_factor,
                    horizontal_eddy_coefficient,
                ]
            ),
            diapycnal_diffusivity,
        ]
    )
    planes = jnp.concatenate([state.reshape(channels * levels, rows, cols), params])
    channel_sign = jnp.array([1.0, 1.0, -1.0, -1.0, 1.0], jnp.float32)
    sign = jnp.concatenate(
        [jnp.repeat(channel_sign, levels), jnp.ones((params.shape[0],), jnp.float32)]
    )
    padded = exchange(planes, sign)
    n_state = channels * levels
    state0 = padded[:n_state].reshape(channels, levels, rows + 2 * HALO, cols + 2 * HALO)
    params_outer = padded[n_state:, 1:-1, 1:-1]
    state1 = step(state0, params_outer, levels, layer_height)
    is_bottom = lax.axis_index("lat") == 0
    first_row = jnp.where(is_bottom, 0.0, state1[:, :, :1, :])
    state1 = jnp.concatenate([first_row, state1[:, :, 1:, :]], axis=2)
    params_inner = params
    state2 = step(state1, params_inner, levels, layer_height)
    return (state2[0], state2[1], state2[2], state2[3])


def solution(mesh):
    return jax.shard_map(
        shards,
        mesh=mesh,
        in_specs=(
            P(None, "lat", "lon"),
            P(None, "lat", "lon"),
            P(None, "lat", "lon"),
            P(None, "lat", "lon"),
            P(None, "lat", "lon"),
            P("lat", "lon"),
            P("lat", "lon"),
            P("lat", "lon"),
            P("lat", "lon"),
            P("lat", "lon"),
            P(None, "lat", "lon"),
            P(),
        ),
        out_specs=(
            P(None, "lat", "lon"),
            P(None, "lat", "lon"),
            P(None, "lat", "lon"),
            P(None, "lat", "lon"),
        ),
        check_vma=False,
    )
```

```python
import jax
import jax.numpy as jnp
from jax import lax
from jax.sharding import PartitionSpec as P

TIME_STEP = 0.25
EXPANSION = 0.2
CONTRACTION = 0.8
BOTTOM_DRAG = 1.0
HALO = 2


def pressure(temp_part, salt_part, layer_height):
    layer_mass = (CONTRACTION * salt_part - EXPANSION * temp_part) * layer_height[:, None, None]
    return jnp.cumsum(layer_mass, axis=0) - 0.5 * layer_mass


def mix_vertically(fields, water_share, diapycnal_diffusivity, layer_height):
    contrast = fields[:, 1:] - fields[:, :-1]
    fluxes = diapycnal_diffusivity * (water_share[1:] * water_share[:-1]) * contrast
    boundary = jnp.zeros_like(fluxes[:, :1])
    flux_below = jnp.concatenate([fluxes, boundary], axis=1)
    flux_above = jnp.concatenate([boundary, fluxes], axis=1)
    return (flux_below - flux_above) / (layer_height * layer_height)[None, :, None, None]


def advance(
    central,
    eastern,
    western,
    northern,
    southern,
    at_bottom,
    zonal_spacing,
    meridional_spacing,
    planetary_rotation_factor,
    horizontal_eddy_coefficient,
    diapycnal_diffusivity,
    layer_height,
):
    water_share = central[4]
    fields = central[:4]
    weight_east = water_share * eastern[4]
    weight_west = water_share * western[4]
    weight_north = water_share * northern[4]
    weight_south = water_share * southern[4]
    diffusion = horizontal_eddy_coefficient * (
        (weight_east * (eastern[:4] - fields) + weight_west * (western[:4] - fields))
        / (zonal_spacing * zonal_spacing)
        + (weight_north * (northern[:4] - fields) + weight_south * (southern[:4] - fields))
        / (meridional_spacing * meridional_spacing)
    )
    zonal = fields[2]
    merid = fields[3]
    advection = -(
        zonal * (eastern[:4] - western[:4]) * (0.5 / zonal_spacing)
        + merid * (northern[:4] - southern[:4]) * (0.5 / meridional_spacing)
    )
    pressure_east = pressure(eastern[0], eastern[1], layer_height)
    pressure_west = pressure(western[0], western[1], layer_height)
    pressure_north = pressure(northern[0], northern[1], layer_height)
    pressure_south = pressure(southern[0], southern[1], layer_height)
    gradient_x = -(pressure_east - pressure_west) * (0.5 / zonal_spacing)
    gradient_y = -(pressure_north - pressure_south) * (0.5 / meridional_spacing)
    mixing = mix_vertically(fields, water_share, diapycnal_diffusivity, layer_height)
    tendency = advection + diffusion + mixing
    tend_zonal = (
        tendency[2]
        + planetary_rotation_factor * merid
        + gradient_x
        - BOTTOM_DRAG * at_bottom * zonal
    )
    tend_merid = (
        tendency[3]
        - planetary_rotation_factor * zonal
        + gradient_y
        - BOTTOM_DRAG * at_bottom * merid
    )
    tendency = jnp.stack([tendency[0], tendency[1], tend_zonal, tend_merid])
    updated = water_share * (fields + TIME_STEP * tendency)
    return jnp.concatenate([updated, water_share[None]], axis=0)


def step(state, params, levels, layer_height):
    floor_index = params[0]
    at_bottom = (
        lax.broadcasted_iota(jnp.int32, (levels, 1, 1), 0).astype(jnp.float32) == floor_index[None]
    ).astype(jnp.float32)
    return advance(
        state[:, :, 1:-1, 1:-1],
        state[:, :, 1:-1, 2:],
        state[:, :, 1:-1, :-2],
        state[:, :, 2:, 1:-1],
        state[:, :, :-2, 1:-1],
        at_bottom,
        params[1],
        params[2],
        params[3],
        params[4],
        params[5:8],
        layer_height,
    )


def fold_pairs(lon_count, lat_count, target_of):
    top = lat_count - 1
    return [(i * lat_count + top, (target_of(i) % lon_count) * lat_count + top) for i in range(lon_count)]


def exchange(take, sign):
    lon_count = lax.axis_size("lon")
    lat_count = lax.axis_size("lat")
    h = HALO
    every = slice(None)

    east_pairs = [(i, (i + 1) % lon_count) for i in range(lon_count)]
    west_pairs = [(j, i) for i, j in east_pairs]
    west = lax.ppermute(take(every, slice(-h, None)), "lon", east_pairs)
    east = lax.ppermute(take(every, slice(0, h)), "lon", west_pairs)

    axes = ("lon", "lat")
    rows_hi = take(slice(-h, None), every)
    rows_lo = take(slice(0, h), every)
    mirror = lax.ppermute(rows_hi, axes, fold_pairs(lon_count, lat_count, lambda i: lon_count - 1 - i))
    mirror_lo = lax.ppermute(
        rows_hi[:, :, :h], axes, fold_pairs(lon_count, lat_count, lambda i: lon_count - i)
    )
    mirror_hi = lax.ppermute(
        rows_hi[:, :, -h:], axes, fold_pairs(lon_count, lat_count, lambda i: lon_count - 2 - i)
    )
    mirrored = jnp.concatenate(
        [mirror_lo[:, :, ::-1], mirror[:, :, ::-1], mirror_hi[:, :, ::-1]], axis=2
    )
    folded = jnp.concatenate([mirrored[:, 1:2, :], mirrored[:, 0:1, :]], axis=1)
    folded = folded * sign[:, None, None]

    north_pairs = [(j, j + 1) for j in range(lat_count - 1)]
    south_pairs = [(j, i) for i, j in north_pairs]
    top_band = jnp.concatenate([west[:, -h:, :], rows_hi, east[:, -h:, :]], axis=2)
    bottom_band = jnp.concatenate([west[:, :h, :], rows_lo, east[:, :h, :]], axis=2)
    south = lax.ppermute(top_band, "lat", north_pairs)
    north = lax.ppermute(bottom_band, "lat", south_pairs)
    is_top = lax.axis_index("lat") == lat_count - 1
    north = jnp.where(is_top, folded, north)
    return west, east, south, north


def shards(
    potential_heat,
    salt_anomaly_field,
    zonal_current,
    meridional_current,
    water_indicator,
    floor_layer_index,
    zonal_spacing,
    meridional_spacing,
    planetary_rotation_factor,
    horizontal_eddy_coefficient,
    diapycnal_diffusivity,
    layer_height,
):
    fields = (potential_heat, salt_anomaly_field, zonal_current, meridional_current)
    surfaces = (
        floor_layer_index,
        zonal_spacing,
        meridional_spacing,
        planetary_rotation_factor,
        horizontal_eddy_coefficient,
    )

    def take(rs, cs):
        wet = water_indicator[:, rs, cs].astype(jnp.float32)
        parts = [f[:, rs, cs] * wet for f in fields] + [wet]
        parts += [s[None, rs, cs].astype(jnp.float32) for s in surfaces]
        parts.append(diapycnal_diffusivity[:, rs, cs])
        return jnp.concatenate(parts, axis=0)

    channels = len(fields) + 1
    levels, rows, cols = potential_heat.shape
    channel_sign = jnp.array([1.0, 1.0, -1.0, -1.0, 1.0], jnp.float32)
    sign = jnp.concatenate(
        [jnp.repeat(channel_sign, levels), jnp.ones((len(surfaces) + levels - 1,), jnp.float32)]
    )
    west, east, south, north = exchange(take, sign)
    every = slice(None)
    middle = jnp.concatenate([west, take(every, every), east], axis=2)
    padded = jnp.concatenate([south, middle, north], axis=1)
    n_state = channels * levels
    state0 = padded[:n_state].reshape(channels, levels, rows + 2 * HALO, cols + 2 * HALO)
    params_outer = padded[n_state:, 1:-1, 1:-1]
    state1 = step(state0, params_outer, levels, layer_height)
    is_bottom = lax.axis_index("lat") == 0
    first_row = jnp.where(is_bottom, 0.0, state1[:, :, :1, :])
    state1 = jnp.concatenate([first_row, state1[:, :, 1:, :]], axis=2)
    params_inner = padded[n_state:, HALO:-HALO, HALO:-HALO]
    state2 = step(state1, params_inner, levels, layer_height)
    return (state2[0], state2[1], state2[2], state2[3])


def solution(mesh):
    return jax.shard_map(
        shards,
        mesh=mesh,
        in_specs=(
            P(None, "lat", "lon"),
            P(None, "lat", "lon"),
            P(None, "lat", "lon"),
            P(None, "lat", "lon"),
            P(None, "lat", "lon"),
            P("lat", "lon"),
            P("lat", "lon"),
            P("lat", "lon"),
            P("lat", "lon"),
            P("lat", "lon"),
            P(None, "lat", "lon"),
            P(),
        ),
        out_specs=(
            P(None, "lat", "lon"),
            P(None, "lat", "lon"),
            P(None, "lat", "lon"),
            P(None, "lat", "lon"),
        ),
        check_vma=False,
    )
```

```python
import jax
import jax.numpy as jnp
from jax import lax
from jax.sharding import PartitionSpec as P

TIME_STEP = 0.25
EXPANSION = 0.2
CONTRACTION = 0.8
BOTTOM_DRAG = 1.0
HALO = 2


def pressure(temp_part, salt_part, layer_height):
    layer_mass = (CONTRACTION * salt_part - EXPANSION * temp_part) * layer_height[:, None, None]
    return jnp.cumsum(layer_mass, axis=0) - 0.5 * layer_mass


def mix_vertically(fields, water_share, diapycnal_diffusivity, layer_height):
    contrast = fields[:, 1:] - fields[:, :-1]
    fluxes = diapycnal_diffusivity * (water_share[1:] * water_share[:-1]) * contrast
    boundary = jnp.zeros_like(fluxes[:, :1])
    flux_below = jnp.concatenate([fluxes, boundary], axis=1)
    flux_above = jnp.concatenate([boundary, fluxes], axis=1)
    return (flux_below - flux_above) / (layer_height * layer_height)[None, :, None, None]


def advance(
    central,
    eastern,
    western,
    northern,
    southern,
    at_bottom,
    zonal_spacing,
    meridional_spacing,
    planetary_rotation_factor,
    horizontal_eddy_coefficient,
    diapycnal_diffusivity,
    layer_height,
):
    water_share = central[4]
    fields = central[:4]
    weight_east = water_share * eastern[4]
    weight_west = water_share * western[4]
    weight_north = water_share * northern[4]
    weight_south = water_share * southern[4]
    diffusion = horizontal_eddy_coefficient * (
        (weight_east * (eastern[:4] - fields) + weight_west * (western[:4] - fields))
        / (zonal_spacing * zonal_spacing)
        + (weight_north * (northern[:4] - fields) + weight_south * (southern[:4] - fields))
        / (meridional_spacing * meridional_spacing)
    )
    zonal = fields[2]
    merid = fields[3]
    advection = -(
        zonal * (eastern[:4] - western[:4]) * (0.5 / zonal_spacing)
        + merid * (northern[:4] - southern[:4]) * (0.5 / meridional_spacing)
    )
    pressure_east = pressure(eastern[0], eastern[1], layer_height)
    pressure_west = pressure(western[0], western[1], layer_height)
    pressure_north = pressure(northern[0], northern[1], layer_height)
    pressure_south = pressure(southern[0], southern[1], layer_height)
    gradient_x = -(pressure_east - pressure_west) * (0.5 / zonal_spacing)
    gradient_y = -(pressure_north - pressure_south) * (0.5 / meridional_spacing)
    mixing = mix_vertically(fields, water_share, diapycnal_diffusivity, layer_height)
    tendency = advection + diffusion + mixing
    tend_zonal = (
        tendency[2]
        + planetary_rotation_factor * merid
        + gradient_x
        - BOTTOM_DRAG * at_bottom * zonal
    )
    tend_merid = (
        tendency[3]
        - planetary_rotation_factor * zonal
        + gradient_y
        - BOTTOM_DRAG * at_bottom * merid
    )
    tendency = jnp.stack([tendency[0], tendency[1], tend_zonal, tend_merid])
    updated = water_share * (fields + TIME_STEP * tendency)
    return jnp.concatenate([updated, water_share[None]], axis=0)


def step(state, params, levels, layer_height):
    floor_index = params[0]
    at_bottom = (
        lax.broadcasted_iota(jnp.int32, (levels, 1, 1), 0).astype(jnp.float32) == floor_index[None]
    ).astype(jnp.float32)
    return advance(
        state[:, :, 1:-1, 1:-1],
        state[:, :, 1:-1, 2:],
        state[:, :, 1:-1, :-2],
        state[:, :, 2:, 1:-1],
        state[:, :, :-2, 1:-1],
        at_bottom,
        params[1],
        params[2],
        params[3],
        params[4],
        params[5:8],
        layer_height,
    )


def fold_pairs(lon_count, lat_count, target_of):
    top = lat_count - 1
    return [(i * lat_count + top, (target_of(i) % lon_count) * lat_count + top) for i in range(lon_count)]


def exchange(take, sign):
    lon_count = lax.axis_size("lon")
    lat_count = lax.axis_size("lat")
    h = HALO
    every = slice(None)

    east_pairs = [(i, (i + 1) % lon_count) for i in range(lon_count)]
    west_pairs = [(j, i) for i, j in east_pairs]
    west = lax.ppermute(take(every, slice(-h, None)), "lon", east_pairs)
    east = lax.ppermute(take(every, slice(0, h)), "lon", west_pairs)

    axes = ("lon", "lat")
    rows_hi = take(slice(-h, None), every)
    rows_lo = take(slice(0, h), every)
    mirror = lax.ppermute(rows_hi, axes, fold_pairs(lon_count, lat_count, lambda i: lon_count - 1 - i))
    mirror_lo = lax.ppermute(
        rows_hi[:, :, :h], axes, fold_pairs(lon_count, lat_count, lambda i: lon_count - i)
    )
    mirror_hi = lax.ppermute(
        rows_hi[:, :, -h:], axes, fold_pairs(lon_count, lat_count, lambda i: lon_count - 2 - i)
    )
    mirrored = jnp.concatenate(
        [mirror_lo[:, :, ::-1], mirror[:, :, ::-1], mirror_hi[:, :, ::-1]], axis=2
    )
    folded = jnp.concatenate([mirrored[:, 1:2, :], mirrored[:, 0:1, :]], axis=1)
    folded = folded * sign[:, None, None]

    north_pairs = [(j, j + 1) for j in range(lat_count - 1)]
    south_pairs = [(j, i) for i, j in north_pairs]
    top_band = jnp.concatenate([west[:, -h:, :], rows_hi, east[:, -h:, :]], axis=2)
    bottom_band = jnp.concatenate([west[:, :h, :], rows_lo, east[:, :h, :]], axis=2)
    south = lax.ppermute(top_band, "lat", north_pairs)
    north = lax.ppermute(bottom_band, "lat", south_pairs)
    is_top = lax.axis_index("lat") == lat_count - 1
    north = jnp.where(is_top, folded, north)
    return west, east, south, north


def shards(
    potential_heat,
    salt_anomaly_field,
    zonal_current,
    meridional_current,
    water_indicator,
    floor_layer_index,
    zonal_spacing,
    meridional_spacing,
    planetary_rotation_factor,
    horizontal_eddy_coefficient,
    diapycnal_diffusivity,
    layer_height,
):
    fields = (potential_heat, salt_anomaly_field, zonal_current, meridional_current)
    surfaces = (
        floor_layer_index,
        zonal_spacing,
        meridional_spacing,
        planetary_rotation_factor,
        horizontal_eddy_coefficient,
    )

    def take(rs, cs):
        wet = water_indicator[:, rs, cs].astype(jnp.float32)
        parts = [f[:, rs, cs] * wet for f in fields] + [wet]
        parts += [s[None, rs, cs].astype(jnp.float32) for s in surfaces]
        parts.append(diapycnal_diffusivity[:, rs, cs])
        return jnp.concatenate(parts, axis=0)

    channels = len(fields) + 1
    levels, rows, cols = potential_heat.shape
    channel_sign = jnp.array([1.0, 1.0, -1.0, -1.0, 1.0], jnp.float32)
    sign = jnp.concatenate(
        [jnp.repeat(channel_sign, levels), jnp.ones((len(surfaces) + levels - 1,), jnp.float32)]
    )
    west, east, south, north = exchange(take, sign)
    every = slice(None)
    n_state = channels * levels

    def split(planes):
        count = planes.shape[1]
        return planes[:n_state].reshape(channels, levels, count, planes.shape[2]), planes[n_state:]

    middle = jnp.concatenate([west, take(every, every), east], axis=2)
    state_mid, params_mid = split(middle)
    inner = slice(HALO, -HALO)
    state1_core = step(state_mid, params_mid[:, 1:-1, 1:-1], levels, layer_height)
    state2_core = step(state1_core, params_mid[:, 2:-2, inner], levels, layer_height)

    state_low, params_low = split(jnp.concatenate([south, middle[:, :HALO]], axis=1))
    state1_low = step(state_low, params_low[:, 1:-1, 1:-1], levels, layer_height)
    is_bottom = lax.axis_index("lat") == 0
    state1_low = jnp.concatenate(
        [jnp.where(is_bottom, 0.0, state1_low[:, :, :1]), state1_low[:, :, 1:]], axis=2
    )
    state_high, params_high = split(jnp.concatenate([middle[:, -HALO:], north], axis=1))
    state1_high = step(state_high, params_high[:, 1:-1, 1:-1], levels, layer_height)

    band_low = jnp.concatenate([state1_low, state1_core[:, :, :2]], axis=2)
    state2_low = step(band_low, params_mid[:, :2, inner], levels, layer_height)
    band_high = jnp.concatenate([state1_core[:, :, -2:], state1_high], axis=2)
    state2_high = step(band_high, params_mid[:, -2:, inner], levels, layer_height)
    state2 = jnp.concatenate([state2_low, state2_core, state2_high], axis=2)
    return (state2[0], state2[1], state2[2], state2[3])


def solution(mesh):
    return jax.shard_map(
        shards,
        mesh=mesh,
        in_specs=(
            P(None, "lat", "lon"),
            P(None, "lat", "lon"),
            P(None, "lat", "lon"),
            P(None, "lat", "lon"),
            P(None, "lat", "lon"),
            P("lat", "lon"),
            P("lat", "lon"),
            P("lat", "lon"),
            P("lat", "lon"),
            P("lat", "lon"),
            P(None, "lat", "lon"),
            P(),
        ),
        out_specs=(
            P(None, "lat", "lon"),
            P(None, "lat", "lon"),
            P(None, "lat", "lon"),
            P(None, "lat", "lon"),
        ),
        check_vma=False,
    )
```

```python
import jax
import jax.numpy as jnp
from jax import lax
from jax.sharding import PartitionSpec as P

TIME_STEP = 0.25
EXPANSION = 0.2
CONTRACTION = 0.8
BOTTOM_DRAG = 1.0
HALO = 2


def pressure(temp_part, salt_part, layer_height):
    layer_mass = (CONTRACTION * salt_part - EXPANSION * temp_part) * layer_height[:, None, None]
    running = [layer_mass[0]]
    for level in range(1, layer_mass.shape[0]):
        running.append(running[-1] + layer_mass[level])
    return jnp.stack(running) - 0.5 * layer_mass


def mix_vertically(fields, water_share, diapycnal_diffusivity, layer_height):
    contrast = fields[:, 1:] - fields[:, :-1]
    fluxes = diapycnal_diffusivity * (water_share[1:] * water_share[:-1]) * contrast
    boundary = jnp.zeros_like(fluxes[:, :1])
    flux_below = jnp.concatenate([fluxes, boundary], axis=1)
    flux_above = jnp.concatenate([boundary, fluxes], axis=1)
    return (flux_below - flux_above) / (layer_height * layer_height)[None, :, None, None]


def advance(
    central,
    eastern,
    western,
    northern,
    southern,
    at_bottom,
    zonal_spacing,
    meridional_spacing,
    planetary_rotation_factor,
    horizontal_eddy_coefficient,
    diapycnal_diffusivity,
    layer_height,
    pressures,
):
    water_share = central[4]
    fields = central[:4]
    weight_east = water_share * eastern[4]
    weight_west = water_share * western[4]
    weight_north = water_share * northern[4]
    weight_south = water_share * southern[4]
    diffusion = horizontal_eddy_coefficient * (
        (weight_east * (eastern[:4] - fields) + weight_west * (western[:4] - fields))
        / (zonal_spacing * zonal_spacing)
        + (weight_north * (northern[:4] - fields) + weight_south * (southern[:4] - fields))
        / (meridional_spacing * meridional_spacing)
    )
    zonal = fields[2]
    merid = fields[3]
    advection = -(
        zonal * (eastern[:4] - western[:4]) * (0.5 / zonal_spacing)
        + merid * (northern[:4] - southern[:4]) * (0.5 / meridional_spacing)
    )
    pressure_east, pressure_west, pressure_north, pressure_south = pressures
    gradient_x = -(pressure_east - pressure_west) * (0.5 / zonal_spacing)
    gradient_y = -(pressure_north - pressure_south) * (0.5 / meridional_spacing)
    mixing = mix_vertically(fields, water_share, diapycnal_diffusivity, layer_height)
    tendency = advection + diffusion + mixing
    tend_zonal = (
        tendency[2]
        + planetary_rotation_factor * merid
        + gradient_x
        - BOTTOM_DRAG * at_bottom * zonal
    )
    tend_merid = (
        tendency[3]
        - planetary_rotation_factor * zonal
        + gradient_y
        - BOTTOM_DRAG * at_bottom * merid
    )
    tendency = jnp.stack([tendency[0], tendency[1], tend_zonal, tend_merid])
    updated = water_share * (fields + TIME_STEP * tendency)
    return jnp.concatenate([updated, water_share[None]], axis=0)


def step(state, params, levels, layer_height):
    floor_index = params[0]
    at_bottom = (
        lax.broadcasted_iota(jnp.int32, (levels, 1, 1), 0).astype(jnp.float32) == floor_index[None]
    ).astype(jnp.float32)
    column = pressure(state[0], state[1], layer_height)
    pressures = (
        column[:, 1:-1, 2:],
        column[:, 1:-1, :-2],
        column[:, 2:, 1:-1],
        column[:, :-2, 1:-1],
    )
    return advance(
        state[:, :, 1:-1, 1:-1],
        state[:, :, 1:-1, 2:],
        state[:, :, 1:-1, :-2],
        state[:, :, 2:, 1:-1],
        state[:, :, :-2, 1:-1],
        at_bottom,
        params[1],
        params[2],
        params[3],
        params[4],
        params[5:8],
        layer_height,
        pressures,
    )


def fold_pairs(lon_count, lat_count, target_of):
    top = lat_count - 1
    return [(i * lat_count + top, (target_of(i) % lon_count) * lat_count + top) for i in range(lon_count)]


def exchange(take, sign):
    lon_count = lax.axis_size("lon")
    lat_count = lax.axis_size("lat")
    h = HALO
    every = slice(None)

    east_pairs = [(i, (i + 1) % lon_count) for i in range(lon_count)]
    west_pairs = [(j, i) for i, j in east_pairs]
    west = lax.ppermute(take(every, slice(-h, None)), "lon", east_pairs)
    east = lax.ppermute(take(every, slice(0, h)), "lon", west_pairs)

    axes = ("lon", "lat")
    rows_hi = take(slice(-h, None), every)
    rows_lo = take(slice(0, h), every)
    mirror = lax.ppermute(rows_hi, axes, fold_pairs(lon_count, lat_count, lambda i: lon_count - 1 - i))
    mirror_lo = lax.ppermute(
        rows_hi[:, :, :h], axes, fold_pairs(lon_count, lat_count, lambda i: lon_count - i)
    )
    mirror_hi = lax.ppermute(
        rows_hi[:, :, -h:], axes, fold_pairs(lon_count, lat_count, lambda i: lon_count - 2 - i)
    )
    mirrored = jnp.concatenate(
        [mirror_lo[:, :, ::-1], mirror[:, :, ::-1], mirror_hi[:, :, ::-1]], axis=2
    )
    folded = jnp.concatenate([mirrored[:, 1:2, :], mirrored[:, 0:1, :]], axis=1)
    folded = folded * sign[:, None, None]

    north_pairs = [(j, j + 1) for j in range(lat_count - 1)]
    south_pairs = [(j, i) for i, j in north_pairs]
    top_band = jnp.concatenate([west[:, -h:, :], rows_hi, east[:, -h:, :]], axis=2)
    bottom_band = jnp.concatenate([west[:, :h, :], rows_lo, east[:, :h, :]], axis=2)
    south = lax.ppermute(top_band, "lat", north_pairs)
    north = lax.ppermute(bottom_band, "lat", south_pairs)
    is_top = lax.axis_index("lat") == lat_count - 1
    north = jnp.where(is_top, folded, north)
    return west, east, south, north


def shards(
    potential_heat,
    salt_anomaly_field,
    zonal_current,
    meridional_current,
    water_indicator,
    floor_layer_index,
    zonal_spacing,
    meridional_spacing,
    planetary_rotation_factor,
    horizontal_eddy_coefficient,
    diapycnal_diffusivity,
    layer_height,
):
    fields = (potential_heat, salt_anomaly_field, zonal_current, meridional_current)
    surfaces = (
        floor_layer_index,
        zonal_spacing,
        meridional_spacing,
        planetary_rotation_factor,
        horizontal_eddy_coefficient,
    )

    def take(rs, cs):
        wet = water_indicator[:, rs, cs].astype(jnp.float32)
        parts = [f[:, rs, cs] * wet for f in fields] + [wet]
        parts += [s[None, rs, cs].astype(jnp.float32) for s in surfaces]
        parts.append(diapycnal_diffusivity[:, rs, cs])
        return jnp.concatenate(parts, axis=0)

    channels = len(fields) + 1
    levels, rows, cols = potential_heat.shape
    channel_sign = jnp.array([1.0, 1.0, -1.0, -1.0, 1.0], jnp.float32)
    sign = jnp.concatenate(
        [jnp.repeat(channel_sign, levels), jnp.ones((len(surfaces) + levels - 1,), jnp.float32)]
    )
    west, east, south, north = exchange(take, sign)
    every = slice(None)
    middle = jnp.concatenate([west, take(every, every), east], axis=2)
    padded = jnp.concatenate([south, middle, north], axis=1)
    n_state = channels * levels
    state0 = padded[:n_state].reshape(channels, levels, rows + 2 * HALO, cols + 2 * HALO)
    params_outer = padded[n_state:, 1:-1, 1:-1]
    state1 = step(state0, params_outer, levels, layer_height)
    is_bottom = lax.axis_index("lat") == 0
    first_row = jnp.where(is_bottom, 0.0, state1[:, :, :1, :])
    state1 = jnp.concatenate([first_row, state1[:, :, 1:, :]], axis=2)
    params_inner = padded[n_state:, HALO:-HALO, HALO:-HALO]
    state2 = step(state1, params_inner, levels, layer_height)
    return (state2[0], state2[1], state2[2], state2[3])


def solution(mesh):
    return jax.shard_map(
        shards,
        mesh=mesh,
        in_specs=(
            P(None, "lat", "lon"),
            P(None, "lat", "lon"),
            P(None, "lat", "lon"),
            P(None, "lat", "lon"),
            P(None, "lat", "lon"),
            P("lat", "lon"),
            P("lat", "lon"),
            P("lat", "lon"),
            P("lat", "lon"),
            P("lat", "lon"),
            P(None, "lat", "lon"),
            P(),
        ),
        out_specs=(
            P(None, "lat", "lon"),
            P(None, "lat", "lon"),
            P(None, "lat", "lon"),
            P(None, "lat", "lon"),
        ),
        check_vma=False,
    )
```

```python
import jax
import jax.numpy as jnp
from jax import lax
from jax.sharding import PartitionSpec as P

TIME_STEP = 0.25
EXPANSION = 0.2
CONTRACTION = 0.8
BOTTOM_DRAG = 1.0
HALO = 2


def pressure(temp_part, salt_part, layer_height):
    layer_mass = (CONTRACTION * salt_part - EXPANSION * temp_part) * layer_height[:, None, None]
    return jnp.cumsum(layer_mass, axis=0) - 0.5 * layer_mass


def mix_vertically(fields, water_share, diapycnal_diffusivity, layer_height):
    contrast = fields[:, 1:] - fields[:, :-1]
    fluxes = diapycnal_diffusivity * (water_share[1:] * water_share[:-1]) * contrast
    boundary = jnp.zeros_like(fluxes[:, :1])
    flux_below = jnp.concatenate([fluxes, boundary], axis=1)
    flux_above = jnp.concatenate([boundary, fluxes], axis=1)
    return (flux_below - flux_above) / (layer_height * layer_height)[None, :, None, None]


def advance(
    central,
    eastern,
    western,
    northern,
    southern,
    at_bottom,
    zonal_spacing,
    meridional_spacing,
    planetary_rotation_factor,
    horizontal_eddy_coefficient,
    diapycnal_diffusivity,
    layer_height,
):
    water_share = central[4]
    fields = central[:4]
    weight_east = water_share * eastern[4]
    weight_west = water_share * western[4]
    weight_north = water_share * northern[4]
    weight_south = water_share * southern[4]
    diffusion = horizontal_eddy_coefficient * (
        (weight_east * (eastern[:4] - fields) + weight_west * (western[:4] - fields))
        / (zonal_spacing * zonal_spacing)
        + (weight_north * (northern[:4] - fields) + weight_south * (southern[:4] - fields))
        / (meridional_spacing * meridional_spacing)
    )
    zonal = fields[2]
    merid = fields[3]
    advection = -(
        zonal * (eastern[:4] - western[:4]) * (0.5 / zonal_spacing)
        + merid * (northern[:4] - southern[:4]) * (0.5 / meridional_spacing)
    )
    pressure_east = pressure(eastern[0], eastern[1], layer_height)
    pressure_west = pressure(western[0], western[1], layer_height)
    pressure_north = pressure(northern[0], northern[1], layer_height)
    pressure_south = pressure(southern[0], southern[1], layer_height)
    gradient_x = -(pressure_east - pressure_west) * (0.5 / zonal_spacing)
    gradient_y = -(pressure_north - pressure_south) * (0.5 / meridional_spacing)
    mixing = mix_vertically(fields, water_share, diapycnal_diffusivity, layer_height)
    tendency = advection + diffusion + mixing
    tend_zonal = (
        tendency[2]
        + planetary_rotation_factor * merid
        + gradient_x
        - BOTTOM_DRAG * at_bottom * zonal
    )
    tend_merid = (
        tendency[3]
        - planetary_rotation_factor * zonal
        + gradient_y
        - BOTTOM_DRAG * at_bottom * merid
    )
    tendency = jnp.stack([tendency[0], tendency[1], tend_zonal, tend_merid])
    updated = water_share * (fields + TIME_STEP * tendency)
    return jnp.concatenate([updated, water_share[None]], axis=0)


def step(state, params, levels, layer_height):
    floor_index = params[0]
    at_bottom = (
        lax.broadcasted_iota(jnp.int32, (levels, 1, 1), 0).astype(jnp.float32) == floor_index[None]
    ).astype(jnp.float32)
    return advance(
        state[:, :, 1:-1, 1:-1],
        state[:, :, 1:-1, 2:],
        state[:, :, 1:-1, :-2],
        state[:, :, 2:, 1:-1],
        state[:, :, :-2, 1:-1],
        at_bottom,
        params[1],
        params[2],
        params[3],
        params[4],
        params[5:8],
        layer_height,
    )


def fold_pairs(lon_count, lat_count, target_of):
    top = lat_count - 1
    return [(i * lat_count + top, (target_of(i) % lon_count) * lat_count + top) for i in range(lon_count)]


def exchange(take, sign):
    lon_count = lax.axis_size("lon")
    lat_count = lax.axis_size("lat")
    h = HALO
    every = slice(None)

    east_pairs = [(i, (i + 1) % lon_count) for i in range(lon_count)]
    west_pairs = [(j, i) for i, j in east_pairs]
    west = lax.ppermute(take(every, slice(-h, None)), "lon", east_pairs)
    east = lax.ppermute(take(every, slice(0, h)), "lon", west_pairs)

    rows_hi = take(slice(-h, None), every)
    rows_lo = take(slice(0, h), every)
    top_band = jnp.concatenate([west[:, -h:, :], rows_hi, east[:, -h:, :]], axis=2)
    bottom_band = jnp.concatenate([west[:, :h, :], rows_lo, east[:, :h, :]], axis=2)

    mirror = lax.ppermute(
        top_band, ("lon", "lat"), fold_pairs(lon_count, lat_count, lambda i: lon_count - 1 - i)
    )
    mirrored = mirror[:, :, ::-1]
    folded = jnp.concatenate([mirrored[:, 1:2, :], mirrored[:, 0:1, :]], axis=1)
    folded = folded * sign[:, None, None]

    north_pairs = [(j, j + 1) for j in range(lat_count - 1)]
    south_pairs = [(j, i) for i, j in north_pairs]
    south = lax.ppermute(top_band, "lat", north_pairs)
    north = lax.ppermute(bottom_band, "lat", south_pairs)
    is_top = lax.axis_index("lat") == lat_count - 1
    north = jnp.where(is_top, folded, north)
    return west, east, south, north


def shards(
    potential_heat,
    salt_anomaly_field,
    zonal_current,
    meridional_current,
    water_indicator,
    floor_layer_index,
    zonal_spacing,
    meridional_spacing,
    planetary_rotation_factor,
    horizontal_eddy_coefficient,
    diapycnal_diffusivity,
    layer_height,
):
    fields = (potential_heat, salt_anomaly_field, zonal_current, meridional_current)
    surfaces = (
        floor_layer_index,
        zonal_spacing,
        meridional_spacing,
        planetary_rotation_factor,
        horizontal_eddy_coefficient,
    )

    def take(rs, cs):
        wet = water_indicator[:, rs, cs].astype(jnp.float32)
        parts = [f[:, rs, cs] * wet for f in fields] + [wet]
        parts += [s[None, rs, cs].astype(jnp.float32) for s in surfaces]
        parts.append(diapycnal_diffusivity[:, rs, cs])
        return jnp.concatenate(parts, axis=0)

    channels = len(fields) + 1
    levels, rows, cols = potential_heat.shape
    channel_sign = jnp.array([1.0, 1.0, -1.0, -1.0, 1.0], jnp.float32)
    sign = jnp.concatenate(
        [jnp.repeat(channel_sign, levels), jnp.ones((len(surfaces) + levels - 1,), jnp.float32)]
    )
    west, east, south, north = exchange(take, sign)
    every = slice(None)
    middle = jnp.concatenate([west, take(every, every), east], axis=2)
    padded = jnp.concatenate([south, middle, north], axis=1)
    n_state = channels * levels
    state0 = padded[:n_state].reshape(channels, levels, rows + 2 * HALO, cols + 2 * HALO)
    params_outer = padded[n_state:, 1:-1, 1:-1]
    state1 = step(state0, params_outer, levels, layer_height)
    is_bottom = lax.axis_index("lat") == 0
    first_row = jnp.where(is_bottom, 0.0, state1[:, :, :1, :])
    state1 = jnp.concatenate([first_row, state1[:, :, 1:, :]], axis=2)
    params_inner = padded[n_state:, HALO:-HALO, HALO:-HALO]
    state2 = step(state1, params_inner, levels, layer_height)
    return (state2[0], state2[1], state2[2], state2[3])


def solution(mesh):
    return jax.shard_map(
        shards,
        mesh=mesh,
        in_specs=(
            P(None, "lat", "lon"),
            P(None, "lat", "lon"),
            P(None, "lat", "lon"),
            P(None, "lat", "lon"),
            P(None, "lat", "lon"),
            P("lat", "lon"),
            P("lat", "lon"),
            P("lat", "lon"),
            P("lat", "lon"),
            P("lat", "lon"),
            P(None, "lat", "lon"),
            P(),
        ),
        out_specs=(
            P(None, "lat", "lon"),
            P(None, "lat", "lon"),
            P(None, "lat", "lon"),
            P(None, "lat", "lon"),
        ),
        check_vma=False,
    )
```

```python
import jax
import jax.numpy as jnp
from jax import lax
from jax.sharding import PartitionSpec as P
from jax.experimental import pallas as pl
from jax.experimental.pallas import tpu as pltpu

TIME_STEP = 0.25
EXPANSION = 0.2
CONTRACTION = 0.8
BOTTOM_DRAG = 1.0
HALO = 2


def pressure(temp_part, salt_part, layer_height):
    layer_mass = (CONTRACTION * salt_part - EXPANSION * temp_part) * layer_height[:, None, None]
    return jnp.cumsum(layer_mass, axis=0) - 0.5 * layer_mass


def mix_vertically(fields, water_share, diapycnal_diffusivity, layer_height):
    contrast = fields[:, 1:] - fields[:, :-1]
    fluxes = diapycnal_diffusivity * (water_share[1:] * water_share[:-1]) * contrast
    boundary = jnp.zeros_like(fluxes[:, :1])
    flux_below = jnp.concatenate([fluxes, boundary], axis=1)
    flux_above = jnp.concatenate([boundary, fluxes], axis=1)
    return (flux_below - flux_above) / (layer_height * layer_height)[None, :, None, None]


def advance(
    central,
    eastern,
    western,
    northern,
    southern,
    at_bottom,
    zonal_spacing,
    meridional_spacing,
    planetary_rotation_factor,
    horizontal_eddy_coefficient,
    diapycnal_diffusivity,
    layer_height,
):
    water_share = central[4]
    fields = central[:4]
    weight_east = water_share * eastern[4]
    weight_west = water_share * western[4]
    weight_north = water_share * northern[4]
    weight_south = water_share * southern[4]
    diffusion = horizontal_eddy_coefficient * (
        (weight_east * (eastern[:4] - fields) + weight_west * (western[:4] - fields))
        / (zonal_spacing * zonal_spacing)
        + (weight_north * (northern[:4] - fields) + weight_south * (southern[:4] - fields))
        / (meridional_spacing * meridional_spacing)
    )
    zonal = fields[2]
    merid = fields[3]
    advection = -(
        zonal * (eastern[:4] - western[:4]) * (0.5 / zonal_spacing)
        + merid * (northern[:4] - southern[:4]) * (0.5 / meridional_spacing)
    )
    pressure_east = pressure(eastern[0], eastern[1], layer_height)
    pressure_west = pressure(western[0], western[1], layer_height)
    pressure_north = pressure(northern[0], northern[1], layer_height)
    pressure_south = pressure(southern[0], southern[1], layer_height)
    gradient_x = -(pressure_east - pressure_west) * (0.5 / zonal_spacing)
    gradient_y = -(pressure_north - pressure_south) * (0.5 / meridional_spacing)
    mixing = mix_vertically(fields, water_share, diapycnal_diffusivity, layer_height)
    tendency = advection + diffusion + mixing
    tend_zonal = (
        tendency[2]
        + planetary_rotation_factor * merid
        + gradient_x
        - BOTTOM_DRAG * at_bottom * zonal
    )
    tend_merid = (
        tendency[3]
        - planetary_rotation_factor * zonal
        + gradient_y
        - BOTTOM_DRAG * at_bottom * merid
    )
    tendency = jnp.stack([tendency[0], tendency[1], tend_zonal, tend_merid])
    updated = water_share * (fields + TIME_STEP * tendency)
    return jnp.concatenate([updated, water_share[None]], axis=0)


def step(state, params, levels, layer_height):
    floor_index = params[0]
    at_bottom = (
        lax.broadcasted_iota(jnp.int32, (levels, 1, 1), 0).astype(jnp.float32) == floor_index[None]
    ).astype(jnp.float32)
    return advance(
        state[:, :, 1:-1, 1:-1],
        state[:, :, 1:-1, 2:],
        state[:, :, 1:-1, :-2],
        state[:, :, 2:, 1:-1],
        state[:, :, :-2, 1:-1],
        at_bottom,
        params[1],
        params[2],
        params[3],
        params[4],
        params[5:8],
        layer_height,
    )


def fold_pairs(lon_count, lat_count, target_of):
    top = lat_count - 1
    return [(i * lat_count + top, (target_of(i) % lon_count) * lat_count + top) for i in range(lon_count)]


def exchange(take, sign):
    lon_count = lax.axis_size("lon")
    lat_count = lax.axis_size("lat")
    h = HALO
    every = slice(None)

    east_pairs = [(i, (i + 1) % lon_count) for i in range(lon_count)]
    west_pairs = [(j, i) for i, j in east_pairs]
    west = lax.ppermute(take(every, slice(-h, None)), "lon", east_pairs)
    east = lax.ppermute(take(every, slice(0, h)), "lon", west_pairs)

    rows_hi = take(slice(-h, None), every)
    rows_lo = take(slice(0, h), every)
    top_band = jnp.concatenate([west[:, -h:, :], rows_hi, east[:, -h:, :]], axis=2)
    bottom_band = jnp.concatenate([west[:, :h, :], rows_lo, east[:, :h, :]], axis=2)

    mirror = lax.ppermute(
        top_band, ("lon", "lat"), fold_pairs(lon_count, lat_count, lambda i: lon_count - 1 - i)
    )
    mirrored = mirror[:, :, ::-1]
    folded = jnp.concatenate([mirrored[:, 1:2, :], mirrored[:, 0:1, :]], axis=1)
    folded = folded * sign[:, None, None]

    north_pairs = [(j, j + 1) for j in range(lat_count - 1)]
    south_pairs = [(j, i) for i, j in north_pairs]
    south = lax.ppermute(top_band, "lat", north_pairs)
    north = lax.ppermute(bottom_band, "lat", south_pairs)
    is_top = lax.axis_index("lat") == lat_count - 1
    north = jnp.where(is_top, folded, north)
    return west, east, south, north


def shards(
    potential_heat,
    salt_anomaly_field,
    zonal_current,
    meridional_current,
    water_indicator,
    floor_layer_index,
    zonal_spacing,
    meridional_spacing,
    planetary_rotation_factor,
    horizontal_eddy_coefficient,
    diapycnal_diffusivity,
    layer_height,
):
    fields = (potential_heat, salt_anomaly_field, zonal_current, meridional_current)
    surfaces = (
        floor_layer_index,
        zonal_spacing,
        meridional_spacing,
        planetary_rotation_factor,
        horizontal_eddy_coefficient,
    )

    def take(rs, cs):
        wet = water_indicator[:, rs, cs].astype(jnp.float32)
        parts = [f[:, rs, cs] * wet for f in fields] + [wet]
        parts += [s[None, rs, cs].astype(jnp.float32) for s in surfaces]
        parts.append(diapycnal_diffusivity[:, rs, cs])
        return jnp.concatenate(parts, axis=0)

    channels = len(fields) + 1
    levels, rows, cols = potential_heat.shape
    channel_sign = jnp.array([1.0, 1.0, -1.0, -1.0, 1.0], jnp.float32)
    sign = jnp.concatenate(
        [jnp.repeat(channel_sign, levels), jnp.ones((len(surfaces) + levels - 1,), jnp.float32)]
    )
    west, east, south, north = exchange(take, sign)
    block = take(slice(None), slice(None))
    lanes = 2 * cols
    gap = lanes - cols - 2 * HALO

    def to_lanes(band):
        count = band.shape[1]
        return jnp.concatenate(
            [
                band[:, :, HALO:-HALO],
                band[:, :, -HALO:],
                jnp.zeros((band.shape[0], count, gap), jnp.float32),
                band[:, :, :HALO],
            ],
            axis=2,
        )

    middle = jnp.concatenate(
        [block, east, jnp.zeros((block.shape[0], rows, gap), jnp.float32), west], axis=2
    )
    lead = ROW_OFFSET - HALO
    tail = ROW_PAD - ROW_OFFSET - rows - HALO
    grid = jnp.concatenate(
        [
            jnp.zeros((block.shape[0], lead, lanes), jnp.float32),
            to_lanes(south),
            middle,
            to_lanes(north),
            jnp.zeros((block.shape[0], tail, lanes), jnp.float32),
        ],
        axis=1,
    )
    flags = jnp.stack(
        [(lax.axis_index("lat") == 0).astype(jnp.float32), jnp.float32(0.0)]
    )
    out = pl.pallas_call(
        two_steps_kernel,
        out_shape=jax.ShapeDtypeStruct((channels - 1, levels, rows, cols), jnp.float32),
        in_specs=[
            pl.BlockSpec(memory_space=pltpu.SMEM),
            pl.BlockSpec(memory_space=pltpu.SMEM),
            pl.BlockSpec(memory_space=pltpu.VMEM),
        ],
        out_specs=pl.BlockSpec(memory_space=pltpu.VMEM),
    )(layer_height, flags, grid)
    return (out[0], out[1], out[2], out[3])


ROW_OFFSET = 8
ROW_PAD = 112


def two_steps_kernel(height_ref, flag_ref, grid_ref, out_ref):
    levels = out_ref.shape[1]
    rows, cols = out_ref.shape[2], out_ref.shape[3]
    count, width = grid_ref.shape[1], grid_ref.shape[2]
    lane = lax.broadcasted_iota(jnp.int32, (count, width), 1)
    sub = lax.broadcasted_iota(jnp.int32, (count, width), 0)
    lane_fwd = pltpu.roll(lane, 1, 1) == (lane + width - 1) % width
    sub_fwd = pltpu.roll(sub, 1, 0) == (sub + count - 1) % count

    def east_of(x):
        return jnp.where(lane_fwd, pltpu.roll(x, width - 1, 1), pltpu.roll(x, 1, 1))

    def west_of(x):
        return jnp.where(lane_fwd, pltpu.roll(x, 1, 1), pltpu.roll(x, width - 1, 1))

    def north_of(x):
        return jnp.where(sub_fwd, pltpu.roll(x, count - 1, 0), pltpu.roll(x, 1, 0))

    def south_of(x):
        return jnp.where(sub_fwd, pltpu.roll(x, 1, 0), pltpu.roll(x, count - 1, 0))

    n_state = 5 * levels
    floor_index = grid_ref[n_state]
    zonal_spacing = grid_ref[n_state + 1]
    meridional_spacing = grid_ref[n_state + 2]
    rotation = grid_ref[n_state + 3]
    eddy = grid_ref[n_state + 4]
    diapycnal = [grid_ref[n_state + 5 + k] for k in range(levels - 1)]
    heights = [height_ref[k] for k in range(levels)]
    zonal_sq = zonal_spacing * zonal_spacing
    merid_sq = meridional_spacing * meridional_spacing
    half_zonal = 0.5 / zonal_spacing
    half_merid = 0.5 / meridional_spacing
    at_bottom = [(floor_index == float(k)).astype(jnp.float32) for k in range(levels)]

    def one_step(state):
        wet = state[4]
        fields = state[:4]
        pressure_column = []
        running = None
        for k in range(levels):
            mass = (CONTRACTION * fields[1][k] - EXPANSION * fields[0][k]) * heights[k]
            running = mass if running is None else running + mass
            pressure_column.append(running - 0.5 * mass)
        fluxes = []
        for c in range(4):
            fluxes.append(
                [
                    diapycnal[k] * (wet[k + 1] * wet[k]) * (fields[c][k + 1] - fields[c][k])
                    for k in range(levels - 1)
                ]
            )
        new_state = [[None] * levels for _ in range(5)]
        for k in range(levels):
            w = wet[k]
            w_e, w_w, w_n, w_s = east_of(w), west_of(w), north_of(w), south_of(w)
            weight_east, weight_west = w * w_e, w * w_w
            weight_north, weight_south = w * w_n, w * w_s
            u = fields[2][k]
            v = fields[3][k]
            p = pressure_column[k]
            gradient_x = -(east_of(p) - west_of(p)) * half_zonal
            gradient_y = -(north_of(p) - south_of(p)) * half_merid
            for c in range(4):
                f = fields[c][k]
                f_e, f_w, f_n, f_s = east_of(f), west_of(f), north_of(f), south_of(f)
                diffusion = eddy * (
                    (weight_east * (f_e - f) + weight_west * (f_w - f)) / zonal_sq
                    + (weight_north * (f_n - f) + weight_south * (f_s - f)) / merid_sq
                )
                advection = -(u * (f_e - f_w) * half_zonal + v * (f_n - f_s) * half_merid)
                below = fluxes[c][k] if k < levels - 1 else 0.0
                above = fluxes[c][k - 1] if k > 0 else 0.0
                mixing = (below - above) / (heights[k] * heights[k])
                tendency = advection + diffusion + mixing
                if c == 2:
                    tendency = tendency + rotation * v + gradient_x - BOTTOM_DRAG * at_bottom[k] * u
                if c == 3:
                    tendency = tendency - rotation * u + gradient_y - BOTTOM_DRAG * at_bottom[k] * v
                new_state[c][k] = w * (f + TIME_STEP * tendency)
            new_state[4][k] = w
        return new_state

    state0 = [[grid_ref[c * levels + k] for k in range(levels)] for c in range(5)]
    state1 = one_step(state0)
    clear = jnp.logical_and(sub == ROW_OFFSET - 1, flag_ref[0] > 0.5)
    state1 = [[jnp.where(clear, 0.0, x) for x in channel] for channel in state1]
    state2 = one_step(state1)
    for c in range(4):
        for k in range(levels):
            out_ref[c, k] = state2[c][k][ROW_OFFSET : ROW_OFFSET + rows, :cols]


def solution(mesh):
    return jax.shard_map(
        shards,
        mesh=mesh,
        in_specs=(
            P(None, "lat", "lon"),
            P(None, "lat", "lon"),
            P(None, "lat", "lon"),
            P(None, "lat", "lon"),
            P(None, "lat", "lon"),
            P("lat", "lon"),
            P("lat", "lon"),
            P("lat", "lon"),
            P("lat", "lon"),
            P("lat", "lon"),
            P(None, "lat", "lon"),
            P(),
        ),
        out_specs=(
            P(None, "lat", "lon"),
            P(None, "lat", "lon"),
            P(None, "lat", "lon"),
            P(None, "lat", "lon"),
        ),
        check_vma=False,
    )
```

```python
import jax
import jax.numpy as jnp
from jax import lax
from jax.sharding import PartitionSpec as P
from jax.experimental import pallas as pl
from jax.experimental.pallas import tpu as pltpu

TIME_STEP = 0.25
EXPANSION = 0.2
CONTRACTION = 0.8
BOTTOM_DRAG = 1.0
HALO = 2


def pressure(temp_part, salt_part, layer_height):
    layer_mass = (CONTRACTION * salt_part - EXPANSION * temp_part) * layer_height[:, None, None]
    return jnp.cumsum(layer_mass, axis=0) - 0.5 * layer_mass


def mix_vertically(fields, water_share, diapycnal_diffusivity, layer_height):
    contrast = fields[:, 1:] - fields[:, :-1]
    fluxes = diapycnal_diffusivity * (water_share[1:] * water_share[:-1]) * contrast
    boundary = jnp.zeros_like(fluxes[:, :1])
    flux_below = jnp.concatenate([fluxes, boundary], axis=1)
    flux_above = jnp.concatenate([boundary, fluxes], axis=1)
    return (flux_below - flux_above) / (layer_height * layer_height)[None, :, None, None]


def advance(
    central,
    eastern,
    western,
    northern,
    southern,
    at_bottom,
    zonal_spacing,
    meridional_spacing,
    planetary_rotation_factor,
    horizontal_eddy_coefficient,
    diapycnal_diffusivity,
    layer_height,
):
    water_share = central[4]
    fields = central[:4]
    weight_east = water_share * eastern[4]
    weight_west = water_share * western[4]
    weight_north = water_share * northern[4]
    weight_south = water_share * southern[4]
    diffusion = horizontal_eddy_coefficient * (
        (weight_east * (eastern[:4] - fields) + weight_west * (western[:4] - fields))
        / (zonal_spacing * zonal_spacing)
        + (weight_north * (northern[:4] - fields) + weight_south * (southern[:4] - fields))
        / (meridional_spacing * meridional_spacing)
    )
    zonal = fields[2]
    merid = fields[3]
    advection = -(
        zonal * (eastern[:4] - western[:4]) * (0.5 / zonal_spacing)
        + merid * (northern[:4] - southern[:4]) * (0.5 / meridional_spacing)
    )
    pressure_east = pressure(eastern[0], eastern[1], layer_height)
    pressure_west = pressure(western[0], western[1], layer_height)
    pressure_north = pressure(northern[0], northern[1], layer_height)
    pressure_south = pressure(southern[0], southern[1], layer_height)
    gradient_x = -(pressure_east - pressure_west) * (0.5 / zonal_spacing)
    gradient_y = -(pressure_north - pressure_south) * (0.5 / meridional_spacing)
    mixing = mix_vertically(fields, water_share, diapycnal_diffusivity, layer_height)
    tendency = advection + diffusion + mixing
    tend_zonal = (
        tendency[2]
        + planetary_rotation_factor * merid
        + gradient_x
        - BOTTOM_DRAG * at_bottom * zonal
    )
    tend_merid = (
        tendency[3]
        - planetary_rotation_factor * zonal
        + gradient_y
        - BOTTOM_DRAG * at_bottom * merid
    )
    tendency = jnp.stack([tendency[0], tendency[1], tend_zonal, tend_merid])
    updated = water_share * (fields + TIME_STEP * tendency)
    return jnp.concatenate([updated, water_share[None]], axis=0)


def step(state, params, levels, layer_height):
    floor_index = params[0]
    at_bottom = (
        lax.broadcasted_iota(jnp.int32, (levels, 1, 1), 0).astype(jnp.float32) == floor_index[None]
    ).astype(jnp.float32)
    return advance(
        state[:, :, 1:-1, 1:-1],
        state[:, :, 1:-1, 2:],
        state[:, :, 1:-1, :-2],
        state[:, :, 2:, 1:-1],
        state[:, :, :-2, 1:-1],
        at_bottom,
        params[1],
        params[2],
        params[3],
        params[4],
        params[5:8],
        layer_height,
    )


def fold_pairs(lon_count, lat_count, target_of):
    top = lat_count - 1
    return [(i * lat_count + top, (target_of(i) % lon_count) * lat_count + top) for i in range(lon_count)]


def exchange(take, sign):
    lon_count = lax.axis_size("lon")
    lat_count = lax.axis_size("lat")
    h = HALO
    every = slice(None)

    east_pairs = [(i, (i + 1) % lon_count) for i in range(lon_count)]
    west_pairs = [(j, i) for i, j in east_pairs]
    west = lax.ppermute(take(every, slice(-h, None)), "lon", east_pairs)
    east = lax.ppermute(take(every, slice(0, h)), "lon", west_pairs)

    rows_hi = take(slice(-h, None), every)
    rows_lo = take(slice(0, h), every)
    top_band = jnp.concatenate([west[:, -h:, :], rows_hi, east[:, -h:, :]], axis=2)
    bottom_band = jnp.concatenate([west[:, :h, :], rows_lo, east[:, :h, :]], axis=2)

    mirror = lax.ppermute(
        top_band, ("lon", "lat"), fold_pairs(lon_count, lat_count, lambda i: lon_count - 1 - i)
    )
    mirrored = mirror[:, :, ::-1]
    folded = jnp.concatenate([mirrored[:, 1:2, :], mirrored[:, 0:1, :]], axis=1)
    folded = folded * sign[:, None, None]

    north_pairs = [(j, j + 1) for j in range(lat_count - 1)]
    south_pairs = [(j, i) for i, j in north_pairs]
    south = lax.ppermute(top_band, "lat", north_pairs)
    north = lax.ppermute(bottom_band, "lat", south_pairs)
    is_top = lax.axis_index("lat") == lat_count - 1
    north = jnp.where(is_top, folded, north)
    return west, east, south, north


def shards(
    potential_heat,
    salt_anomaly_field,
    zonal_current,
    meridional_current,
    water_indicator,
    floor_layer_index,
    zonal_spacing,
    meridional_spacing,
    planetary_rotation_factor,
    horizontal_eddy_coefficient,
    diapycnal_diffusivity,
    layer_height,
):
    fields = (potential_heat, salt_anomaly_field, zonal_current, meridional_current)
    surfaces = (
        floor_layer_index,
        zonal_spacing,
        meridional_spacing,
        planetary_rotation_factor,
        horizontal_eddy_coefficient,
    )

    def take(rs, cs):
        wet = water_indicator[:, rs, cs].astype(jnp.float32)
        parts = [f[:, rs, cs] * wet for f in fields] + [wet]
        parts += [s[None, rs, cs].astype(jnp.float32) for s in surfaces]
        parts.append(diapycnal_diffusivity[:, rs, cs])
        return jnp.concatenate(parts, axis=0)

    channels = len(fields) + 1
    levels, rows, cols = potential_heat.shape
    channel_sign = jnp.array([1.0, 1.0, -1.0, -1.0, 1.0], jnp.float32)
    sign = jnp.concatenate(
        [jnp.repeat(channel_sign, levels), jnp.ones((len(surfaces) + levels - 1,), jnp.float32)]
    )
    west, east, south, north = exchange(take, sign)
    block = take(slice(None), slice(None))
    lanes = 2 * cols
    gap = lanes - cols - 2 * HALO

    def to_lanes(band):
        count = band.shape[1]
        return jnp.concatenate(
            [
                band[:, :, HALO:-HALO],
                band[:, :, -HALO:],
                jnp.zeros((band.shape[0], count, gap), jnp.float32),
                band[:, :, :HALO],
            ],
            axis=2,
        )

    middle = jnp.concatenate(
        [block, east, jnp.zeros((block.shape[0], rows, gap), jnp.float32), west], axis=2
    )
    lead = ROW_OFFSET - HALO
    tail = ROW_PAD - ROW_OFFSET - rows - HALO
    grid = jnp.concatenate(
        [
            jnp.zeros((block.shape[0], lead, lanes), jnp.float32),
            to_lanes(south),
            middle,
            to_lanes(north),
            jnp.zeros((block.shape[0], tail, lanes), jnp.float32),
        ],
        axis=1,
    )
    flags = jnp.stack(
        [(lax.axis_index("lat") == 0).astype(jnp.float32), jnp.float32(0.0)]
    )
    field_shape = jax.ShapeDtypeStruct((levels, rows, cols), jnp.float32)
    out = pl.pallas_call(
        two_steps_kernel,
        out_shape=[field_shape] * (channels - 1),
        in_specs=[
            pl.BlockSpec(memory_space=pltpu.SMEM),
            pl.BlockSpec(memory_space=pltpu.SMEM),
            pl.BlockSpec(memory_space=pltpu.VMEM),
        ],
        out_specs=[pl.BlockSpec(memory_space=pltpu.VMEM)] * (channels - 1),
        compiler_params=pltpu.CompilerParams(allow_input_fusion=[False, False, True]),
    )(layer_height, flags, grid)
    return tuple(out)


ROW_OFFSET = 8
ROW_PAD = 112


def two_steps_kernel(height_ref, flag_ref, grid_ref, *out_refs):
    levels = out_refs[0].shape[0]
    rows, cols = out_refs[0].shape[1], out_refs[0].shape[2]
    count, width = grid_ref.shape[1], grid_ref.shape[2]
    lane = lax.broadcasted_iota(jnp.int32, (count, width), 1)
    sub = lax.broadcasted_iota(jnp.int32, (count, width), 0)
    lane_fwd = pltpu.roll(lane, 1, 1) == (lane + width - 1) % width
    sub_fwd = pltpu.roll(sub, 1, 0) == (sub + count - 1) % count

    def east_of(x):
        return jnp.where(lane_fwd, pltpu.roll(x, width - 1, 1), pltpu.roll(x, 1, 1))

    def west_of(x):
        return jnp.where(lane_fwd, pltpu.roll(x, 1, 1), pltpu.roll(x, width - 1, 1))

    def north_of(x):
        return jnp.where(sub_fwd, pltpu.roll(x, count - 1, 0), pltpu.roll(x, 1, 0))

    def south_of(x):
        return jnp.where(sub_fwd, pltpu.roll(x, 1, 0), pltpu.roll(x, count - 1, 0))

    n_state = 5 * levels
    floor_index = grid_ref[n_state]
    zonal_spacing = grid_ref[n_state + 1]
    meridional_spacing = grid_ref[n_state + 2]
    rotation = grid_ref[n_state + 3]
    eddy = grid_ref[n_state + 4]
    diapycnal = [grid_ref[n_state + 5 + k] for k in range(levels - 1)]
    heights = [height_ref[k] for k in range(levels)]
    zonal_sq = zonal_spacing * zonal_spacing
    merid_sq = meridional_spacing * meridional_spacing
    half_zonal = 0.5 / zonal_spacing
    half_merid = 0.5 / meridional_spacing
    at_bottom = [(floor_index == float(k)).astype(jnp.float32) for k in range(levels)]

    def one_step(state):
        wet = state[4]
        fields = state[:4]
        pressure_column = []
        running = None
        for k in range(levels):
            mass = (CONTRACTION * fields[1][k] - EXPANSION * fields[0][k]) * heights[k]
            running = mass if running is None else running + mass
            pressure_column.append(running - 0.5 * mass)
        fluxes = []
        for c in range(4):
            fluxes.append(
                [
                    diapycnal[k] * (wet[k + 1] * wet[k]) * (fields[c][k + 1] - fields[c][k])
                    for k in range(levels - 1)
                ]
            )
        new_state = [[None] * levels for _ in range(5)]
        for k in range(levels):
            w = wet[k]
            w_e, w_w, w_n, w_s = east_of(w), west_of(w), north_of(w), south_of(w)
            weight_east, weight_west = w * w_e, w * w_w
            weight_north, weight_south = w * w_n, w * w_s
            u = fields[2][k]
            v = fields[3][k]
            p = pressure_column[k]
            gradient_x = -(east_of(p) - west_of(p)) * half_zonal
            gradient_y = -(north_of(p) - south_of(p)) * half_merid
            for c in range(4):
                f = fields[c][k]
                f_e, f_w, f_n, f_s = east_of(f), west_of(f), north_of(f), south_of(f)
                diffusion = eddy * (
                    (weight_east * (f_e - f) + weight_west * (f_w - f)) / zonal_sq
                    + (weight_north * (f_n - f) + weight_south * (f_s - f)) / merid_sq
                )
                advection = -(u * (f_e - f_w) * half_zonal + v * (f_n - f_s) * half_merid)
                below = fluxes[c][k] if k < levels - 1 else 0.0
                above = fluxes[c][k - 1] if k > 0 else 0.0
                mixing = (below - above) / (heights[k] * heights[k])
                tendency = advection + diffusion + mixing
                if c == 2:
                    tendency = tendency + rotation * v + gradient_x - BOTTOM_DRAG * at_bottom[k] * u
                if c == 3:
                    tendency = tendency - rotation * u + gradient_y - BOTTOM_DRAG * at_bottom[k] * v
                new_state[c][k] = w * (f + TIME_STEP * tendency)
            new_state[4][k] = w
        return new_state

    state0 = [[grid_ref[c * levels + k] for k in range(levels)] for c in range(5)]
    state1 = one_step(state0)
    clear = jnp.logical_and(sub == ROW_OFFSET - 1, flag_ref[0] > 0.5)
    state1 = [[jnp.where(clear, 0.0, x) for x in channel] for channel in state1]
    state2 = one_step(state1)
    for c in range(4):
        for k in range(levels):
            out_refs[c][k] = state2[c][k][ROW_OFFSET : ROW_OFFSET + rows, :cols]


def solution(mesh):
    return jax.shard_map(
        shards,
        mesh=mesh,
        in_specs=(
            P(None, "lat", "lon"),
            P(None, "lat", "lon"),
            P(None, "lat", "lon"),
            P(None, "lat", "lon"),
            P(None, "lat", "lon"),
            P("lat", "lon"),
            P("lat", "lon"),
            P("lat", "lon"),
            P("lat", "lon"),
            P("lat", "lon"),
            P(None, "lat", "lon"),
            P(),
        ),
        out_specs=(
            P(None, "lat", "lon"),
            P(None, "lat", "lon"),
            P(None, "lat", "lon"),
            P(None, "lat", "lon"),
        ),
        check_vma=False,
    )
```

```python
import jax
import jax.numpy as jnp
from jax import lax
from jax.sharding import PartitionSpec as P
from jax.experimental import pallas as pl
from jax.experimental.pallas import tpu as pltpu

TIME_STEP = 0.25
EXPANSION = 0.2
CONTRACTION = 0.8
BOTTOM_DRAG = 1.0
HALO = 2


def pressure(temp_part, salt_part, layer_height):
    layer_mass = (CONTRACTION * salt_part - EXPANSION * temp_part) * layer_height[:, None, None]
    return jnp.cumsum(layer_mass, axis=0) - 0.5 * layer_mass


def mix_vertically(fields, water_share, diapycnal_diffusivity, layer_height):
    contrast = fields[:, 1:] - fields[:, :-1]
    fluxes = diapycnal_diffusivity * (water_share[1:] * water_share[:-1]) * contrast
    boundary = jnp.zeros_like(fluxes[:, :1])
    flux_below = jnp.concatenate([fluxes, boundary], axis=1)
    flux_above = jnp.concatenate([boundary, fluxes], axis=1)
    return (flux_below - flux_above) / (layer_height * layer_height)[None, :, None, None]


def advance(
    central,
    eastern,
    western,
    northern,
    southern,
    at_bottom,
    zonal_spacing,
    meridional_spacing,
    planetary_rotation_factor,
    horizontal_eddy_coefficient,
    diapycnal_diffusivity,
    layer_height,
):
    water_share = central[4]
    fields = central[:4]
    weight_east = water_share * eastern[4]
    weight_west = water_share * western[4]
    weight_north = water_share * northern[4]
    weight_south = water_share * southern[4]
    diffusion = horizontal_eddy_coefficient * (
        (weight_east * (eastern[:4] - fields) + weight_west * (western[:4] - fields))
        / (zonal_spacing * zonal_spacing)
        + (weight_north * (northern[:4] - fields) + weight_south * (southern[:4] - fields))
        / (meridional_spacing * meridional_spacing)
    )
    zonal = fields[2]
    merid = fields[3]
    advection = -(
        zonal * (eastern[:4] - western[:4]) * (0.5 / zonal_spacing)
        + merid * (northern[:4] - southern[:4]) * (0.5 / meridional_spacing)
    )
    pressure_east = pressure(eastern[0], eastern[1], layer_height)
    pressure_west = pressure(western[0], western[1], layer_height)
    pressure_north = pressure(northern[0], northern[1], layer_height)
    pressure_south = pressure(southern[0], southern[1], layer_height)
    gradient_x = -(pressure_east - pressure_west) * (0.5 / zonal_spacing)
    gradient_y = -(pressure_north - pressure_south) * (0.5 / meridional_spacing)
    mixing = mix_vertically(fields, water_share, diapycnal_diffusivity, layer_height)
    tendency = advection + diffusion + mixing
    tend_zonal = (
        tendency[2]
        + planetary_rotation_factor * merid
        + gradient_x
        - BOTTOM_DRAG * at_bottom * zonal
    )
    tend_merid = (
        tendency[3]
        - planetary_rotation_factor * zonal
        + gradient_y
        - BOTTOM_DRAG * at_bottom * merid
    )
    tendency = jnp.stack([tendency[0], tendency[1], tend_zonal, tend_merid])
    updated = water_share * (fields + TIME_STEP * tendency)
    return jnp.concatenate([updated, water_share[None]], axis=0)


def step(state, params, levels, layer_height):
    floor_index = params[0]
    at_bottom = (
        lax.broadcasted_iota(jnp.int32, (levels, 1, 1), 0).astype(jnp.float32) == floor_index[None]
    ).astype(jnp.float32)
    return advance(
        state[:, :, 1:-1, 1:-1],
        state[:, :, 1:-1, 2:],
        state[:, :, 1:-1, :-2],
        state[:, :, 2:, 1:-1],
        state[:, :, :-2, 1:-1],
        at_bottom,
        params[1],
        params[2],
        params[3],
        params[4],
        params[5:8],
        layer_height,
    )


def fold_pairs(lon_count, lat_count, target_of):
    top = lat_count - 1
    return [(i * lat_count + top, (target_of(i) % lon_count) * lat_count + top) for i in range(lon_count)]


def exchange(take, sign):
    lon_count = lax.axis_size("lon")
    lat_count = lax.axis_size("lat")
    h = HALO
    every = slice(None)

    east_pairs = [(i, (i + 1) % lon_count) for i in range(lon_count)]
    west_pairs = [(j, i) for i, j in east_pairs]
    west = lax.ppermute(take(every, slice(-h, None)), "lon", east_pairs)
    east = lax.ppermute(take(every, slice(0, h)), "lon", west_pairs)

    rows_hi = take(slice(-h, None), every)
    rows_lo = take(slice(0, h), every)
    top_band = jnp.concatenate([west[:, -h:, :], rows_hi, east[:, -h:, :]], axis=2)
    bottom_band = jnp.concatenate([west[:, :h, :], rows_lo, east[:, :h, :]], axis=2)

    mirror = lax.ppermute(
        top_band, ("lon", "lat"), fold_pairs(lon_count, lat_count, lambda i: lon_count - 1 - i)
    )
    mirrored = mirror[:, :, ::-1]
    folded = jnp.concatenate([mirrored[:, 1:2, :], mirrored[:, 0:1, :]], axis=1)
    folded = folded * sign[:, None, None]

    north_pairs = [(j, j + 1) for j in range(lat_count - 1)]
    south_pairs = [(j, i) for i, j in north_pairs]
    south = lax.ppermute(top_band, "lat", north_pairs)
    north = lax.ppermute(bottom_band, "lat", south_pairs)
    is_top = lax.axis_index("lat") == lat_count - 1
    north = jnp.where(is_top, folded, north)
    return west, east, south, north


def shards(
    potential_heat,
    salt_anomaly_field,
    zonal_current,
    meridional_current,
    water_indicator,
    floor_layer_index,
    zonal_spacing,
    meridional_spacing,
    planetary_rotation_factor,
    horizontal_eddy_coefficient,
    diapycnal_diffusivity,
    layer_height,
):
    fields = (potential_heat, salt_anomaly_field, zonal_current, meridional_current)
    surfaces = (
        floor_layer_index,
        zonal_spacing,
        meridional_spacing,
        planetary_rotation_factor,
        horizontal_eddy_coefficient,
    )

    def take(rs, cs):
        wet = water_indicator[:, rs, cs].astype(jnp.float32)
        parts = [f[:, rs, cs] * wet for f in fields] + [wet]
        parts += [s[None, rs, cs].astype(jnp.float32) for s in surfaces]
        parts.append(diapycnal_diffusivity[:, rs, cs])
        return jnp.concatenate(parts, axis=0)

    channels = len(fields) + 1
    levels, rows, cols = potential_heat.shape
    channel_sign = jnp.array([1.0, 1.0, -1.0, -1.0, 1.0], jnp.float32)
    sign = jnp.concatenate(
        [jnp.repeat(channel_sign, levels), jnp.ones((len(surfaces) + levels - 1,), jnp.float32)]
    )
    west, east, south, north = exchange(take, sign)
    block = take(slice(None), slice(None))
    lanes = 2 * cols
    gap = lanes - cols - 2 * HALO

    def to_lanes(band):
        count = band.shape[1]
        return jnp.concatenate(
            [
                band[:, :, HALO:-HALO],
                band[:, :, -HALO:],
                jnp.zeros((band.shape[0], count, gap), jnp.float32),
                band[:, :, :HALO],
            ],
            axis=2,
        )

    middle = jnp.concatenate(
        [block, east, jnp.zeros((block.shape[0], rows, gap), jnp.float32), west], axis=2
    )
    lead = ROW_OFFSET - HALO
    tail = ROW_PAD - ROW_OFFSET - rows - HALO
    rim_low = jnp.concatenate(
        [jnp.zeros((block.shape[0], lead, lanes), jnp.float32), to_lanes(south)], axis=1
    )
    rim_high = jnp.concatenate(
        [to_lanes(north), jnp.zeros((block.shape[0], tail, lanes), jnp.float32)], axis=1
    )
    flags = jnp.stack(
        [(lax.axis_index("lat") == 0).astype(jnp.float32), jnp.float32(0.0)]
    )
    field_shape = jax.ShapeDtypeStruct((levels, rows, cols), jnp.float32)
    out = pl.pallas_call(
        two_steps_kernel,
        out_shape=[field_shape] * (channels - 1),
        in_specs=[
            pl.BlockSpec(memory_space=pltpu.SMEM),
            pl.BlockSpec(memory_space=pltpu.SMEM),
            pl.BlockSpec(memory_space=pltpu.VMEM),
            pl.BlockSpec(memory_space=pltpu.VMEM),
            pl.BlockSpec(memory_space=pltpu.VMEM),
        ],
        out_specs=[pl.BlockSpec(memory_space=pltpu.VMEM)] * (channels - 1),
    )(layer_height, flags, rim_low, middle, rim_high)
    return tuple(out)


ROW_OFFSET = 8
ROW_PAD = 112


def two_steps_kernel(height_ref, flag_ref, low_ref, middle_ref, high_ref, *out_refs):
    levels = out_refs[0].shape[0]
    rows, cols = out_refs[0].shape[1], out_refs[0].shape[2]
    count = low_ref.shape[1] + middle_ref.shape[1] + high_ref.shape[1]
    width = middle_ref.shape[2]

    def plane(p):
        return jnp.concatenate([low_ref[p], middle_ref[p], high_ref[p]], axis=0)

    lane = lax.broadcasted_iota(jnp.int32, (count, width), 1)
    sub = lax.broadcasted_iota(jnp.int32, (count, width), 0)
    lane_fwd = pltpu.roll(lane, 1, 1) == (lane + width - 1) % width
    sub_fwd = pltpu.roll(sub, 1, 0) == (sub + count - 1) % count

    def east_of(x):
        return jnp.where(lane_fwd, pltpu.roll(x, width - 1, 1), pltpu.roll(x, 1, 1))

    def west_of(x):
        return jnp.where(lane_fwd, pltpu.roll(x, 1, 1), pltpu.roll(x, width - 1, 1))

    def north_of(x):
        return jnp.where(sub_fwd, pltpu.roll(x, count - 1, 0), pltpu.roll(x, 1, 0))

    def south_of(x):
        return jnp.where(sub_fwd, pltpu.roll(x, 1, 0), pltpu.roll(x, count - 1, 0))

    n_state = 5 * levels
    floor_index = plane(n_state)
    zonal_spacing = plane(n_state + 1)
    meridional_spacing = plane(n_state + 2)
    rotation = plane(n_state + 3)
    eddy = plane(n_state + 4)
    diapycnal = [plane(n_state + 5 + k) for k in range(levels - 1)]
    heights = [height_ref[k] for k in range(levels)]
    zonal_sq = zonal_spacing * zonal_spacing
    merid_sq = meridional_spacing * meridional_spacing
    half_zonal = 0.5 / zonal_spacing
    half_merid = 0.5 / meridional_spacing
    at_bottom = [(floor_index == float(k)).astype(jnp.float32) for k in range(levels)]

    def one_step(state):
        wet = state[4]
        fields = state[:4]
        pressure_column = []
        running = None
        for k in range(levels):
            mass = (CONTRACTION * fields[1][k] - EXPANSION * fields[0][k]) * heights[k]
            running = mass if running is None else running + mass
            pressure_column.append(running - 0.5 * mass)
        fluxes = []
        for c in range(4):
            fluxes.append(
                [
                    diapycnal[k] * (wet[k + 1] * wet[k]) * (fields[c][k + 1] - fields[c][k])
                    for k in range(levels - 1)
                ]
            )
        new_state = [[None] * levels for _ in range(5)]
        for k in range(levels):
            w = wet[k]
            w_e, w_w, w_n, w_s = east_of(w), west_of(w), north_of(w), south_of(w)
            weight_east, weight_west = w * w_e, w * w_w
            weight_north, weight_south = w * w_n, w * w_s
            u = fields[2][k]
            v = fields[3][k]
            p = pressure_column[k]
            gradient_x = -(east_of(p) - west_of(p)) * half_zonal
            gradient_y = -(north_of(p) - south_of(p)) * half_merid
            for c in range(4):
                f = fields[c][k]
                f_e, f_w, f_n, f_s = east_of(f), west_of(f), north_of(f), south_of(f)
                diffusion = eddy * (
                    (weight_east * (f_e - f) + weight_west * (f_w - f)) / zonal_sq
                    + (weight_north * (f_n - f) + weight_south * (f_s - f)) / merid_sq
                )
                advection = -(u * (f_e - f_w) * half_zonal + v * (f_n - f_s) * half_merid)
                below = fluxes[c][k] if k < levels - 1 else 0.0
                above = fluxes[c][k - 1] if k > 0 else 0.0
                mixing = (below - above) / (heights[k] * heights[k])
                tendency = advection + diffusion + mixing
                if c == 2:
                    tendency = tendency + rotation * v + gradient_x - BOTTOM_DRAG * at_bottom[k] * u
                if c == 3:
                    tendency = tendency - rotation * u + gradient_y - BOTTOM_DRAG * at_bottom[k] * v
                new_state[c][k] = w * (f + TIME_STEP * tendency)
            new_state[4][k] = w
        return new_state

    state0 = [[plane(c * levels + k) for k in range(levels)] for c in range(5)]
    state1 = one_step(state0)
    clear = jnp.logical_and(sub == ROW_OFFSET - 1, flag_ref[0] > 0.5)
    state1 = [[jnp.where(clear, 0.0, x) for x in channel] for channel in state1]
    state2 = one_step(state1)
    for c in range(4):
        for k in range(levels):
            out_refs[c][k] = state2[c][k][ROW_OFFSET : ROW_OFFSET + rows, :cols]


def solution(mesh):
    return jax.shard_map(
        shards,
        mesh=mesh,
        in_specs=(
            P(None, "lat", "lon"),
            P(None, "lat", "lon"),
            P(None, "lat", "lon"),
            P(None, "lat", "lon"),
            P(None, "lat", "lon"),
            P("lat", "lon"),
            P("lat", "lon"),
            P("lat", "lon"),
            P("lat", "lon"),
            P("lat", "lon"),
            P(None, "lat", "lon"),
            P(),
        ),
        out_specs=(
            P(None, "lat", "lon"),
            P(None, "lat", "lon"),
            P(None, "lat", "lon"),
            P(None, "lat", "lon"),
        ),
        check_vma=False,
    )
```

```python
import jax
import jax.numpy as jnp
from jax import lax
from jax.sharding import PartitionSpec as P
from jax.experimental import pallas as pl
from jax.experimental.pallas import tpu as pltpu

TIME_STEP = 0.25
EXPANSION = 0.2
CONTRACTION = 0.8
BOTTOM_DRAG = 1.0
HALO = 2


def pressure(temp_part, salt_part, layer_height):
    layer_mass = (CONTRACTION * salt_part - EXPANSION * temp_part) * layer_height[:, None, None]
    return jnp.cumsum(layer_mass, axis=0) - 0.5 * layer_mass


def mix_vertically(fields, water_share, diapycnal_diffusivity, layer_height):
    contrast = fields[:, 1:] - fields[:, :-1]
    fluxes = diapycnal_diffusivity * (water_share[1:] * water_share[:-1]) * contrast
    boundary = jnp.zeros_like(fluxes[:, :1])
    flux_below = jnp.concatenate([fluxes, boundary], axis=1)
    flux_above = jnp.concatenate([boundary, fluxes], axis=1)
    return (flux_below - flux_above) / (layer_height * layer_height)[None, :, None, None]


def advance(
    central,
    eastern,
    western,
    northern,
    southern,
    at_bottom,
    zonal_spacing,
    meridional_spacing,
    planetary_rotation_factor,
    horizontal_eddy_coefficient,
    diapycnal_diffusivity,
    layer_height,
):
    water_share = central[4]
    fields = central[:4]
    weight_east = water_share * eastern[4]
    weight_west = water_share * western[4]
    weight_north = water_share * northern[4]
    weight_south = water_share * southern[4]
    diffusion = horizontal_eddy_coefficient * (
        (weight_east * (eastern[:4] - fields) + weight_west * (western[:4] - fields))
        / (zonal_spacing * zonal_spacing)
        + (weight_north * (northern[:4] - fields) + weight_south * (southern[:4] - fields))
        / (meridional_spacing * meridional_spacing)
    )
    zonal = fields[2]
    merid = fields[3]
    advection = -(
        zonal * (eastern[:4] - western[:4]) * (0.5 / zonal_spacing)
        + merid * (northern[:4] - southern[:4]) * (0.5 / meridional_spacing)
    )
    pressure_east = pressure(eastern[0], eastern[1], layer_height)
    pressure_west = pressure(western[0], western[1], layer_height)
    pressure_north = pressure(northern[0], northern[1], layer_height)
    pressure_south = pressure(southern[0], southern[1], layer_height)
    gradient_x = -(pressure_east - pressure_west) * (0.5 / zonal_spacing)
    gradient_y = -(pressure_north - pressure_south) * (0.5 / meridional_spacing)
    mixing = mix_vertically(fields, water_share, diapycnal_diffusivity, layer_height)
    tendency = advection + diffusion + mixing
    tend_zonal = (
        tendency[2]
        + planetary_rotation_factor * merid
        + gradient_x
        - BOTTOM_DRAG * at_bottom * zonal
    )
    tend_merid = (
        tendency[3]
        - planetary_rotation_factor * zonal
        + gradient_y
        - BOTTOM_DRAG * at_bottom * merid
    )
    tendency = jnp.stack([tendency[0], tendency[1], tend_zonal, tend_merid])
    updated = water_share * (fields + TIME_STEP * tendency)
    return jnp.concatenate([updated, water_share[None]], axis=0)


def step(state, params, levels, layer_height):
    floor_index = params[0]
    at_bottom = (
        lax.broadcasted_iota(jnp.int32, (levels, 1, 1), 0).astype(jnp.float32) == floor_index[None]
    ).astype(jnp.float32)
    return advance(
        state[:, :, 1:-1, 1:-1],
        state[:, :, 1:-1, 2:],
        state[:, :, 1:-1, :-2],
        state[:, :, 2:, 1:-1],
        state[:, :, :-2, 1:-1],
        at_bottom,
        params[1],
        params[2],
        params[3],
        params[4],
        params[5:8],
        layer_height,
    )


def fold_pairs(lon_count, lat_count, target_of):
    top = lat_count - 1
    return [(i * lat_count + top, (target_of(i) % lon_count) * lat_count + top) for i in range(lon_count)]


def exchange(take, sign):
    lon_count = lax.axis_size("lon")
    lat_count = lax.axis_size("lat")
    h = HALO
    every = slice(None)

    east_pairs = [(i, (i + 1) % lon_count) for i in range(lon_count)]
    west_pairs = [(j, i) for i, j in east_pairs]
    west = lax.ppermute(take(every, slice(-h, None)), "lon", east_pairs)
    east = lax.ppermute(take(every, slice(0, h)), "lon", west_pairs)

    rows_hi = take(slice(-h, None), every)
    rows_lo = take(slice(0, h), every)
    top_band = jnp.concatenate([west[:, -h:, :], rows_hi, east[:, -h:, :]], axis=2)
    bottom_band = jnp.concatenate([west[:, :h, :], rows_lo, east[:, :h, :]], axis=2)

    mirror = lax.ppermute(
        top_band, ("lon", "lat"), fold_pairs(lon_count, lat_count, lambda i: lon_count - 1 - i)
    )
    mirrored = mirror[:, :, ::-1]
    folded = jnp.concatenate([mirrored[:, 1:2, :], mirrored[:, 0:1, :]], axis=1)
    folded = folded * sign[:, None, None]

    north_pairs = [(j, j + 1) for j in range(lat_count - 1)]
    south_pairs = [(j, i) for i, j in north_pairs]
    south = lax.ppermute(top_band, "lat", north_pairs)
    north = lax.ppermute(bottom_band, "lat", south_pairs)
    is_top = lax.axis_index("lat") == lat_count - 1
    north = jnp.where(is_top, folded, north)
    return west, east, south, north


def shards(
    potential_heat,
    salt_anomaly_field,
    zonal_current,
    meridional_current,
    water_indicator,
    floor_layer_index,
    zonal_spacing,
    meridional_spacing,
    planetary_rotation_factor,
    horizontal_eddy_coefficient,
    diapycnal_diffusivity,
    layer_height,
):
    fields = (potential_heat, salt_anomaly_field, zonal_current, meridional_current)
    surfaces = (
        floor_layer_index,
        zonal_spacing,
        meridional_spacing,
        planetary_rotation_factor,
        horizontal_eddy_coefficient,
    )

    def take(rs, cs):
        wet = water_indicator[:, rs, cs].astype(jnp.float32)
        parts = [f[:, rs, cs] * wet for f in fields] + [wet]
        parts += [s[None, rs, cs].astype(jnp.float32) for s in surfaces]
        parts.append(diapycnal_diffusivity[:, rs, cs])
        return jnp.concatenate(parts, axis=0)

    channels = len(fields) + 1
    levels, rows, cols = potential_heat.shape
    channel_sign = jnp.array([1.0, 1.0, -1.0, -1.0, 1.0], jnp.float32)
    sign = jnp.concatenate(
        [jnp.repeat(channel_sign, levels), jnp.ones((len(surfaces) + levels - 1,), jnp.float32)]
    )
    west, east, south, north = exchange(take, sign)
    block = take(slice(None), slice(None))
    lanes = 2 * cols
    gap = lanes - cols - 2 * HALO

    def to_lanes(band):
        count = band.shape[1]
        return jnp.concatenate(
            [
                band[:, :, HALO:-HALO],
                band[:, :, -HALO:],
                jnp.zeros((band.shape[0], count, gap), jnp.float32),
                band[:, :, :HALO],
            ],
            axis=2,
        )

    middle = jnp.concatenate(
        [block, east, jnp.zeros((block.shape[0], rows, gap), jnp.float32), west], axis=2
    )
    lead = ROW_OFFSET - HALO
    tail = ROW_PAD - ROW_OFFSET - rows - HALO
    rim_low = jnp.concatenate(
        [jnp.zeros((block.shape[0], lead, lanes), jnp.float32), to_lanes(south)], axis=1
    )
    rim_high = jnp.concatenate(
        [to_lanes(north), jnp.zeros((block.shape[0], tail, lanes), jnp.float32)], axis=1
    )
    flags = jnp.stack(
        [(lax.axis_index("lat") == 0).astype(jnp.float32), jnp.float32(0.0)]
    )
    field_shape = jax.ShapeDtypeStruct((levels, rows, cols), jnp.float32)
    out = pl.pallas_call(
        two_steps_kernel,
        out_shape=[field_shape] * (channels - 1),
        in_specs=[
            pl.BlockSpec(memory_space=pltpu.SMEM),
            pl.BlockSpec(memory_space=pltpu.SMEM),
            pl.BlockSpec(memory_space=pltpu.VMEM),
            pl.BlockSpec(memory_space=pltpu.VMEM),
            pl.BlockSpec(memory_space=pltpu.VMEM),
        ],
        out_specs=[pl.BlockSpec(memory_space=pltpu.VMEM)] * (channels - 1),
    )(layer_height, flags, rim_low, middle, rim_high)
    return tuple(out)


ROW_OFFSET = 8
ROW_PAD = 112


def two_steps_kernel(height_ref, flag_ref, low_ref, middle_ref, high_ref, *out_refs):
    levels = out_refs[0].shape[0]
    rows, cols = out_refs[0].shape[1], out_refs[0].shape[2]
    count = low_ref.shape[1] + middle_ref.shape[1] + high_ref.shape[1]
    width = middle_ref.shape[2]

    def plane(p):
        return jnp.concatenate([low_ref[p], middle_ref[p], high_ref[p]], axis=0)

    sub = lax.broadcasted_iota(jnp.int32, (count, width), 0)

    def east_of(x):
        return pltpu.roll(x, width - 1, 1)

    def west_of(x):
        return pltpu.roll(x, 1, 1)

    def north_of(x):
        return pltpu.roll(x, count - 1, 0)

    def south_of(x):
        return pltpu.roll(x, 1, 0)

    n_state = 5 * levels
    floor_index = plane(n_state)
    zonal_spacing = plane(n_state + 1)
    meridional_spacing = plane(n_state + 2)
    rotation = plane(n_state + 3)
    eddy = plane(n_state + 4)
    diapycnal = [plane(n_state + 5 + k) for k in range(levels - 1)]
    heights = [height_ref[k] for k in range(levels)]
    inv_zonal_sq = 1.0 / (zonal_spacing * zonal_spacing)
    inv_merid_sq = 1.0 / (meridional_spacing * meridional_spacing)
    inv_height_sq = [1.0 / (h * h) for h in heights]
    half_zonal = 0.5 / zonal_spacing
    half_merid = 0.5 / meridional_spacing
    at_bottom = [(floor_index == float(k)).astype(jnp.float32) for k in range(levels)]

    def one_step(state):
        wet = state[4]
        fields = state[:4]
        pressure_column = []
        running = None
        for k in range(levels):
            mass = (CONTRACTION * fields[1][k] - EXPANSION * fields[0][k]) * heights[k]
            running = mass if running is None else running + mass
            pressure_column.append(running - 0.5 * mass)
        fluxes = []
        for c in range(4):
            fluxes.append(
                [
                    diapycnal[k] * (wet[k + 1] * wet[k]) * (fields[c][k + 1] - fields[c][k])
                    for k in range(levels - 1)
                ]
            )
        new_state = [[None] * levels for _ in range(5)]
        for k in range(levels):
            w = wet[k]
            w_e, w_w, w_n, w_s = east_of(w), west_of(w), north_of(w), south_of(w)
            weight_east, weight_west = w * w_e, w * w_w
            weight_north, weight_south = w * w_n, w * w_s
            u = fields[2][k]
            v = fields[3][k]
            p = pressure_column[k]
            gradient_x = -(east_of(p) - west_of(p)) * half_zonal
            gradient_y = -(north_of(p) - south_of(p)) * half_merid
            for c in range(4):
                f = fields[c][k]
                f_e, f_w, f_n, f_s = east_of(f), west_of(f), north_of(f), south_of(f)
                diffusion = eddy * (
                    (weight_east * (f_e - f) + weight_west * (f_w - f)) * inv_zonal_sq
                    + (weight_north * (f_n - f) + weight_south * (f_s - f)) * inv_merid_sq
                )
                advection = -(u * (f_e - f_w) * half_zonal + v * (f_n - f_s) * half_merid)
                below = fluxes[c][k] if k < levels - 1 else 0.0
                above = fluxes[c][k - 1] if k > 0 else 0.0
                mixing = (below - above) * inv_height_sq[k]
                tendency = advection + diffusion + mixing
                if c == 2:
                    tendency = tendency + rotation * v + gradient_x - BOTTOM_DRAG * at_bottom[k] * u
                if c == 3:
                    tendency = tendency - rotation * u + gradient_y - BOTTOM_DRAG * at_bottom[k] * v
                new_state[c][k] = w * (f + TIME_STEP * tendency)
            new_state[4][k] = w
        return new_state

    state0 = [[plane(c * levels + k) for k in range(levels)] for c in range(5)]
    state1 = one_step(state0)
    clear = jnp.logical_and(sub == ROW_OFFSET - 1, flag_ref[0] > 0.5)
    state1 = [[jnp.where(clear, 0.0, x) for x in channel] for channel in state1]
    state2 = one_step(state1)
    for c in range(4):
        for k in range(levels):
            out_refs[c][k] = state2[c][k][ROW_OFFSET : ROW_OFFSET + rows, :cols]


def solution(mesh):
    return jax.shard_map(
        shards,
        mesh=mesh,
        in_specs=(
            P(None, "lat", "lon"),
            P(None, "lat", "lon"),
            P(None, "lat", "lon"),
            P(None, "lat", "lon"),
            P(None, "lat", "lon"),
            P("lat", "lon"),
            P("lat", "lon"),
            P("lat", "lon"),
            P("lat", "lon"),
            P("lat", "lon"),
            P(None, "lat", "lon"),
            P(),
        ),
        out_specs=(
            P(None, "lat", "lon"),
            P(None, "lat", "lon"),
            P(None, "lat", "lon"),
            P(None, "lat", "lon"),
        ),
        check_vma=False,
    )
```

```python
import jax
import jax.numpy as jnp
from jax import lax
from jax.sharding import PartitionSpec as P
from jax.experimental import pallas as pl
from jax.experimental.pallas import tpu as pltpu

TIME_STEP = 0.25
EXPANSION = 0.2
CONTRACTION = 0.8
BOTTOM_DRAG = 1.0
HALO = 2


def pressure(temp_part, salt_part, layer_height):
    layer_mass = (CONTRACTION * salt_part - EXPANSION * temp_part) * layer_height[:, None, None]
    return jnp.cumsum(layer_mass, axis=0) - 0.5 * layer_mass


def mix_vertically(fields, water_share, diapycnal_diffusivity, layer_height):
    contrast = fields[:, 1:] - fields[:, :-1]
    fluxes = diapycnal_diffusivity * (water_share[1:] * water_share[:-1]) * contrast
    boundary = jnp.zeros_like(fluxes[:, :1])
    flux_below = jnp.concatenate([fluxes, boundary], axis=1)
    flux_above = jnp.concatenate([boundary, fluxes], axis=1)
    return (flux_below - flux_above) / (layer_height * layer_height)[None, :, None, None]


def advance(
    central,
    eastern,
    western,
    northern,
    southern,
    at_bottom,
    zonal_spacing,
    meridional_spacing,
    planetary_rotation_factor,
    horizontal_eddy_coefficient,
    diapycnal_diffusivity,
    layer_height,
):
    water_share = central[4]
    fields = central[:4]
    weight_east = water_share * eastern[4]
    weight_west = water_share * western[4]
    weight_north = water_share * northern[4]
    weight_south = water_share * southern[4]
    diffusion = horizontal_eddy_coefficient * (
        (weight_east * (eastern[:4] - fields) + weight_west * (western[:4] - fields))
        / (zonal_spacing * zonal_spacing)
        + (weight_north * (northern[:4] - fields) + weight_south * (southern[:4] - fields))
        / (meridional_spacing * meridional_spacing)
    )
    zonal = fields[2]
    merid = fields[3]
    advection = -(
        zonal * (eastern[:4] - western[:4]) * (0.5 / zonal_spacing)
        + merid * (northern[:4] - southern[:4]) * (0.5 / meridional_spacing)
    )
    pressure_east = pressure(eastern[0], eastern[1], layer_height)
    pressure_west = pressure(western[0], western[1], layer_height)
    pressure_north = pressure(northern[0], northern[1], layer_height)
    pressure_south = pressure(southern[0], southern[1], layer_height)
    gradient_x = -(pressure_east - pressure_west) * (0.5 / zonal_spacing)
    gradient_y = -(pressure_north - pressure_south) * (0.5 / meridional_spacing)
    mixing = mix_vertically(fields, water_share, diapycnal_diffusivity, layer_height)
    tendency = advection + diffusion + mixing
    tend_zonal = (
        tendency[2]
        + planetary_rotation_factor * merid
        + gradient_x
        - BOTTOM_DRAG * at_bottom * zonal
    )
    tend_merid = (
        tendency[3]
        - planetary_rotation_factor * zonal
        + gradient_y
        - BOTTOM_DRAG * at_bottom * merid
    )
    tendency = jnp.stack([tendency[0], tendency[1], tend_zonal, tend_merid])
    updated = water_share * (fields + TIME_STEP * tendency)
    return jnp.concatenate([updated, water_share[None]], axis=0)


def step(state, params, levels, layer_height):
    floor_index = params[0]
    at_bottom = (
        lax.broadcasted_iota(jnp.int32, (levels, 1, 1), 0).astype(jnp.float32) == floor_index[None]
    ).astype(jnp.float32)
    return advance(
        state[:, :, 1:-1, 1:-1],
        state[:, :, 1:-1, 2:],
        state[:, :, 1:-1, :-2],
        state[:, :, 2:, 1:-1],
        state[:, :, :-2, 1:-1],
        at_bottom,
        params[1],
        params[2],
        params[3],
        params[4],
        params[5:8],
        layer_height,
    )


def fold_pairs(lon_count, lat_count, target_of):
    top = lat_count - 1
    return [(i * lat_count + top, (target_of(i) % lon_count) * lat_count + top) for i in range(lon_count)]


def exchange(take, sign):
    lon_count = lax.axis_size("lon")
    lat_count = lax.axis_size("lat")
    h = HALO
    every = slice(None)

    east_pairs = [(i, (i + 1) % lon_count) for i in range(lon_count)]
    west_pairs = [(j, i) for i, j in east_pairs]
    west = lax.ppermute(take(every, slice(-h, None)), "lon", east_pairs)
    east = lax.ppermute(take(every, slice(0, h)), "lon", west_pairs)

    rows_hi = take(slice(-h, None), every)
    rows_lo = take(slice(0, h), every)
    top_band = jnp.concatenate([west[:, -h:, :], rows_hi, east[:, -h:, :]], axis=2)
    bottom_band = jnp.concatenate([west[:, :h, :], rows_lo, east[:, :h, :]], axis=2)

    mirror = lax.ppermute(
        top_band, ("lon", "lat"), fold_pairs(lon_count, lat_count, lambda i: lon_count - 1 - i)
    )
    mirrored = mirror[:, :, ::-1]
    folded = jnp.concatenate([mirrored[:, 1:2, :], mirrored[:, 0:1, :]], axis=1)
    folded = folded * sign[:, None, None]

    north_pairs = [(j, j + 1) for j in range(lat_count - 1)]
    south_pairs = [(j, i) for i, j in north_pairs]
    south = lax.ppermute(top_band, "lat", north_pairs)
    north = lax.ppermute(bottom_band, "lat", south_pairs)
    is_top = lax.axis_index("lat") == lat_count - 1
    north = jnp.where(is_top, folded, north)
    return west, east, south, north


def shards(
    potential_heat,
    salt_anomaly_field,
    zonal_current,
    meridional_current,
    water_indicator,
    floor_layer_index,
    zonal_spacing,
    meridional_spacing,
    planetary_rotation_factor,
    horizontal_eddy_coefficient,
    diapycnal_diffusivity,
    layer_height,
):
    fields = (potential_heat, salt_anomaly_field, zonal_current, meridional_current)
    surfaces = (
        floor_layer_index,
        zonal_spacing,
        meridional_spacing,
        planetary_rotation_factor,
        horizontal_eddy_coefficient,
    )

    def take(rs, cs):
        wet = water_indicator[:, rs, cs].astype(jnp.float32)
        parts = [f[:, rs, cs] * wet for f in fields] + [wet]
        parts += [s[None, rs, cs].astype(jnp.float32) for s in surfaces]
        parts.append(diapycnal_diffusivity[:, rs, cs])
        return jnp.concatenate(parts, axis=0)

    channels = len(fields) + 1
    levels, rows, cols = potential_heat.shape
    channel_sign = jnp.array([1.0, 1.0, -1.0, -1.0, 1.0], jnp.float32)
    sign = jnp.concatenate(
        [jnp.repeat(channel_sign, levels), jnp.ones((len(surfaces) + levels - 1,), jnp.float32)]
    )
    west, east, south, north = exchange(take, sign)
    block = take(slice(None), slice(None))
    lanes = 2 * cols
    gap = lanes - cols - 2 * HALO

    def to_lanes(band):
        count = band.shape[1]
        return jnp.concatenate(
            [
                band[:, :, HALO:-HALO],
                band[:, :, -HALO:],
                jnp.zeros((band.shape[0], count, gap), jnp.float32),
                band[:, :, :HALO],
            ],
            axis=2,
        )

    middle = jnp.concatenate(
        [block, east, jnp.zeros((block.shape[0], rows, gap), jnp.float32), west], axis=2
    )
    lead = ROW_OFFSET - HALO
    tail = ROW_PAD - ROW_OFFSET - rows - HALO
    rim_low = jnp.concatenate(
        [jnp.zeros((block.shape[0], lead, lanes), jnp.float32), to_lanes(south)], axis=1
    )
    rim_high = jnp.concatenate(
        [to_lanes(north), jnp.zeros((block.shape[0], tail, lanes), jnp.float32)], axis=1
    )
    flags = jnp.stack(
        [(lax.axis_index("lat") == 0).astype(jnp.float32), jnp.float32(0.0)]
    )
    field_shape = jax.ShapeDtypeStruct((levels, rows, cols), jnp.float32)
    out = pl.pallas_call(
        two_steps_kernel,
        out_shape=[field_shape] * (channels - 1),
        in_specs=[
            pl.BlockSpec(memory_space=pltpu.SMEM),
            pl.BlockSpec(memory_space=pltpu.SMEM),
            pl.BlockSpec(memory_space=pltpu.VMEM),
            pl.BlockSpec(memory_space=pltpu.VMEM),
            pl.BlockSpec(memory_space=pltpu.VMEM),
        ],
        out_specs=[pl.BlockSpec(memory_space=pltpu.VMEM)] * (channels - 1),
    )(layer_height, flags, rim_low, middle, rim_high)
    return tuple(out)


ROW_OFFSET = 8
ROW_PAD = 112


def two_steps_kernel(height_ref, flag_ref, low_ref, middle_ref, high_ref, *out_refs):
    levels = out_refs[0].shape[0]
    rows, cols = out_refs[0].shape[1], out_refs[0].shape[2]
    count = low_ref.shape[1] + middle_ref.shape[1] + high_ref.shape[1]
    width = middle_ref.shape[2]

    def plane(p):
        return jnp.concatenate([low_ref[p], middle_ref[p], high_ref[p]], axis=0)

    sub = lax.broadcasted_iota(jnp.int32, (count, width), 0)

    def east_of(x):
        return pltpu.roll(x, width - 1, 1)

    def west_of(x):
        return pltpu.roll(x, 1, 1)

    def north_of(x):
        return pltpu.roll(x, count - 1, 0)

    def south_of(x):
        return pltpu.roll(x, 1, 0)

    n_state = 5 * levels
    floor_index = plane(n_state)
    zonal_spacing = plane(n_state + 1)
    meridional_spacing = plane(n_state + 2)
    rotation = plane(n_state + 3)
    eddy = plane(n_state + 4)
    diapycnal = [plane(n_state + 5 + k) for k in range(levels - 1)]
    heights = [height_ref[k] for k in range(levels)]
    inv_zonal_sq = 1.0 / (zonal_spacing * zonal_spacing)
    inv_merid_sq = 1.0 / (meridional_spacing * meridional_spacing)
    inv_height_sq = [1.0 / (h * h) for h in heights]
    half_zonal = 0.5 / zonal_spacing
    half_merid = 0.5 / meridional_spacing
    at_bottom = [(floor_index == float(k)).astype(jnp.float32) for k in range(levels)]

    def one_step(state, win):
        wet = state[4]
        fields = state[:4]
        pressure_column = []
        running = None
        for k in range(levels):
            mass = (CONTRACTION * fields[1][k] - EXPANSION * fields[0][k]) * heights[k]
            running = mass if running is None else running + mass
            pressure_column.append(running - 0.5 * mass)
        wet_c = [win(x) for x in wet]
        fields_c = [[win(x) for x in channel] for channel in fields]
        fluxes = []
        for c in range(4):
            fluxes.append(
                [
                    win(diapycnal[k])
                    * (wet_c[k + 1] * wet_c[k])
                    * (fields_c[c][k + 1] - fields_c[c][k])
                    for k in range(levels - 1)
                ]
            )
        inv_zonal_sq_c, inv_merid_sq_c = win(inv_zonal_sq), win(inv_merid_sq)
        half_zonal_c, half_merid_c = win(half_zonal), win(half_merid)
        eddy_c, rotation_c = win(eddy), win(rotation)
        new_state = [[None] * levels for _ in range(5)]
        for k in range(levels):
            w = wet_c[k]
            weight_east, weight_west = w * win(east_of(wet[k])), w * win(west_of(wet[k]))
            weight_north, weight_south = w * win(north_of(wet[k])), w * win(south_of(wet[k]))
            u = fields_c[2][k]
            v = fields_c[3][k]
            p = pressure_column[k]
            gradient_x = -(win(east_of(p)) - win(west_of(p))) * half_zonal_c
            gradient_y = -(win(north_of(p)) - win(south_of(p))) * half_merid_c
            bottom = win(at_bottom[k])
            for c in range(4):
                full = fields[c][k]
                f = fields_c[c][k]
                f_e, f_w = win(east_of(full)), win(west_of(full))
                f_n, f_s = win(north_of(full)), win(south_of(full))
                diffusion = eddy_c * (
                    (weight_east * (f_e - f) + weight_west * (f_w - f)) * inv_zonal_sq_c
                    + (weight_north * (f_n - f) + weight_south * (f_s - f)) * inv_merid_sq_c
                )
                advection = -(u * (f_e - f_w) * half_zonal_c + v * (f_n - f_s) * half_merid_c)
                below = fluxes[c][k] if k < levels - 1 else 0.0
                above = fluxes[c][k - 1] if k > 0 else 0.0
                mixing = (below - above) * inv_height_sq[k]
                tendency = advection + diffusion + mixing
                if c == 2:
                    tendency = tendency + rotation_c * v + gradient_x - BOTTOM_DRAG * bottom * u
                if c == 3:
                    tendency = tendency - rotation_c * u + gradient_y - BOTTOM_DRAG * bottom * v
                new_state[c][k] = w * (f + TIME_STEP * tendency)
            new_state[4][k] = w
        return new_state

    state0 = [[plane(c * levels + k) for k in range(levels)] for c in range(5)]
    state1 = one_step(state0, lambda x: x)
    clear = jnp.logical_and(sub == ROW_OFFSET - 1, flag_ref[0] > 0.5)
    state1 = [[jnp.where(clear, 0.0, x) for x in channel] for channel in state1]
    state2 = one_step(state1, lambda x: x[ROW_OFFSET : ROW_OFFSET + rows, :cols])
    for c in range(4):
        for k in range(levels):
            out_refs[c][k] = state2[c][k]


def solution(mesh):
    return jax.shard_map(
        shards,
        mesh=mesh,
        in_specs=(
            P(None, "lat", "lon"),
            P(None, "lat", "lon"),
            P(None, "lat", "lon"),
            P(None, "lat", "lon"),
            P(None, "lat", "lon"),
            P("lat", "lon"),
            P("lat", "lon"),
            P("lat", "lon"),
            P("lat", "lon"),
            P("lat", "lon"),
            P(None, "lat", "lon"),
            P(),
        ),
        out_specs=(
            P(None, "lat", "lon"),
            P(None, "lat", "lon"),
            P(None, "lat", "lon"),
            P(None, "lat", "lon"),
        ),
        check_vma=False,
    )
```

```python
import jax
import jax.numpy as jnp
from jax import lax
from jax.sharding import PartitionSpec as P
from jax.experimental import pallas as pl
from jax.experimental.pallas import tpu as pltpu

TIME_STEP = 0.25
EXPANSION = 0.2
CONTRACTION = 0.8
BOTTOM_DRAG = 1.0
HALO = 2


def pressure(temp_part, salt_part, layer_height):
    layer_mass = (CONTRACTION * salt_part - EXPANSION * temp_part) * layer_height[:, None, None]
    return jnp.cumsum(layer_mass, axis=0) - 0.5 * layer_mass


def mix_vertically(fields, water_share, diapycnal_diffusivity, layer_height):
    contrast = fields[:, 1:] - fields[:, :-1]
    fluxes = diapycnal_diffusivity * (water_share[1:] * water_share[:-1]) * contrast
    boundary = jnp.zeros_like(fluxes[:, :1])
    flux_below = jnp.concatenate([fluxes, boundary], axis=1)
    flux_above = jnp.concatenate([boundary, fluxes], axis=1)
    return (flux_below - flux_above) / (layer_height * layer_height)[None, :, None, None]


def advance(
    central,
    eastern,
    western,
    northern,
    southern,
    at_bottom,
    zonal_spacing,
    meridional_spacing,
    planetary_rotation_factor,
    horizontal_eddy_coefficient,
    diapycnal_diffusivity,
    layer_height,
):
    water_share = central[4]
    fields = central[:4]
    weight_east = water_share * eastern[4]
    weight_west = water_share * western[4]
    weight_north = water_share * northern[4]
    weight_south = water_share * southern[4]
    diffusion = horizontal_eddy_coefficient * (
        (weight_east * (eastern[:4] - fields) + weight_west * (western[:4] - fields))
        / (zonal_spacing * zonal_spacing)
        + (weight_north * (northern[:4] - fields) + weight_south * (southern[:4] - fields))
        / (meridional_spacing * meridional_spacing)
    )
    zonal = fields[2]
    merid = fields[3]
    advection = -(
        zonal * (eastern[:4] - western[:4]) * (0.5 / zonal_spacing)
        + merid * (northern[:4] - southern[:4]) * (0.5 / meridional_spacing)
    )
    pressure_east = pressure(eastern[0], eastern[1], layer_height)
    pressure_west = pressure(western[0], western[1], layer_height)
    pressure_north = pressure(northern[0], northern[1], layer_height)
    pressure_south = pressure(southern[0], southern[1], layer_height)
    gradient_x = -(pressure_east - pressure_west) * (0.5 / zonal_spacing)
    gradient_y = -(pressure_north - pressure_south) * (0.5 / meridional_spacing)
    mixing = mix_vertically(fields, water_share, diapycnal_diffusivity, layer_height)
    tendency = advection + diffusion + mixing
    tend_zonal = (
        tendency[2]
        + planetary_rotation_factor * merid
        + gradient_x
        - BOTTOM_DRAG * at_bottom * zonal
    )
    tend_merid = (
        tendency[3]
        - planetary_rotation_factor * zonal
        + gradient_y
        - BOTTOM_DRAG * at_bottom * merid
    )
    tendency = jnp.stack([tendency[0], tendency[1], tend_zonal, tend_merid])
    updated = water_share * (fields + TIME_STEP * tendency)
    return jnp.concatenate([updated, water_share[None]], axis=0)


def step(state, params, levels, layer_height):
    floor_index = params[0]
    at_bottom = (
        lax.broadcasted_iota(jnp.int32, (levels, 1, 1), 0).astype(jnp.float32) == floor_index[None]
    ).astype(jnp.float32)
    return advance(
        state[:, :, 1:-1, 1:-1],
        state[:, :, 1:-1, 2:],
        state[:, :, 1:-1, :-2],
        state[:, :, 2:, 1:-1],
        state[:, :, :-2, 1:-1],
        at_bottom,
        params[1],
        params[2],
        params[3],
        params[4],
        params[5:8],
        layer_height,
    )


def fold_pairs(lon_count, lat_count, target_of):
    top = lat_count - 1
    return [(i * lat_count + top, (target_of(i) % lon_count) * lat_count + top) for i in range(lon_count)]


def swap_edges(axis, size, low_edge, high_edge, periodic):
    if size % 2:
        up = [(i, (i + 1) % size) for i in range(size if periodic else size - 1)]
        down = [(j, i) for i, j in up]
        return lax.ppermute(high_edge, axis, up), lax.ppermute(low_edge, axis, down)
    even = lax.axis_index(axis) % 2 == 0
    inner = []
    for i in range(0, size, 2):
        inner += [(i, i + 1), (i + 1, i)]
    outer = []
    for i in range(1, size if periodic else size - 1, 2):
        outer += [(i, (i + 1) % size), ((i + 1) % size, i)]
    from_inner = lax.ppermute(jnp.where(even, high_edge, low_edge), axis, inner)
    from_outer = lax.ppermute(jnp.where(even, low_edge, high_edge), axis, outer)
    from_lower = jnp.where(even, from_outer, from_inner)
    from_upper = jnp.where(even, from_inner, from_outer)
    return from_lower, from_upper


def exchange(take, sign):
    lon_count = lax.axis_size("lon")
    lat_count = lax.axis_size("lat")
    h = HALO
    every = slice(None)

    west, east = swap_edges("lon", lon_count, take(every, slice(0, h)), take(every, slice(-h, None)), True)

    rows_hi = take(slice(-h, None), every)
    rows_lo = take(slice(0, h), every)
    top_band = jnp.concatenate([west[:, -h:, :], rows_hi, east[:, -h:, :]], axis=2)
    bottom_band = jnp.concatenate([west[:, :h, :], rows_lo, east[:, :h, :]], axis=2)

    mirror = lax.ppermute(
        top_band, ("lon", "lat"), fold_pairs(lon_count, lat_count, lambda i: lon_count - 1 - i)
    )
    mirrored = mirror[:, :, ::-1]
    folded = jnp.concatenate([mirrored[:, 1:2, :], mirrored[:, 0:1, :]], axis=1)
    folded = folded * sign[:, None, None]

    south, north = swap_edges("lat", lat_count, bottom_band, top_band, False)
    is_top = lax.axis_index("lat") == lat_count - 1
    north = jnp.where(is_top, folded, north)
    return west, east, south, north


def shards(
    potential_heat,
    salt_anomaly_field,
    zonal_current,
    meridional_current,
    water_indicator,
    floor_layer_index,
    zonal_spacing,
    meridional_spacing,
    planetary_rotation_factor,
    horizontal_eddy_coefficient,
    diapycnal_diffusivity,
    layer_height,
):
    fields = (potential_heat, salt_anomaly_field, zonal_current, meridional_current)
    surfaces = (
        floor_layer_index,
        zonal_spacing,
        meridional_spacing,
        planetary_rotation_factor,
        horizontal_eddy_coefficient,
    )

    def take(rs, cs):
        wet = water_indicator[:, rs, cs].astype(jnp.float32)
        parts = [f[:, rs, cs] * wet for f in fields] + [wet]
        parts += [s[None, rs, cs].astype(jnp.float32) for s in surfaces]
        parts.append(diapycnal_diffusivity[:, rs, cs])
        return jnp.concatenate(parts, axis=0)

    channels = len(fields) + 1
    levels, rows, cols = potential_heat.shape
    channel_sign = jnp.array([1.0, 1.0, -1.0, -1.0, 1.0], jnp.float32)
    sign = jnp.concatenate(
        [jnp.repeat(channel_sign, levels), jnp.ones((len(surfaces) + levels - 1,), jnp.float32)]
    )
    west, east, south, north = exchange(take, sign)
    block = take(slice(None), slice(None))
    lanes = 2 * cols
    gap = lanes - cols - 2 * HALO

    def to_lanes(band):
        count = band.shape[1]
        return jnp.concatenate(
            [
                band[:, :, HALO:-HALO],
                band[:, :, -HALO:],
                jnp.zeros((band.shape[0], count, gap), jnp.float32),
                band[:, :, :HALO],
            ],
            axis=2,
        )

    middle = jnp.concatenate(
        [block, east, jnp.zeros((block.shape[0], rows, gap), jnp.float32), west], axis=2
    )
    lead = ROW_OFFSET - HALO
    tail = ROW_PAD - ROW_OFFSET - rows - HALO
    rim_low = jnp.concatenate(
        [jnp.zeros((block.shape[0], lead, lanes), jnp.float32), to_lanes(south)], axis=1
    )
    rim_high = jnp.concatenate(
        [to_lanes(north), jnp.zeros((block.shape[0], tail, lanes), jnp.float32)], axis=1
    )
    flags = jnp.stack(
        [(lax.axis_index("lat") == 0).astype(jnp.float32), jnp.float32(0.0)]
    )
    field_shape = jax.ShapeDtypeStruct((levels, rows, cols), jnp.float32)
    out = pl.pallas_call(
        two_steps_kernel,
        out_shape=[field_shape] * (channels - 1),
        in_specs=[
            pl.BlockSpec(memory_space=pltpu.SMEM),
            pl.BlockSpec(memory_space=pltpu.SMEM),
            pl.BlockSpec(memory_space=pltpu.VMEM),
            pl.BlockSpec(memory_space=pltpu.VMEM),
            pl.BlockSpec(memory_space=pltpu.VMEM),
        ],
        out_specs=[pl.BlockSpec(memory_space=pltpu.VMEM)] * (channels - 1),
    )(layer_height, flags, rim_low, middle, rim_high)
    return tuple(out)


ROW_OFFSET = 8
ROW_PAD = 112


def two_steps_kernel(height_ref, flag_ref, low_ref, middle_ref, high_ref, *out_refs):
    levels = out_refs[0].shape[0]
    rows, cols = out_refs[0].shape[1], out_refs[0].shape[2]
    count = low_ref.shape[1] + middle_ref.shape[1] + high_ref.shape[1]
    width = middle_ref.shape[2]

    def plane(p):
        return jnp.concatenate([low_ref[p], middle_ref[p], high_ref[p]], axis=0)

    sub = lax.broadcasted_iota(jnp.int32, (count, width), 0)

    def east_of(x):
        return pltpu.roll(x, width - 1, 1)

    def west_of(x):
        return pltpu.roll(x, 1, 1)

    def north_of(x):
        return pltpu.roll(x, count - 1, 0)

    def south_of(x):
        return pltpu.roll(x, 1, 0)

    n_state = 5 * levels
    floor_index = plane(n_state)
    zonal_spacing = plane(n_state + 1)
    meridional_spacing = plane(n_state + 2)
    rotation = plane(n_state + 3)
    eddy = plane(n_state + 4)
    diapycnal = [plane(n_state + 5 + k) for k in range(levels - 1)]
    heights = [height_ref[k] for k in range(levels)]
    inv_zonal_sq = 1.0 / (zonal_spacing * zonal_spacing)
    inv_merid_sq = 1.0 / (meridional_spacing * meridional_spacing)
    inv_height_sq = [1.0 / (h * h) for h in heights]
    half_zonal = 0.5 / zonal_spacing
    half_merid = 0.5 / meridional_spacing
    at_bottom = [(floor_index == float(k)).astype(jnp.float32) for k in range(levels)]

    def one_step(state, win):
        wet = state[4]
        fields = state[:4]
        pressure_column = []
        running = None
        for k in range(levels):
            mass = (CONTRACTION * fields[1][k] - EXPANSION * fields[0][k]) * heights[k]
            running = mass if running is None else running + mass
            pressure_column.append(running - 0.5 * mass)
        wet_c = [win(x) for x in wet]
        fields_c = [[win(x) for x in channel] for channel in fields]
        fluxes = []
        for c in range(4):
            fluxes.append(
                [
                    win(diapycnal[k])
                    * (wet_c[k + 1] * wet_c[k])
                    * (fields_c[c][k + 1] - fields_c[c][k])
                    for k in range(levels - 1)
                ]
            )
        inv_zonal_sq_c, inv_merid_sq_c = win(inv_zonal_sq), win(inv_merid_sq)
        half_zonal_c, half_merid_c = win(half_zonal), win(half_merid)
        eddy_c, rotation_c = win(eddy), win(rotation)
        new_state = [[None] * levels for _ in range(5)]
        for k in range(levels):
            w = wet_c[k]
            weight_east, weight_west = w * win(east_of(wet[k])), w * win(west_of(wet[k]))
            weight_north, weight_south = w * win(north_of(wet[k])), w * win(south_of(wet[k]))
            u = fields_c[2][k]
            v = fields_c[3][k]
            p = pressure_column[k]
            gradient_x = -(win(east_of(p)) - win(west_of(p))) * half_zonal_c
            gradient_y = -(win(north_of(p)) - win(south_of(p))) * half_merid_c
            bottom = win(at_bottom[k])
            for c in range(4):
                full = fields[c][k]
                f = fields_c[c][k]
                f_e, f_w = win(east_of(full)), win(west_of(full))
                f_n, f_s = win(north_of(full)), win(south_of(full))
                diffusion = eddy_c * (
                    (weight_east * (f_e - f) + weight_west * (f_w - f)) * inv_zonal_sq_c
                    + (weight_north * (f_n - f) + weight_south * (f_s - f)) * inv_merid_sq_c
                )
                advection = -(u * (f_e - f_w) * half_zonal_c + v * (f_n - f_s) * half_merid_c)
                below = fluxes[c][k] if k < levels - 1 else 0.0
                above = fluxes[c][k - 1] if k > 0 else 0.0
                mixing = (below - above) * inv_height_sq[k]
                tendency = advection + diffusion + mixing
                if c == 2:
                    tendency = tendency + rotation_c * v + gradient_x - BOTTOM_DRAG * bottom * u
                if c == 3:
                    tendency = tendency - rotation_c * u + gradient_y - BOTTOM_DRAG * bottom * v
                new_state[c][k] = w * (f + TIME_STEP * tendency)
            new_state[4][k] = w
        return new_state

    state0 = [[plane(c * levels + k) for k in range(levels)] for c in range(5)]
    state1 = one_step(state0, lambda x: x)
    clear = jnp.logical_and(sub == ROW_OFFSET - 1, flag_ref[0] > 0.5)
    state1 = [[jnp.where(clear, 0.0, x) for x in channel] for channel in state1]
    state2 = one_step(state1, lambda x: x[ROW_OFFSET : ROW_OFFSET + rows, :cols])
    for c in range(4):
        for k in range(levels):
            out_refs[c][k] = state2[c][k]


def solution(mesh):
    return jax.shard_map(
        shards,
        mesh=mesh,
        in_specs=(
            P(None, "lat", "lon"),
            P(None, "lat", "lon"),
            P(None, "lat", "lon"),
            P(None, "lat", "lon"),
            P(None, "lat", "lon"),
            P("lat", "lon"),
            P("lat", "lon"),
            P("lat", "lon"),
            P("lat", "lon"),
            P("lat", "lon"),
            P(None, "lat", "lon"),
            P(),
        ),
        out_specs=(
            P(None, "lat", "lon"),
            P(None, "lat", "lon"),
            P(None, "lat", "lon"),
            P(None, "lat", "lon"),
        ),
        check_vma=False,
    )
```

```python
import jax
import jax.numpy as jnp
from jax import lax
from jax.sharding import PartitionSpec as P
from jax.experimental import pallas as pl
from jax.experimental.pallas import tpu as pltpu

TIME_STEP = 0.25
EXPANSION = 0.2
CONTRACTION = 0.8
BOTTOM_DRAG = 1.0
HALO = 2


def pressure(temp_part, salt_part, layer_height):
    layer_mass = (CONTRACTION * salt_part - EXPANSION * temp_part) * layer_height[:, None, None]
    return jnp.cumsum(layer_mass, axis=0) - 0.5 * layer_mass


def mix_vertically(fields, water_share, diapycnal_diffusivity, layer_height):
    contrast = fields[:, 1:] - fields[:, :-1]
    fluxes = diapycnal_diffusivity * (water_share[1:] * water_share[:-1]) * contrast
    boundary = jnp.zeros_like(fluxes[:, :1])
    flux_below = jnp.concatenate([fluxes, boundary], axis=1)
    flux_above = jnp.concatenate([boundary, fluxes], axis=1)
    return (flux_below - flux_above) / (layer_height * layer_height)[None, :, None, None]


def advance(
    central,
    eastern,
    western,
    northern,
    southern,
    at_bottom,
    zonal_spacing,
    meridional_spacing,
    planetary_rotation_factor,
    horizontal_eddy_coefficient,
    diapycnal_diffusivity,
    layer_height,
):
    water_share = central[4]
    fields = central[:4]
    weight_east = water_share * eastern[4]
    weight_west = water_share * western[4]
    weight_north = water_share * northern[4]
    weight_south = water_share * southern[4]
    diffusion = horizontal_eddy_coefficient * (
        (weight_east * (eastern[:4] - fields) + weight_west * (western[:4] - fields))
        / (zonal_spacing * zonal_spacing)
        + (weight_north * (northern[:4] - fields) + weight_south * (southern[:4] - fields))
        / (meridional_spacing * meridional_spacing)
    )
    zonal = fields[2]
    merid = fields[3]
    advection = -(
        zonal * (eastern[:4] - western[:4]) * (0.5 / zonal_spacing)
        + merid * (northern[:4] - southern[:4]) * (0.5 / meridional_spacing)
    )
    pressure_east = pressure(eastern[0], eastern[1], layer_height)
    pressure_west = pressure(western[0], western[1], layer_height)
    pressure_north = pressure(northern[0], northern[1], layer_height)
    pressure_south = pressure(southern[0], southern[1], layer_height)
    gradient_x = -(pressure_east - pressure_west) * (0.5 / zonal_spacing)
    gradient_y = -(pressure_north - pressure_south) * (0.5 / meridional_spacing)
    mixing = mix_vertically(fields, water_share, diapycnal_diffusivity, layer_height)
    tendency = advection + diffusion + mixing
    tend_zonal = (
        tendency[2]
        + planetary_rotation_factor * merid
        + gradient_x
        - BOTTOM_DRAG * at_bottom * zonal
    )
    tend_merid = (
        tendency[3]
        - planetary_rotation_factor * zonal
        + gradient_y
        - BOTTOM_DRAG * at_bottom * merid
    )
    tendency = jnp.stack([tendency[0], tendency[1], tend_zonal, tend_merid])
    updated = water_share * (fields + TIME_STEP * tendency)
    return jnp.concatenate([updated, water_share[None]], axis=0)


def step(state, params, levels, layer_height):
    floor_index = params[0]
    at_bottom = (
        lax.broadcasted_iota(jnp.int32, (levels, 1, 1), 0).astype(jnp.float32) == floor_index[None]
    ).astype(jnp.float32)
    return advance(
        state[:, :, 1:-1, 1:-1],
        state[:, :, 1:-1, 2:],
        state[:, :, 1:-1, :-2],
        state[:, :, 2:, 1:-1],
        state[:, :, :-2, 1:-1],
        at_bottom,
        params[1],
        params[2],
        params[3],
        params[4],
        params[5:8],
        layer_height,
    )


def fold_pairs(lon_count, lat_count, target_of):
    top = lat_count - 1
    return [(i * lat_count + top, (target_of(i) % lon_count) * lat_count + top) for i in range(lon_count)]


def exchange(take, take_edge, take_edge_size, sign):
    lon_count = lax.axis_size("lon")
    lat_count = lax.axis_size("lat")
    h = HALO
    every = slice(None)

    if lon_count % 2:
        east_pairs = [(i, (i + 1) % lon_count) for i in range(lon_count)]
        west_pairs = [(j, i) for i, j in east_pairs]
        west = lax.ppermute(take(every, slice(-h, None)), "lon", east_pairs)
        east = lax.ppermute(take(every, slice(0, h)), "lon", west_pairs)
    else:
        even = lax.axis_index("lon") % 2 == 0
        high = take_edge_size() - h
        inner = []
        for i in range(0, lon_count, 2):
            inner += [(i, i + 1), (i + 1, i)]
        outer = []
        for i in range(1, lon_count, 2):
            outer += [(i, (i + 1) % lon_count), ((i + 1) % lon_count, i)]
        from_inner = lax.ppermute(take_edge(jnp.where(even, high, 0)), "lon", inner)
        from_outer = lax.ppermute(take_edge(jnp.where(even, 0, high)), "lon", outer)
        west = jnp.where(even, from_outer, from_inner)
        east = jnp.where(even, from_inner, from_outer)

    rows_hi = take(slice(-h, None), every)
    rows_lo = take(slice(0, h), every)
    top_band = jnp.concatenate([west[:, -h:, :], rows_hi, east[:, -h:, :]], axis=2)
    bottom_band = jnp.concatenate([west[:, :h, :], rows_lo, east[:, :h, :]], axis=2)

    mirror = lax.ppermute(
        top_band, ("lon", "lat"), fold_pairs(lon_count, lat_count, lambda i: lon_count - 1 - i)
    )
    mirrored = mirror[:, :, ::-1]
    folded = jnp.concatenate([mirrored[:, 1:2, :], mirrored[:, 0:1, :]], axis=1)
    folded = folded * sign[:, None, None]

    north_pairs = [(j, j + 1) for j in range(lat_count - 1)]
    south_pairs = [(j, i) for i, j in north_pairs]
    south = lax.ppermute(top_band, "lat", north_pairs)
    north = lax.ppermute(bottom_band, "lat", south_pairs)
    is_top = lax.axis_index("lat") == lat_count - 1
    north = jnp.where(is_top, folded, north)
    return west, east, south, north


def shards(
    potential_heat,
    salt_anomaly_field,
    zonal_current,
    meridional_current,
    water_indicator,
    floor_layer_index,
    zonal_spacing,
    meridional_spacing,
    planetary_rotation_factor,
    horizontal_eddy_coefficient,
    diapycnal_diffusivity,
    layer_height,
):
    fields = (potential_heat, salt_anomaly_field, zonal_current, meridional_current)
    surfaces = (
        floor_layer_index,
        zonal_spacing,
        meridional_spacing,
        planetary_rotation_factor,
        horizontal_eddy_coefficient,
    )

    def take(rs, cs):
        wet = water_indicator[:, rs, cs].astype(jnp.float32)
        parts = [f[:, rs, cs] * wet for f in fields] + [wet]
        parts += [s[None, rs, cs].astype(jnp.float32) for s in surfaces]
        parts.append(diapycnal_diffusivity[:, rs, cs])
        return jnp.concatenate(parts, axis=0)

    def take_edge(start):
        def cut(a):
            return lax.dynamic_slice_in_dim(a, start, HALO, axis=a.ndim - 1)

        wet = cut(water_indicator).astype(jnp.float32)
        parts = [cut(f) * wet for f in fields] + [wet]
        parts += [cut(s)[None].astype(jnp.float32) for s in surfaces]
        parts.append(cut(diapycnal_diffusivity))
        return jnp.concatenate(parts, axis=0)

    channels = len(fields) + 1
    levels, rows, cols = potential_heat.shape
    channel_sign = jnp.array([1.0, 1.0, -1.0, -1.0, 1.0], jnp.float32)
    sign = jnp.concatenate(
        [jnp.repeat(channel_sign, levels), jnp.ones((len(surfaces) + levels - 1,), jnp.float32)]
    )
    west, east, south, north = exchange(take, take_edge, lambda: cols, sign)
    block = take(slice(None), slice(None))
    lanes = 2 * cols
    gap = lanes - cols - 2 * HALO

    def to_lanes(band):
        count = band.shape[1]
        return jnp.concatenate(
            [
                band[:, :, HALO:-HALO],
                band[:, :, -HALO:],
                jnp.zeros((band.shape[0], count, gap), jnp.float32),
                band[:, :, :HALO],
            ],
            axis=2,
        )

    middle = jnp.concatenate(
        [block, east, jnp.zeros((block.shape[0], rows, gap), jnp.float32), west], axis=2
    )
    lead = ROW_OFFSET - HALO
    tail = ROW_PAD - ROW_OFFSET - rows - HALO
    rim_low = jnp.concatenate(
        [jnp.zeros((block.shape[0], lead, lanes), jnp.float32), to_lanes(south)], axis=1
    )
    rim_high = jnp.concatenate(
        [to_lanes(north), jnp.zeros((block.shape[0], tail, lanes), jnp.float32)], axis=1
    )
    flags = jnp.stack(
        [(lax.axis_index("lat") == 0).astype(jnp.float32), jnp.float32(0.0)]
    )
    field_shape = jax.ShapeDtypeStruct((levels, rows, cols), jnp.float32)
    out = pl.pallas_call(
        two_steps_kernel,
        out_shape=[field_shape] * (channels - 1),
        in_specs=[
            pl.BlockSpec(memory_space=pltpu.SMEM),
            pl.BlockSpec(memory_space=pltpu.SMEM),
            pl.BlockSpec(memory_space=pltpu.VMEM),
            pl.BlockSpec(memory_space=pltpu.VMEM),
            pl.BlockSpec(memory_space=pltpu.VMEM),
        ],
        out_specs=[pl.BlockSpec(memory_space=pltpu.VMEM)] * (channels - 1),
    )(layer_height, flags, rim_low, middle, rim_high)
    return tuple(out)


ROW_OFFSET = 8
ROW_PAD = 112


def two_steps_kernel(height_ref, flag_ref, low_ref, middle_ref, high_ref, *out_refs):
    levels = out_refs[0].shape[0]
    rows, cols = out_refs[0].shape[1], out_refs[0].shape[2]
    count = low_ref.shape[1] + middle_ref.shape[1] + high_ref.shape[1]
    width = middle_ref.shape[2]

    def plane(p):
        return jnp.concatenate([low_ref[p], middle_ref[p], high_ref[p]], axis=0)

    sub = lax.broadcasted_iota(jnp.int32, (count, width), 0)

    def east_of(x):
        return pltpu.roll(x, width - 1, 1)

    def west_of(x):
        return pltpu.roll(x, 1, 1)

    def north_of(x):
        return pltpu.roll(x, count - 1, 0)

    def south_of(x):
        return pltpu.roll(x, 1, 0)

    n_state = 5 * levels
    floor_index = plane(n_state)
    zonal_spacing = plane(n_state + 1)
    meridional_spacing = plane(n_state + 2)
    rotation = plane(n_state + 3)
    eddy = plane(n_state + 4)
    diapycnal = [plane(n_state + 5 + k) for k in range(levels - 1)]
    heights = [height_ref[k] for k in range(levels)]
    inv_zonal_sq = 1.0 / (zonal_spacing * zonal_spacing)
    inv_merid_sq = 1.0 / (meridional_spacing * meridional_spacing)
    inv_height_sq = [1.0 / (h * h) for h in heights]
    half_zonal = 0.5 / zonal_spacing
    half_merid = 0.5 / meridional_spacing
    at_bottom = [(floor_index == float(k)).astype(jnp.float32) for k in range(levels)]

    def one_step(state, win):
        wet = state[4]
        fields = state[:4]
        pressure_column = []
        running = None
        for k in range(levels):
            mass = (CONTRACTION * fields[1][k] - EXPANSION * fields[0][k]) * heights[k]
            running = mass if running is None else running + mass
            pressure_column.append(running - 0.5 * mass)
        wet_c = [win(x) for x in wet]
        fields_c = [[win(x) for x in channel] for channel in fields]
        fluxes = []
        for c in range(4):
            fluxes.append(
                [
                    win(diapycnal[k])
                    * (wet_c[k + 1] * wet_c[k])
                    * (fields_c[c][k + 1] - fields_c[c][k])
                    for k in range(levels - 1)
                ]
            )
        inv_zonal_sq_c, inv_merid_sq_c = win(inv_zonal_sq), win(inv_merid_sq)
        half_zonal_c, half_merid_c = win(half_zonal), win(half_merid)
        eddy_c, rotation_c = win(eddy), win(rotation)
        new_state = [[None] * levels for _ in range(5)]
        for k in range(levels):
            w = wet_c[k]
            weight_east, weight_west = w * win(east_of(wet[k])), w * win(west_of(wet[k]))
            weight_north, weight_south = w * win(north_of(wet[k])), w * win(south_of(wet[k]))
            u = fields_c[2][k]
            v = fields_c[3][k]
            p = pressure_column[k]
            gradient_x = -(win(east_of(p)) - win(west_of(p))) * half_zonal_c
            gradient_y = -(win(north_of(p)) - win(south_of(p))) * half_merid_c
            bottom = win(at_bottom[k])
            for c in range(4):
                full = fields[c][k]
                f = fields_c[c][k]
                f_e, f_w = win(east_of(full)), win(west_of(full))
                f_n, f_s = win(north_of(full)), win(south_of(full))
                diffusion = eddy_c * (
                    (weight_east * (f_e - f) + weight_west * (f_w - f)) * inv_zonal_sq_c
                    + (weight_north * (f_n - f) + weight_south * (f_s - f)) * inv_merid_sq_c
                )
                advection = -(u * (f_e - f_w) * half_zonal_c + v * (f_n - f_s) * half_merid_c)
                below = fluxes[c][k] if k < levels - 1 else 0.0
                above = fluxes[c][k - 1] if k > 0 else 0.0
                mixing = (below - above) * inv_height_sq[k]
                tendency = advection + diffusion + mixing
                if c == 2:
                    tendency = tendency + rotation_c * v + gradient_x - BOTTOM_DRAG * bottom * u
                if c == 3:
                    tendency = tendency - rotation_c * u + gradient_y - BOTTOM_DRAG * bottom * v
                new_state[c][k] = w * (f + TIME_STEP * tendency)
            new_state[4][k] = w
        return new_state

    state0 = [[plane(c * levels + k) for k in range(levels)] for c in range(5)]
    state1 = one_step(state0, lambda x: x)
    clear = jnp.logical_and(sub == ROW_OFFSET - 1, flag_ref[0] > 0.5)
    state1 = [[jnp.where(clear, 0.0, x) for x in channel] for channel in state1]
    state2 = one_step(state1, lambda x: x[ROW_OFFSET : ROW_OFFSET + rows, :cols])
    for c in range(4):
        for k in range(levels):
            out_refs[c][k] = state2[c][k]


def solution(mesh):
    return jax.shard_map(
        shards,
        mesh=mesh,
        in_specs=(
            P(None, "lat", "lon"),
            P(None, "lat", "lon"),
            P(None, "lat", "lon"),
            P(None, "lat", "lon"),
            P(None, "lat", "lon"),
            P("lat", "lon"),
            P("lat", "lon"),
            P("lat", "lon"),
            P("lat", "lon"),
            P("lat", "lon"),
            P(None, "lat", "lon"),
            P(),
        ),
        out_specs=(
            P(None, "lat", "lon"),
            P(None, "lat", "lon"),
            P(None, "lat", "lon"),
            P(None, "lat", "lon"),
        ),
        check_vma=False,
    )
```

```python
import jax
import jax.numpy as jnp
from jax import lax
from jax.sharding import PartitionSpec as P
from jax.experimental import pallas as pl
from jax.experimental.pallas import tpu as pltpu

TIME_STEP = 0.25
EXPANSION = 0.2
CONTRACTION = 0.8
BOTTOM_DRAG = 1.0
HALO = 2


def pressure(temp_part, salt_part, layer_height):
    layer_mass = (CONTRACTION * salt_part - EXPANSION * temp_part) * layer_height[:, None, None]
    return jnp.cumsum(layer_mass, axis=0) - 0.5 * layer_mass


def mix_vertically(fields, water_share, diapycnal_diffusivity, layer_height):
    contrast = fields[:, 1:] - fields[:, :-1]
    fluxes = diapycnal_diffusivity * (water_share[1:] * water_share[:-1]) * contrast
    boundary = jnp.zeros_like(fluxes[:, :1])
    flux_below = jnp.concatenate([fluxes, boundary], axis=1)
    flux_above = jnp.concatenate([boundary, fluxes], axis=1)
    return (flux_below - flux_above) / (layer_height * layer_height)[None, :, None, None]


def advance(
    central,
    eastern,
    western,
    northern,
    southern,
    at_bottom,
    zonal_spacing,
    meridional_spacing,
    planetary_rotation_factor,
    horizontal_eddy_coefficient,
    diapycnal_diffusivity,
    layer_height,
):
    water_share = central[4]
    fields = central[:4]
    weight_east = water_share * eastern[4]
    weight_west = water_share * western[4]
    weight_north = water_share * northern[4]
    weight_south = water_share * southern[4]
    diffusion = horizontal_eddy_coefficient * (
        (weight_east * (eastern[:4] - fields) + weight_west * (western[:4] - fields))
        / (zonal_spacing * zonal_spacing)
        + (weight_north * (northern[:4] - fields) + weight_south * (southern[:4] - fields))
        / (meridional_spacing * meridional_spacing)
    )
    zonal = fields[2]
    merid = fields[3]
    advection = -(
        zonal * (eastern[:4] - western[:4]) * (0.5 / zonal_spacing)
        + merid * (northern[:4] - southern[:4]) * (0.5 / meridional_spacing)
    )
    pressure_east = pressure(eastern[0], eastern[1], layer_height)
    pressure_west = pressure(western[0], western[1], layer_height)
    pressure_north = pressure(northern[0], northern[1], layer_height)
    pressure_south = pressure(southern[0], southern[1], layer_height)
    gradient_x = -(pressure_east - pressure_west) * (0.5 / zonal_spacing)
    gradient_y = -(pressure_north - pressure_south) * (0.5 / meridional_spacing)
    mixing = mix_vertically(fields, water_share, diapycnal_diffusivity, layer_height)
    tendency = advection + diffusion + mixing
    tend_zonal = (
        tendency[2]
        + planetary_rotation_factor * merid
        + gradient_x
        - BOTTOM_DRAG * at_bottom * zonal
    )
    tend_merid = (
        tendency[3]
        - planetary_rotation_factor * zonal
        + gradient_y
        - BOTTOM_DRAG * at_bottom * merid
    )
    tendency = jnp.stack([tendency[0], tendency[1], tend_zonal, tend_merid])
    updated = water_share * (fields + TIME_STEP * tendency)
    return jnp.concatenate([updated, water_share[None]], axis=0)


def step(state, params, levels, layer_height):
    floor_index = params[0]
    at_bottom = (
        lax.broadcasted_iota(jnp.int32, (levels, 1, 1), 0).astype(jnp.float32) == floor_index[None]
    ).astype(jnp.float32)
    return advance(
        state[:, :, 1:-1, 1:-1],
        state[:, :, 1:-1, 2:],
        state[:, :, 1:-1, :-2],
        state[:, :, 2:, 1:-1],
        state[:, :, :-2, 1:-1],
        at_bottom,
        params[1],
        params[2],
        params[3],
        params[4],
        params[5:8],
        layer_height,
    )


def fold_pairs(lon_count, lat_count, target_of):
    top = lat_count - 1
    return [(i * lat_count + top, (target_of(i) % lon_count) * lat_count + top) for i in range(lon_count)]


def exchange(take, take_edge, take_edge_size, sign):
    lon_count = lax.axis_size("lon")
    lat_count = lax.axis_size("lat")
    h = HALO
    every = slice(None)

    if lon_count % 2:
        east_pairs = [(i, (i + 1) % lon_count) for i in range(lon_count)]
        west_pairs = [(j, i) for i, j in east_pairs]
        west = lax.ppermute(take(every, slice(-h, None)), "lon", east_pairs)
        east = lax.ppermute(take(every, slice(0, h)), "lon", west_pairs)
    else:
        even = lax.axis_index("lon") % 2 == 0
        high = take_edge_size(2) - h
        inner = []
        for i in range(0, lon_count, 2):
            inner += [(i, i + 1), (i + 1, i)]
        outer = []
        for i in range(1, lon_count, 2):
            outer += [(i, (i + 1) % lon_count), ((i + 1) % lon_count, i)]
        from_inner = lax.ppermute(take_edge(jnp.where(even, high, 0)), "lon", inner)
        from_outer = lax.ppermute(take_edge(jnp.where(even, 0, high)), "lon", outer)
        west = jnp.where(even, from_outer, from_inner)
        east = jnp.where(even, from_inner, from_outer)

    rows_hi = take(slice(-h, None), every)
    rows_lo = take(slice(0, h), every)
    top_band = jnp.concatenate([west[:, -h:, :], rows_hi, east[:, -h:, :]], axis=2)
    bottom_band = jnp.concatenate([west[:, :h, :], rows_lo, east[:, :h, :]], axis=2)

    mirror = lax.ppermute(
        top_band, ("lon", "lat"), fold_pairs(lon_count, lat_count, lambda i: lon_count - 1 - i)
    )
    mirrored = mirror[:, :, ::-1]
    folded = jnp.concatenate([mirrored[:, 1:2, :], mirrored[:, 0:1, :]], axis=1)
    folded = folded * sign[:, None, None]

    if lat_count % 2:
        north_pairs = [(j, j + 1) for j in range(lat_count - 1)]
        south_pairs = [(j, i) for i, j in north_pairs]
        south = lax.ppermute(top_band, "lat", north_pairs)
        north = lax.ppermute(bottom_band, "lat", south_pairs)
    else:
        even = lax.axis_index("lat") % 2 == 0
        high_row = take_edge_size(1) - h

        def band(start):
            def cut(a):
                return lax.dynamic_slice_in_dim(a, start, h, axis=1)

            return jnp.concatenate([cut(west), take_edge(start, 1), cut(east)], axis=2)

        inner = []
        for j in range(0, lat_count, 2):
            inner += [(j, j + 1), (j + 1, j)]
        outer = []
        for j in range(1, lat_count - 1, 2):
            outer += [(j, j + 1), (j + 1, j)]
        from_inner = lax.ppermute(band(jnp.where(even, high_row, 0)), "lat", inner)
        from_outer = lax.ppermute(band(jnp.where(even, 0, high_row)), "lat", outer)
        south = jnp.where(even, from_outer, from_inner)
        north = jnp.where(even, from_inner, from_outer)
    is_top = lax.axis_index("lat") == lat_count - 1
    north = jnp.where(is_top, folded, north)
    return west, east, south, north


def shards(
    potential_heat,
    salt_anomaly_field,
    zonal_current,
    meridional_current,
    water_indicator,
    floor_layer_index,
    zonal_spacing,
    meridional_spacing,
    planetary_rotation_factor,
    horizontal_eddy_coefficient,
    diapycnal_diffusivity,
    layer_height,
):
    fields = (potential_heat, salt_anomaly_field, zonal_current, meridional_current)
    surfaces = (
        floor_layer_index,
        zonal_spacing,
        meridional_spacing,
        planetary_rotation_factor,
        horizontal_eddy_coefficient,
    )

    def take(rs, cs):
        wet = water_indicator[:, rs, cs].astype(jnp.float32)
        parts = [f[:, rs, cs] * wet for f in fields] + [wet]
        parts += [s[None, rs, cs].astype(jnp.float32) for s in surfaces]
        parts.append(diapycnal_diffusivity[:, rs, cs])
        return jnp.concatenate(parts, axis=0)

    def take_edge(start, axis=2):
        def cut(a):
            return lax.dynamic_slice_in_dim(a, start, HALO, axis=a.ndim + axis - 3)

        wet = cut(water_indicator).astype(jnp.float32)
        parts = [cut(f) * wet for f in fields] + [wet]
        parts += [cut(s)[None].astype(jnp.float32) for s in surfaces]
        parts.append(cut(diapycnal_diffusivity))
        return jnp.concatenate(parts, axis=0)

    channels = len(fields) + 1
    levels, rows, cols = potential_heat.shape
    channel_sign = jnp.array([1.0, 1.0, -1.0, -1.0, 1.0], jnp.float32)
    sign = jnp.concatenate(
        [jnp.repeat(channel_sign, levels), jnp.ones((len(surfaces) + levels - 1,), jnp.float32)]
    )
    west, east, south, north = exchange(take, take_edge, lambda axis: (rows, cols)[axis - 1], sign)
    block = take(slice(None), slice(None))
    lanes = 2 * cols
    gap = lanes - cols - 2 * HALO

    def to_lanes(band):
        count = band.shape[1]
        return jnp.concatenate(
            [
                band[:, :, HALO:-HALO],
                band[:, :, -HALO:],
                jnp.zeros((band.shape[0], count, gap), jnp.float32),
                band[:, :, :HALO],
            ],
            axis=2,
        )

    middle = jnp.concatenate(
        [block, east, jnp.zeros((block.shape[0], rows, gap), jnp.float32), west], axis=2
    )
    lead = ROW_OFFSET - HALO
    tail = ROW_PAD - ROW_OFFSET - rows - HALO
    rim_low = jnp.concatenate(
        [jnp.zeros((block.shape[0], lead, lanes), jnp.float32), to_lanes(south)], axis=1
    )
    rim_high = jnp.concatenate(
        [to_lanes(north), jnp.zeros((block.shape[0], tail, lanes), jnp.float32)], axis=1
    )
    flags = jnp.stack(
        [(lax.axis_index("lat") == 0).astype(jnp.float32), jnp.float32(0.0)]
    )
    field_shape = jax.ShapeDtypeStruct((levels, rows, cols), jnp.float32)
    out = pl.pallas_call(
        two_steps_kernel,
        out_shape=[field_shape] * (channels - 1),
        in_specs=[
            pl.BlockSpec(memory_space=pltpu.SMEM),
            pl.BlockSpec(memory_space=pltpu.SMEM),
            pl.BlockSpec(memory_space=pltpu.VMEM),
            pl.BlockSpec(memory_space=pltpu.VMEM),
            pl.BlockSpec(memory_space=pltpu.VMEM),
        ],
        out_specs=[pl.BlockSpec(memory_space=pltpu.VMEM)] * (channels - 1),
    )(layer_height, flags, rim_low, middle, rim_high)
    return tuple(out)


ROW_OFFSET = 8
ROW_PAD = 112


def two_steps_kernel(height_ref, flag_ref, low_ref, middle_ref, high_ref, *out_refs):
    levels = out_refs[0].shape[0]
    rows, cols = out_refs[0].shape[1], out_refs[0].shape[2]
    count = low_ref.shape[1] + middle_ref.shape[1] + high_ref.shape[1]
    width = middle_ref.shape[2]

    def plane(p):
        return jnp.concatenate([low_ref[p], middle_ref[p], high_ref[p]], axis=0)

    sub = lax.broadcasted_iota(jnp.int32, (count, width), 0)

    def east_of(x):
        return pltpu.roll(x, width - 1, 1)

    def west_of(x):
        return pltpu.roll(x, 1, 1)

    def north_of(x):
        return pltpu.roll(x, count - 1, 0)

    def south_of(x):
        return pltpu.roll(x, 1, 0)

    n_state = 5 * levels
    floor_index = plane(n_state)
    zonal_spacing = plane(n_state + 1)
    meridional_spacing = plane(n_state + 2)
    rotation = plane(n_state + 3)
    eddy = plane(n_state + 4)
    diapycnal = [plane(n_state + 5 + k) for k in range(levels - 1)]
    heights = [height_ref[k] for k in range(levels)]
    inv_zonal_sq = 1.0 / (zonal_spacing * zonal_spacing)
    inv_merid_sq = 1.0 / (meridional_spacing * meridional_spacing)
    inv_height_sq = [1.0 / (h * h) for h in heights]
    half_zonal = 0.5 / zonal_spacing
    half_merid = 0.5 / meridional_spacing
    at_bottom = [(floor_index == float(k)).astype(jnp.float32) for k in range(levels)]

    def one_step(state, win):
        wet = state[4]
        fields = state[:4]
        pressure_column = []
        running = None
        for k in range(levels):
            mass = (CONTRACTION * fields[1][k] - EXPANSION * fields[0][k]) * heights[k]
            running = mass if running is None else running + mass
            pressure_column.append(running - 0.5 * mass)
        wet_c = [win(x) for x in wet]
        fields_c = [[win(x) for x in channel] for channel in fields]
        fluxes = []
        for c in range(4):
            fluxes.append(
                [
                    win(diapycnal[k])
                    * (wet_c[k + 1] * wet_c[k])
                    * (fields_c[c][k + 1] - fields_c[c][k])
                    for k in range(levels - 1)
                ]
            )
        inv_zonal_sq_c, inv_merid_sq_c = win(inv_zonal_sq), win(inv_merid_sq)
        half_zonal_c, half_merid_c = win(half_zonal), win(half_merid)
        eddy_c, rotation_c = win(eddy), win(rotation)
        new_state = [[None] * levels for _ in range(5)]
        for k in range(levels):
            w = wet_c[k]
            weight_east, weight_west = w * win(east_of(wet[k])), w * win(west_of(wet[k]))
            weight_north, weight_south = w * win(north_of(wet[k])), w * win(south_of(wet[k]))
            u = fields_c[2][k]
            v = fields_c[3][k]
            p = pressure_column[k]
            gradient_x = -(win(east_of(p)) - win(west_of(p))) * half_zonal_c
            gradient_y = -(win(north_of(p)) - win(south_of(p))) * half_merid_c
            bottom = win(at_bottom[k])
            for c in range(4):
                full = fields[c][k]
                f = fields_c[c][k]
                f_e, f_w = win(east_of(full)), win(west_of(full))
                f_n, f_s = win(north_of(full)), win(south_of(full))
                diffusion = eddy_c * (
                    (weight_east * (f_e - f) + weight_west * (f_w - f)) * inv_zonal_sq_c
                    + (weight_north * (f_n - f) + weight_south * (f_s - f)) * inv_merid_sq_c
                )
                advection = -(u * (f_e - f_w) * half_zonal_c + v * (f_n - f_s) * half_merid_c)
                below = fluxes[c][k] if k < levels - 1 else 0.0
                above = fluxes[c][k - 1] if k > 0 else 0.0
                mixing = (below - above) * inv_height_sq[k]
                tendency = advection + diffusion + mixing
                if c == 2:
                    tendency = tendency + rotation_c * v + gradient_x - BOTTOM_DRAG * bottom * u
                if c == 3:
                    tendency = tendency - rotation_c * u + gradient_y - BOTTOM_DRAG * bottom * v
                new_state[c][k] = w * (f + TIME_STEP * tendency)
            new_state[4][k] = w
        return new_state

    state0 = [[plane(c * levels + k) for k in range(levels)] for c in range(5)]
    state1 = one_step(state0, lambda x: x)
    clear = jnp.logical_and(sub == ROW_OFFSET - 1, flag_ref[0] > 0.5)
    state1 = [[jnp.where(clear, 0.0, x) for x in channel] for channel in state1]
    state2 = one_step(state1, lambda x: x[ROW_OFFSET : ROW_OFFSET + rows, :cols])
    for c in range(4):
        for k in range(levels):
            out_refs[c][k] = state2[c][k]


def solution(mesh):
    return jax.shard_map(
        shards,
        mesh=mesh,
        in_specs=(
            P(None, "lat", "lon"),
            P(None, "lat", "lon"),
            P(None, "lat", "lon"),
            P(None, "lat", "lon"),
            P(None, "lat", "lon"),
            P("lat", "lon"),
            P("lat", "lon"),
            P("lat", "lon"),
            P("lat", "lon"),
            P("lat", "lon"),
            P(None, "lat", "lon"),
            P(),
        ),
        out_specs=(
            P(None, "lat", "lon"),
            P(None, "lat", "lon"),
            P(None, "lat", "lon"),
            P(None, "lat", "lon"),
        ),
        check_vma=False,
    )
```

```python
import jax
import jax.numpy as jnp
from jax import lax
from jax.sharding import PartitionSpec as P
from jax.experimental import pallas as pl
from jax.experimental.pallas import tpu as pltpu

TIME_STEP = 0.25
EXPANSION = 0.2
CONTRACTION = 0.8
BOTTOM_DRAG = 1.0
HALO = 2


def pressure(temp_part, salt_part, layer_height):
    layer_mass = (CONTRACTION * salt_part - EXPANSION * temp_part) * layer_height[:, None, None]
    return jnp.cumsum(layer_mass, axis=0) - 0.5 * layer_mass


def mix_vertically(fields, water_share, diapycnal_diffusivity, layer_height):
    contrast = fields[:, 1:] - fields[:, :-1]
    fluxes = diapycnal_diffusivity * (water_share[1:] * water_share[:-1]) * contrast
    boundary = jnp.zeros_like(fluxes[:, :1])
    flux_below = jnp.concatenate([fluxes, boundary], axis=1)
    flux_above = jnp.concatenate([boundary, fluxes], axis=1)
    return (flux_below - flux_above) / (layer_height * layer_height)[None, :, None, None]


def advance(
    central,
    eastern,
    western,
    northern,
    southern,
    at_bottom,
    zonal_spacing,
    meridional_spacing,
    planetary_rotation_factor,
    horizontal_eddy_coefficient,
    diapycnal_diffusivity,
    layer_height,
):
    water_share = central[4]
    fields = central[:4]
    weight_east = water_share * eastern[4]
    weight_west = water_share * western[4]
    weight_north = water_share * northern[4]
    weight_south = water_share * southern[4]
    diffusion = horizontal_eddy_coefficient * (
        (weight_east * (eastern[:4] - fields) + weight_west * (western[:4] - fields))
        / (zonal_spacing * zonal_spacing)
        + (weight_north * (northern[:4] - fields) + weight_south * (southern[:4] - fields))
        / (meridional_spacing * meridional_spacing)
    )
    zonal = fields[2]
    merid = fields[3]
    advection = -(
        zonal * (eastern[:4] - western[:4]) * (0.5 / zonal_spacing)
        + merid * (northern[:4] - southern[:4]) * (0.5 / meridional_spacing)
    )
    pressure_east = pressure(eastern[0], eastern[1], layer_height)
    pressure_west = pressure(western[0], western[1], layer_height)
    pressure_north = pressure(northern[0], northern[1], layer_height)
    pressure_south = pressure(southern[0], southern[1], layer_height)
    gradient_x = -(pressure_east - pressure_west) * (0.5 / zonal_spacing)
    gradient_y = -(pressure_north - pressure_south) * (0.5 / meridional_spacing)
    mixing = mix_vertically(fields, water_share, diapycnal_diffusivity, layer_height)
    tendency = advection + diffusion + mixing
    tend_zonal = (
        tendency[2]
        + planetary_rotation_factor * merid
        + gradient_x
        - BOTTOM_DRAG * at_bottom * zonal
    )
    tend_merid = (
        tendency[3]
        - planetary_rotation_factor * zonal
        + gradient_y
        - BOTTOM_DRAG * at_bottom * merid
    )
    tendency = jnp.stack([tendency[0], tendency[1], tend_zonal, tend_merid])
    updated = water_share * (fields + TIME_STEP * tendency)
    return jnp.concatenate([updated, water_share[None]], axis=0)


def step(state, params, levels, layer_height):
    floor_index = params[0]
    at_bottom = (
        lax.broadcasted_iota(jnp.int32, (levels, 1, 1), 0).astype(jnp.float32) == floor_index[None]
    ).astype(jnp.float32)
    return advance(
        state[:, :, 1:-1, 1:-1],
        state[:, :, 1:-1, 2:],
        state[:, :, 1:-1, :-2],
        state[:, :, 2:, 1:-1],
        state[:, :, :-2, 1:-1],
        at_bottom,
        params[1],
        params[2],
        params[3],
        params[4],
        params[5:8],
        layer_height,
    )


def fold_pairs(lon_count, lat_count, target_of):
    top = lat_count - 1
    return [(i * lat_count + top, (target_of(i) % lon_count) * lat_count + top) for i in range(lon_count)]


def exchange(take, take_edge, take_edge_size, sign):
    lon_count = lax.axis_size("lon")
    lat_count = lax.axis_size("lat")
    h = HALO
    every = slice(None)

    if lon_count % 2:
        east_pairs = [(i, (i + 1) % lon_count) for i in range(lon_count)]
        west_pairs = [(j, i) for i, j in east_pairs]
        west = lax.ppermute(take(every, slice(-h, None)), "lon", east_pairs)
        east = lax.ppermute(take(every, slice(0, h)), "lon", west_pairs)
    else:
        even = lax.axis_index("lon") % 2 == 0
        high = take_edge_size() - h
        inner = []
        for i in range(0, lon_count, 2):
            inner += [(i, i + 1), (i + 1, i)]
        outer = []
        for i in range(1, lon_count, 2):
            outer += [(i, (i + 1) % lon_count), ((i + 1) % lon_count, i)]
        from_inner = lax.ppermute(take_edge(jnp.where(even, high, 0)), "lon", inner)
        from_outer = lax.ppermute(take_edge(jnp.where(even, 0, high)), "lon", outer)
        west = jnp.where(even, from_outer, from_inner)
        east = jnp.where(even, from_inner, from_outer)

    rows_hi = take(slice(-h, None), every)
    rows_lo = take(slice(0, h), every)
    top_band = jnp.concatenate([west[:, -h:, :], rows_hi, east[:, -h:, :]], axis=2)
    bottom_band = jnp.concatenate([west[:, :h, :], rows_lo, east[:, :h, :]], axis=2)

    mirror = lax.ppermute(
        top_band, ("lon", "lat"), fold_pairs(lon_count, lat_count, lambda i: lon_count - 1 - i)
    )
    mirrored = mirror[:, :, ::-1]
    folded = jnp.concatenate([mirrored[:, 1:2, :], mirrored[:, 0:1, :]], axis=1)
    folded = folded * sign[:, None, None]

    north_pairs = [(j, j + 1) for j in range(lat_count - 1)]
    south_pairs = [(j, i) for i, j in north_pairs]
    south = lax.ppermute(top_band, "lat", north_pairs)
    north = lax.ppermute(bottom_band, "lat", south_pairs)
    is_top = lax.axis_index("lat") == lat_count - 1
    north = jnp.where(is_top, folded, north)
    return west, east, south, north


def shards(
    potential_heat,
    salt_anomaly_field,
    zonal_current,
    meridional_current,
    water_indicator,
    floor_layer_index,
    zonal_spacing,
    meridional_spacing,
    planetary_rotation_factor,
    horizontal_eddy_coefficient,
    diapycnal_diffusivity,
    layer_height,
):
    fields = (potential_heat, salt_anomaly_field, zonal_current, meridional_current)
    surfaces = (
        floor_layer_index,
        zonal_spacing,
        meridional_spacing,
        planetary_rotation_factor,
        horizontal_eddy_coefficient,
    )

    def take(rs, cs):
        wet = water_indicator[:, rs, cs].astype(jnp.float32)
        parts = [f[:, rs, cs] * wet for f in fields] + [wet]
        parts += [s[None, rs, cs].astype(jnp.float32) for s in surfaces]
        parts.append(diapycnal_diffusivity[:, rs, cs])
        return jnp.concatenate(parts, axis=0)

    def take_edge(start):
        def cut(a):
            return lax.dynamic_slice_in_dim(a, start, HALO, axis=a.ndim - 1)

        wet = cut(water_indicator).astype(jnp.float32)
        parts = [cut(f) * wet for f in fields] + [wet]
        parts += [cut(s)[None].astype(jnp.float32) for s in surfaces]
        parts.append(cut(diapycnal_diffusivity))
        return jnp.concatenate(parts, axis=0)

    channels = len(fields) + 1
    levels, rows, cols = potential_heat.shape
    channel_sign = jnp.array([1.0, 1.0, -1.0, -1.0, 1.0], jnp.float32)
    sign = jnp.concatenate(
        [jnp.repeat(channel_sign, levels), jnp.ones((len(surfaces) + levels - 1,), jnp.float32)]
    )
    west, east, south, north = exchange(take, take_edge, lambda: cols, sign)
    block = take(slice(None), slice(None))
    lanes = 2 * cols
    gap = lanes - cols - 2 * HALO

    def to_lanes(band):
        count = band.shape[1]
        return jnp.concatenate(
            [
                band[:, :, HALO:-HALO],
                band[:, :, -HALO:],
                jnp.zeros((band.shape[0], count, gap), jnp.float32),
                band[:, :, :HALO],
            ],
            axis=2,
        )

    edge = jnp.concatenate(
        [east, jnp.zeros((east.shape[0], rows, gap), jnp.float32), west], axis=2
    )
    lead = ROW_OFFSET - HALO
    tail = ROW_PAD - ROW_OFFSET - rows - HALO
    rim_low = jnp.concatenate(
        [jnp.zeros((block.shape[0], lead, lanes), jnp.float32), to_lanes(south)], axis=1
    )
    rim_high = jnp.concatenate(
        [to_lanes(north), jnp.zeros((block.shape[0], tail, lanes), jnp.float32)], axis=1
    )
    flags = jnp.stack(
        [(lax.axis_index("lat") == 0).astype(jnp.float32), jnp.float32(0.0)]
    )
    field_shape = jax.ShapeDtypeStruct((levels, rows, cols), jnp.float32)
    out = pl.pallas_call(
        two_steps_kernel,
        out_shape=[field_shape] * (channels - 1),
        in_specs=[
            pl.BlockSpec(memory_space=pltpu.SMEM),
            pl.BlockSpec(memory_space=pltpu.SMEM),
        ]
        + [pl.BlockSpec(memory_space=pltpu.VMEM)] * (3 + len(fields) + 1 + len(surfaces) + 1),
        out_specs=[pl.BlockSpec(memory_space=pltpu.VMEM)] * (channels - 1),
    )(
        layer_height,
        flags,
        rim_low,
        edge,
        rim_high,
        *fields,
        water_indicator,
        *surfaces,
        diapycnal_diffusivity,
    )
    return tuple(out)


ROW_OFFSET = 8
ROW_PAD = 112


def two_steps_kernel(height_ref, flag_ref, low_ref, edge_ref, high_ref, *refs):
    field_refs, wet_ref = refs[:4], refs[4]
    surface_refs, diapycnal_ref = refs[5:10], refs[10]
    out_refs = refs[11:]
    levels = out_refs[0].shape[0]
    rows, cols = out_refs[0].shape[1], out_refs[0].shape[2]
    count = low_ref.shape[1] + edge_ref.shape[1] + high_ref.shape[1]
    width = 2 * edge_ref.shape[2]
    wet_levels = [wet_ref[k].astype(jnp.float32) for k in range(levels)]

    def centre(p):
        if p < 4 * levels:
            return field_refs[p // levels][p % levels] * wet_levels[p % levels]
        if p < 5 * levels:
            return wet_levels[p - 4 * levels]
        q = p - 5 * levels
        if q < len(surface_refs):
            return surface_refs[q][...].astype(jnp.float32)
        return diapycnal_ref[q - len(surface_refs)]

    def plane(p):
        middle = jnp.concatenate([centre(p), edge_ref[p]], axis=1)
        return jnp.concatenate([low_ref[p], middle, high_ref[p]], axis=0)

    sub = lax.broadcasted_iota(jnp.int32, (count, width), 0)

    def east_of(x):
        return pltpu.roll(x, width - 1, 1)

    def west_of(x):
        return pltpu.roll(x, 1, 1)

    def north_of(x):
        return pltpu.roll(x, count - 1, 0)

    def south_of(x):
        return pltpu.roll(x, 1, 0)

    n_state = 5 * levels
    floor_index = plane(n_state)
    zonal_spacing = plane(n_state + 1)
    meridional_spacing = plane(n_state + 2)
    rotation = plane(n_state + 3)
    eddy = plane(n_state + 4)
    diapycnal = [plane(n_state + 5 + k) for k in range(levels - 1)]
    heights = [height_ref[k] for k in range(levels)]
    inv_zonal_sq = 1.0 / (zonal_spacing * zonal_spacing)
    inv_merid_sq = 1.0 / (meridional_spacing * meridional_spacing)
    inv_height_sq = [1.0 / (h * h) for h in heights]
    half_zonal = 0.5 / zonal_spacing
    half_merid = 0.5 / meridional_spacing
    at_bottom = [(floor_index == float(k)).astype(jnp.float32) for k in range(levels)]

    def one_step(state, win):
        wet = state[4]
        fields = state[:4]
        pressure_column = []
        running = None
        for k in range(levels):
            mass = (CONTRACTION * fields[1][k] - EXPANSION * fields[0][k]) * heights[k]
            running = mass if running is None else running + mass
            pressure_column.append(running - 0.5 * mass)
        wet_c = [win(x) for x in wet]
        fields_c = [[win(x) for x in channel] for channel in fields]
        fluxes = []
        for c in range(4):
            fluxes.append(
                [
                    win(diapycnal[k])
                    * (wet_c[k + 1] * wet_c[k])
                    * (fields_c[c][k + 1] - fields_c[c][k])
                    for k in range(levels - 1)
                ]
            )
        inv_zonal_sq_c, inv_merid_sq_c = win(inv_zonal_sq), win(inv_merid_sq)
        half_zonal_c, half_merid_c = win(half_zonal), win(half_merid)
        eddy_c, rotation_c = win(eddy), win(rotation)
        new_state = [[None] * levels for _ in range(5)]
        for k in range(levels):
            w = wet_c[k]
            weight_east, weight_west = w * win(east_of(wet[k])), w * win(west_of(wet[k]))
            weight_north, weight_south = w * win(north_of(wet[k])), w * win(south_of(wet[k]))
            u = fields_c[2][k]
            v = fields_c[3][k]
            p = pressure_column[k]
            gradient_x = -(win(east_of(p)) - win(west_of(p))) * half_zonal_c
            gradient_y = -(win(north_of(p)) - win(south_of(p))) * half_merid_c
            bottom = win(at_bottom[k])
            for c in range(4):
                full = fields[c][k]
                f = fields_c[c][k]
                f_e, f_w = win(east_of(full)), win(west_of(full))
                f_n, f_s = win(north_of(full)), win(south_of(full))
                diffusion = eddy_c * (
                    (weight_east * (f_e - f) + weight_west * (f_w - f)) * inv_zonal_sq_c
                    + (weight_north * (f_n - f) + weight_south * (f_s - f)) * inv_merid_sq_c
                )
                advection = -(u * (f_e - f_w) * half_zonal_c + v * (f_n - f_s) * half_merid_c)
                below = fluxes[c][k] if k < levels - 1 else 0.0
                above = fluxes[c][k - 1] if k > 0 else 0.0
                mixing = (below - above) * inv_height_sq[k]
                tendency = advection + diffusion + mixing
                if c == 2:
                    tendency = tendency + rotation_c * v + gradient_x - BOTTOM_DRAG * bottom * u
                if c == 3:
                    tendency = tendency - rotation_c * u + gradient_y - BOTTOM_DRAG * bottom * v
                new_state[c][k] = w * (f + TIME_STEP * tendency)
            new_state[4][k] = w
        return new_state

    state0 = [[plane(c * levels + k) for k in range(levels)] for c in range(5)]
    state1 = one_step(state0, lambda x: x)
    clear = jnp.logical_and(sub == ROW_OFFSET - 1, flag_ref[0] > 0.5)
    state1 = [[jnp.where(clear, 0.0, x) for x in channel] for channel in state1]
    state2 = one_step(state1, lambda x: x[ROW_OFFSET : ROW_OFFSET + rows, :cols])
    for c in range(4):
        for k in range(levels):
            out_refs[c][k] = state2[c][k]


def solution(mesh):
    return jax.shard_map(
        shards,
        mesh=mesh,
        in_specs=(
            P(None, "lat", "lon"),
            P(None, "lat", "lon"),
            P(None, "lat", "lon"),
            P(None, "lat", "lon"),
            P(None, "lat", "lon"),
            P("lat", "lon"),
            P("lat", "lon"),
            P("lat", "lon"),
            P("lat", "lon"),
            P("lat", "lon"),
            P(None, "lat", "lon"),
            P(),
        ),
        out_specs=(
            P(None, "lat", "lon"),
            P(None, "lat", "lon"),
            P(None, "lat", "lon"),
            P(None, "lat", "lon"),
        ),
        check_vma=False,
    )
```
